32 devices in a mesh: gx: 8 (over z, x), ka: 4 (over y, core).
Axes of the slice: x: 2, y: 2, z: 4, core: 2. Of those that a mesh axis runs over, the one named last changes fastest.
Arguments:
- direct_snapshots: bfloat16 [128, 32, 64, 128], P('ka', 'gx'), may hold values from -40 to 40
- adjoint_snapshots: bfloat16 [128, 32, 64, 128], P('ka', 'gx'), may hold values from -40 to 40
- quad_weight: float32 [32, 64], P('gx'), may hold values from 0.5 to 2
- mean_velocity: float32 [32, 64], P('gx'), may hold values from 0.2 to 1.2
- diffusivity: float32 [32, 64], P('gx'), may hold values from 0.05 to 0.5
Outputs:
- hankel_gram: float32 [8192, 128], P(('ka', 'gx'))
- reduced_operator: float32 [8192, 128], P(('ka', 'gx'))
- hankel_norm: float32 [128], P('ka')
The draws below stay inside these ranges and needn't reach their ends.
All inputs are finite; a program needn't handle non-finite values.
Results may differ from the reference program's by a relative error of at most 0.0071.
Values may be sent and summed in bfloat16 or wider, within the bound.
No kernel may reach another device: no remote copies, remote signals or barrier semaphores. Data moves between devices by JAX's collectives and lax.ppermute only.
A program may use at most 64 MiB of HBM per device.

```python
import math
import jax
import jax.numpy as jnp
from jax import lax

NT = 128
NR = 64
S = 64
NX = 32


def snapshot_field(key):
    first_key = jax.random.fold_in(key, 0)
    shape_all = (NT, NX, NR, 2 * S)
    column = jnp.arange(2 * S) % S
    exponent = column.astype(jnp.float32) / (S - 1)
    values = jnp.clip(jax.random.normal(first_key, shape_all, jnp.float32), -5.0, 5.0)
    amplitude = 10.0 ** (0.5 * exponent)
    return (values * amplitude).astype(jnp.bfloat16)


def draw_direct_snapshots(key, part):
    return snapshot_field(jax.random.fold_in(key, 11))


def draw_adjoint_snapshots(key, part):
    return snapshot_field(jax.random.fold_in(key, 23))


def level_of(own_key, dims, cuts, low, top_value):
    def one(position, shards_of):
        draws = jax.random.uniform(jax.random.fold_in(jax.random.fold_in(own_key, 6), position), (shards_of,), jnp.float32, low / len(cuts), top_value / len(cuts))
        return jnp.repeat(jnp.exp(draws), dims[position] // shards_of).reshape((-1,) + (1,) * (len(dims) - position - 1))

    gain = one(*cuts[0])
    for cut in cuts[1:]:
        gain = gain * one(*cut)
    return gain


def setup_inputs(seed: int = 0) -> dict:
    arg_keys = jax.random.split(jax.random.key(seed), 6)
    return {
        "direct_snapshots": draw_direct_snapshots(jax.random.fold_in(arg_keys[5], 71), 0),
        "adjoint_snapshots": draw_adjoint_snapshots(jax.random.fold_in(arg_keys[5], 71), 0),
        "quad_weight": jnp.clip(jnp.exp(math.log(2.0) - 1.3862944 * jax.random.uniform(arg_keys[2], (NX, NR), jnp.float32) ** level_of(arg_keys[2], (NX, NR), ((0, 8),), -0.2, 0.2)), 0.5, 2.0),
        "mean_velocity": jnp.clip(0.2 + 1 * jax.random.uniform(arg_keys[3], (NX, NR), jnp.float32) ** level_of(arg_keys[3], (NX, NR), ((0, 8),), -0.2, 0.2), 0.2, 1.2),
        "diffusivity": jnp.clip(jnp.exp(math.log(0.5) - 2.3025851 * jax.random.uniform(arg_keys[4], (NX, NR), jnp.float32) ** level_of(arg_keys[4], (NX, NR), ((0, 8),), -0.2, 0.2)), 0.05, 0.5),
    }


epsilon = 1e-06

def dft_tables(count):
    wave_index = jnp.arange(count, dtype=jnp.int32) - count // 2
    angle_index = jnp.arange(count, dtype=jnp.int32)
    residues = wave_index[:, None] * angle_index[None, :] % count
    phases = 2.0 * math.pi * residues.astype(jnp.float32) / count
    scaling = 1.0 / math.sqrt(count)
    return ((jnp.cos(phases) * scaling).astype(jnp.bfloat16), (jnp.sin(phases) * scaling).astype(jnp.bfloat16))

def combine_parts(cos_part, sin_part, half):
    real_part = cos_part[..., :half] + sin_part[..., half:]
    imag_part = cos_part[..., half:] - sin_part[..., :half]
    return jnp.concatenate([real_part, imag_part], axis=-1).astype(jnp.bfloat16)

def transform(snapshots, cos_table, sin_table):
    flattened = snapshots.reshape(NT, -1)
    cos_part = jnp.dot(cos_table, flattened, preferred_element_type=jnp.float32).reshape(snapshots.shape)
    sin_part = jnp.dot(sin_table, flattened, preferred_element_type=jnp.float32).reshape(snapshots.shape)
    return combine_parts(cos_part, sin_part, S)

def complex_blocks(product, half):
    upper_rows = product[..., :half, :]
    lower_rows = product[..., half:, :]
    pieces = []
    for offset in (0, 2 * half):
        pieces.append(upper_rows[..., offset:offset + half] + lower_rows[..., offset + half:offset + 2 * half])
        pieces.append(upper_rows[..., offset + half:offset + 2 * half] - lower_rows[..., offset:offset + half])
    return jnp.concatenate(pieces, axis=-1)

def apply_operator(mode_field, velocity, diffusion, wavenumber):
    field_f32 = mode_field.astype(jnp.float32)
    padded = jnp.pad(field_f32, ((1, 1), (1, 1), (0, 0)))
    forward = padded[2:, 1:-1]
    behind = padded[:-2, 1:-1]
    outward = padded[1:-1, 2:]
    inward = padded[1:-1, :-2]
    radius = 0.25 + (jnp.arange(NR, dtype=jnp.float32) + 0.5) / NR
    azimuthal = (wavenumber / radius) ** 2
    result = -velocity[..., None] * (forward - behind) * 0.5 + diffusion[..., None] * (forward + behind + outward + inward - 4.0 * field_f32 - azimuthal[None, :, None] * field_f32)
    return result.astype(jnp.bfloat16)

def reference(direct_snapshots, adjoint_snapshots, quad_weight, mean_velocity, diffusivity):
    cos_table, sin_table = dft_tables(NT)
    direct_modes = transform(direct_snapshots, cos_table, sin_table)
    adjoint_modes = transform(adjoint_snapshots, cos_table, sin_table)
    norm_factor = 1.0 / math.sqrt(NX * NR)
    plane_weight = quad_weight * norm_factor
    wavenumbers = (jnp.arange(NT, dtype=jnp.int32) - NT // 2).astype(jnp.float32) / NT

    def per_wave(inputs):
        direct_mode, adjoint_mode, wavenumber = inputs
        image = apply_operator(direct_mode, mean_velocity, diffusivity, wavenumber)
        weighted = (adjoint_mode.astype(jnp.float32) * plane_weight[..., None]).astype(jnp.bfloat16)
        left_side = weighted.reshape(-1, 2 * S)
        right_side = jnp.concatenate([direct_mode, image], axis=-1).reshape(-1, 4 * S)
        product = jnp.dot(left_side.T, right_side, preferred_element_type=jnp.float32)
        return complex_blocks(product, S)
    gram_terms = lax.map(per_wave, (direct_modes, adjoint_modes, wavenumbers))
    energy = lax.optimization_barrier(jnp.sum(gram_terms[..., :2 * S] ** 2, axis=(1, 2)))
    mean_sq = energy / (2.0 * S * S)
    scales = lax.rsqrt(mean_sq + epsilon)
    hankel_gram = (gram_terms[..., :2 * S] * scales[:, None, None]).reshape(NT * S, 2 * S)
    reduced_operator = (gram_terms[..., 2 * S:] * scales[:, None, None]).reshape(NT * S, 2 * S)
    hankel_norm = jnp.sqrt(mean_sq)
    return (hankel_gram, reduced_operator, hankel_norm)
```

```python
import math

import jax
import jax.numpy as jnp
from jax import lax
from jax.sharding import PartitionSpec as P

epsilon = 1e-06


def padded_2(cells, sides, width):
    for axis, dim in sides:
        count = lax.axis_size(axis)
        ends = count - 1
        head = lax.slice_in_dim(cells, 0, width, axis=dim)
        tail = lax.slice_in_dim(cells, cells.shape[dim] - width, cells.shape[dim], axis=dim)
        cells = jnp.concatenate(
            [
                lax.ppermute(tail, axis, [(i, (i + 1) % count) for i in range(ends)]),
                cells,
                lax.ppermute(head, axis, [((i + 1) % count, i) for i in range(ends)]),
            ],
            axis=dim,
        )
    return cells


def dft_tables(count):
    wave_index = jnp.arange(count, dtype=jnp.int32) - count // 2
    angle_index = jnp.arange(count, dtype=jnp.int32)
    residues = wave_index[:, None] * angle_index[None, :] % count
    phases = 2.0 * math.pi * residues.astype(jnp.float32) / count
    scaling = 1.0 / math.sqrt(count)
    return (
        (jnp.cos(phases) * scaling).astype(jnp.bfloat16),
        (jnp.sin(phases) * scaling).astype(jnp.bfloat16),
    )


def combine_parts(cos_part, sin_part, half):
    real_part = cos_part[..., :half] + sin_part[..., half:]
    imag_part = cos_part[..., half:] - sin_part[..., :half]
    return jnp.concatenate([real_part, imag_part], axis=-1).astype(jnp.bfloat16)


def complex_blocks(product, half):
    upper_rows = product[..., :half, :]
    lower_rows = product[..., half:, :]
    pieces = []
    for offset in (0, 2 * half):
        pieces.append(
            upper_rows[..., offset : offset + half]
            + lower_rows[..., offset + half : offset + 2 * half]
        )
        pieces.append(
            upper_rows[..., offset + half : offset + 2 * half]
            - lower_rows[..., offset : offset + half]
        )
    return jnp.concatenate(pieces, axis=-1)


def local(direct_snapshots, adjoint_snapshots, quad_weight, mean_velocity, diffusivity):
    local_angles, axial_cells, radial_cells, columns = direct_snapshots.shape
    snap_count = columns // 2
    total_angles = local_angles * lax.axis_size("ka")
    cos_table, sin_table = dft_tables(total_angles)
    first_wave = lax.axis_index("ka") * local_angles
    moved_direct, moved_adjoint = (
        lax.all_to_all(direct_snapshots, "ka", split_axis=2, concat_axis=0, tiled=True),
        lax.all_to_all(adjoint_snapshots, "ka", split_axis=2, concat_axis=0, tiled=True),
    )

    def transform_all(snapshots):
        flattened = snapshots.reshape(total_angles, -1)
        cos_part = jnp.dot(cos_table, flattened, preferred_element_type=jnp.float32).reshape(
            snapshots.shape
        )
        sin_part = jnp.dot(sin_table, flattened, preferred_element_type=jnp.float32).reshape(
            snapshots.shape
        )
        return combine_parts(cos_part, sin_part, snap_count)

    direct_modes, adjoint_modes = (
        lax.all_to_all(transform_all(moved_direct), "ka", split_axis=0, concat_axis=2, tiled=True),
        lax.all_to_all(transform_all(moved_adjoint), "ka", split_axis=0, concat_axis=2, tiled=True),
    )
    padded = padded_2(direct_modes, (("gx", 1),), 1)
    field_f32 = direct_modes.astype(jnp.float32)
    forward = padded[:, 2:].astype(jnp.float32)
    behind = padded[:, :-2].astype(jnp.float32)
    radial_pad = jnp.pad(field_f32, ((0, 0), (0, 0), (1, 1), (0, 0)))
    outward = radial_pad[:, :, 2:]
    inward = radial_pad[:, :, :-2]
    radius = 0.25 + (jnp.arange(radial_cells, dtype=jnp.float32) + 0.5) / radial_cells
    wavenumber = (
        first_wave + jnp.arange(local_angles, dtype=jnp.int32) - total_angles // 2
    ).astype(jnp.float32) / total_angles
    azimuthal = (wavenumber[:, None] / radius[None, :]) ** 2
    velocity = mean_velocity[None, :, :, None]
    diffusion = diffusivity[None, :, :, None]
    image = (
        -velocity * (forward - behind) * 0.5
        + diffusion
        * (
            forward
            + behind
            + outward
            + inward
            - 4.0 * field_f32
            - azimuthal[:, None, :, None] * field_f32
        )
    ).astype(jnp.bfloat16)
    norm_factor = 1.0 / math.sqrt(axial_cells * lax.axis_size("gx") * radial_cells)
    plane_weight = quad_weight * norm_factor
    weighted = (adjoint_modes.astype(jnp.float32) * plane_weight[None, :, :, None]).astype(
        jnp.bfloat16
    )
    right_side = jnp.concatenate([direct_modes, image], axis=-1)
    product = jnp.einsum(
        "kpa,kpb->kab",
        weighted.reshape(local_angles, -1, columns),
        right_side.reshape(local_angles, -1, 2 * columns),
        preferred_element_type=jnp.float32,
    )
    gram_terms = complex_blocks(product, snap_count).reshape(local_angles * snap_count, 2 * columns)
    row_count = gram_terms.shape[0] // lax.axis_size("gx")
    row_index = lax.axis_index("gx") * row_count + jnp.arange(row_count, dtype=jnp.int32)
    owner = row_index // snap_count
    selector = (owner[:, None] == jnp.arange(local_angles, dtype=jnp.int32)[None, :]).astype(
        jnp.float32
    )
    own_rows = lax.psum_scatter(gram_terms, "gx", scatter_dimension=0, tiled=True)
    row_energy = jnp.sum(own_rows[:, :columns] ** 2, axis=1)
    energy = lax.psum(jnp.sum(selector * row_energy[:, None], axis=0), "gx")
    mean_sq = energy / (2.0 * snap_count * snap_count)
    row_scale = jnp.sum(selector * lax.rsqrt(mean_sq + epsilon)[None, :], axis=1)
    hankel_gram = own_rows[:, :columns] * row_scale[:, None]
    reduced_operator = own_rows[:, columns:] * row_scale[:, None]
    hankel_norm = jnp.sqrt(mean_sq)
    return (hankel_gram, reduced_operator, hankel_norm)


def permuted_tables(count, wave_index):
    angle_index = jnp.arange(count, dtype=jnp.int32)
    residues = wave_index[:, None] * angle_index[None, :] % count
    phases = 2.0 * math.pi * residues.astype(jnp.float32) / count
    scaling = 1.0 / math.sqrt(count)
    return (
        (jnp.cos(phases) * scaling).astype(jnp.bfloat16),
        (jnp.sin(phases) * scaling).astype(jnp.bfloat16),
    )


def by_wavenumber(direct_snapshots, adjoint_snapshots, quad_weight, mean_velocity, diffusivity):
    local_angles, axial_cells, radial_cells, columns = direct_snapshots.shape
    snap_count = columns // 2
    band_count = lax.axis_size("ka")
    axial_count = lax.axis_size("gx")
    total_angles = local_angles * band_count
    devices = band_count * axial_count
    waves_here = total_angles // devices
    points = axial_cells * radial_cells
    band = points // band_count
    band_index = lax.axis_index("ka")
    axial_index = lax.axis_index("gx")

    row = jnp.arange(total_angles, dtype=jnp.int32)
    chunk = row // waves_here
    owner = (chunk % band_count) * axial_count + chunk // band_count
    wave_index = owner * waves_here + row % waves_here - total_angles // 2
    cos_table, sin_table = permuted_tables(total_angles, wave_index)

    fields = jnp.stack([mean_velocity, diffusivity])
    fields = lax.all_gather(fields, "gx", axis=1, tiled=True)

    def gather_angles(snapshots):
        flat = snapshots.reshape(local_angles, points, columns)
        return lax.all_to_all(flat, "ka", split_axis=1, concat_axis=0, tiled=True)

    def transform_all(moved):
        flattened = moved.reshape(total_angles, -1)
        cos_part = jnp.dot(cos_table, flattened, preferred_element_type=jnp.float32).reshape(
            moved.shape
        )
        sin_part = jnp.dot(sin_table, flattened, preferred_element_type=jnp.float32).reshape(
            moved.shape
        )
        return combine_parts(cos_part, sin_part, snap_count)

    def scatter_waves(modes):
        return lax.all_to_all(modes, ("gx", "ka"), split_axis=0, concat_axis=1, tiled=True)

    direct_modes = scatter_waves(transform_all(gather_angles(direct_snapshots)))
    norm_factor = 1.0 / math.sqrt(axial_cells * axial_count * radial_cells)
    plane_weight = (quad_weight * norm_factor).reshape(points)
    band_weight = lax.dynamic_slice_in_dim(plane_weight, band_index * band, band)
    adjoint_modes = transform_all(gather_angles(adjoint_snapshots))
    weighted = (adjoint_modes.astype(jnp.float32) * band_weight[None, :, None]).astype(jnp.bfloat16)
    weighted = scatter_waves(weighted)

    all_axial = axial_cells * axial_count
    field = direct_modes.reshape(waves_here, all_axial, radial_cells, columns)
    field_f32 = field.astype(jnp.float32)
    padded = jnp.pad(field_f32, ((0, 0), (1, 1), (1, 1), (0, 0)))
    forward = padded[:, 2:, 1:-1]
    behind = padded[:, :-2, 1:-1]
    outward = padded[:, 1:-1, 2:]
    inward = padded[:, 1:-1, :-2]
    radius = 0.25 + (jnp.arange(radial_cells, dtype=jnp.float32) + 0.5) / radial_cells
    first_wave = (band_index * axial_count + axial_index) * waves_here
    wavenumber = (
        first_wave + jnp.arange(waves_here, dtype=jnp.int32) - total_angles // 2
    ).astype(jnp.float32) / total_angles
    azimuthal = (wavenumber[:, None] / radius[None, :]) ** 2
    velocity = fields[0][None, :, :, None]
    diffusion = fields[1][None, :, :, None]
    image = (
        -velocity * (forward - behind) * 0.5
        + diffusion
        * (
            forward
            + behind
            + outward
            + inward
            - 4.0 * field_f32
            - azimuthal[:, None, :, None] * field_f32
        )
    ).astype(jnp.bfloat16)
    right_side = jnp.concatenate([field, image], axis=-1)
    product = jnp.einsum(
        "kpa,kpb->kab",
        weighted,
        right_side.reshape(waves_here, -1, 2 * columns),
        preferred_element_type=jnp.float32,
    )
    gram_terms = complex_blocks(product, snap_count)
    energy = jnp.sum(gram_terms[..., :columns] ** 2, axis=(1, 2))
    mean_sq = energy / (2.0 * snap_count * snap_count)
    scales = lax.rsqrt(mean_sq + epsilon)
    hankel_gram = (gram_terms[..., :columns] * scales[:, None, None]).reshape(-1, columns)
    reduced_operator = (gram_terms[..., columns:] * scales[:, None, None]).reshape(-1, columns)
    hankel_norm = lax.all_gather(jnp.sqrt(mean_sq), "gx", tiled=True)
    return (hankel_gram, reduced_operator, hankel_norm)


def dispatch(direct_snapshots, *rest):
    local_angles, axial_cells, radial_cells, _ = direct_snapshots.shape
    band_count = lax.axis_size("ka")
    devices = band_count * lax.axis_size("gx")
    whole_waves = (local_angles * band_count) % devices == 0
    even_bands = (axial_cells * radial_cells) % band_count == 0
    body = by_wavenumber if whole_waves and even_bands else local
    return body(direct_snapshots, *rest)


def solution(mesh):
    placed = (
        P("ka", "gx", None, None),
        P("ka", "gx", None, None),
        P("gx", None),
        P("gx", None),
        P("gx", None),
    )
    return jax.shard_map(
        dispatch,
        mesh=mesh,
        in_specs=placed,
        out_specs=(P(("ka", "gx"), None), P(("ka", "gx"), None), P("ka")),
        check_vma=False,
    )
```

```python
import math

import jax
import jax.numpy as jnp
from jax import lax
from jax.sharding import PartitionSpec as P

epsilon = 1e-06


def padded_2(cells, sides, width):
    for axis, dim in sides:
        count = lax.axis_size(axis)
        ends = count - 1
        head = lax.slice_in_dim(cells, 0, width, axis=dim)
        tail = lax.slice_in_dim(cells, cells.shape[dim] - width, cells.shape[dim], axis=dim)
        cells = jnp.concatenate(
            [
                lax.ppermute(tail, axis, [(i, (i + 1) % count) for i in range(ends)]),
                cells,
                lax.ppermute(head, axis, [((i + 1) % count, i) for i in range(ends)]),
            ],
            axis=dim,
        )
    return cells


def dft_tables(count):
    wave_index = jnp.arange(count, dtype=jnp.int32) - count // 2
    angle_index = jnp.arange(count, dtype=jnp.int32)
    residues = wave_index[:, None] * angle_index[None, :] % count
    phases = 2.0 * math.pi * residues.astype(jnp.float32) / count
    scaling = 1.0 / math.sqrt(count)
    return (
        (jnp.cos(phases) * scaling).astype(jnp.bfloat16),
        (jnp.sin(phases) * scaling).astype(jnp.bfloat16),
    )


def combine_parts(cos_part, sin_part, half):
    real_part = cos_part[..., :half] + sin_part[..., half:]
    imag_part = cos_part[..., half:] - sin_part[..., :half]
    return jnp.concatenate([real_part, imag_part], axis=-1).astype(jnp.bfloat16)


def complex_blocks(product, half):
    upper_rows = product[..., :half, :]
    lower_rows = product[..., half:, :]
    pieces = []
    for offset in (0, 2 * half):
        pieces.append(
            upper_rows[..., offset : offset + half]
            + lower_rows[..., offset + half : offset + 2 * half]
        )
        pieces.append(
            upper_rows[..., offset + half : offset + 2 * half]
            - lower_rows[..., offset : offset + half]
        )
    return jnp.concatenate(pieces, axis=-1)


def local(direct_snapshots, adjoint_snapshots, quad_weight, mean_velocity, diffusivity):
    local_angles, axial_cells, radial_cells, columns = direct_snapshots.shape
    snap_count = columns // 2
    total_angles = local_angles * lax.axis_size("ka")
    cos_table, sin_table = dft_tables(total_angles)
    first_wave = lax.axis_index("ka") * local_angles
    moved_direct, moved_adjoint = (
        lax.all_to_all(direct_snapshots, "ka", split_axis=2, concat_axis=0, tiled=True),
        lax.all_to_all(adjoint_snapshots, "ka", split_axis=2, concat_axis=0, tiled=True),
    )

    def transform_all(snapshots):
        flattened = snapshots.reshape(total_angles, -1)
        cos_part = jnp.dot(cos_table, flattened, preferred_element_type=jnp.float32).reshape(
            snapshots.shape
        )
        sin_part = jnp.dot(sin_table, flattened, preferred_element_type=jnp.float32).reshape(
            snapshots.shape
        )
        return combine_parts(cos_part, sin_part, snap_count)

    direct_modes, adjoint_modes = (
        lax.all_to_all(transform_all(moved_direct), "ka", split_axis=0, concat_axis=2, tiled=True),
        lax.all_to_all(transform_all(moved_adjoint), "ka", split_axis=0, concat_axis=2, tiled=True),
    )
    padded = padded_2(direct_modes, (("gx", 1),), 1)
    field_f32 = direct_modes.astype(jnp.float32)
    forward = padded[:, 2:].astype(jnp.float32)
    behind = padded[:, :-2].astype(jnp.float32)
    radial_pad = jnp.pad(field_f32, ((0, 0), (0, 0), (1, 1), (0, 0)))
    outward = radial_pad[:, :, 2:]
    inward = radial_pad[:, :, :-2]
    radius = 0.25 + (jnp.arange(radial_cells, dtype=jnp.float32) + 0.5) / radial_cells
    wavenumber = (
        first_wave + jnp.arange(local_angles, dtype=jnp.int32) - total_angles // 2
    ).astype(jnp.float32) / total_angles
    azimuthal = (wavenumber[:, None] / radius[None, :]) ** 2
    velocity = mean_velocity[None, :, :, None]
    diffusion = diffusivity[None, :, :, None]
    image = (
        -velocity * (forward - behind) * 0.5
        + diffusion
        * (
            forward
            + behind
            + outward
            + inward
            - 4.0 * field_f32
            - azimuthal[:, None, :, None] * field_f32
        )
    ).astype(jnp.bfloat16)
    norm_factor = 1.0 / math.sqrt(axial_cells * lax.axis_size("gx") * radial_cells)
    plane_weight = quad_weight * norm_factor
    weighted = (adjoint_modes.astype(jnp.float32) * plane_weight[None, :, :, None]).astype(
        jnp.bfloat16
    )
    right_side = jnp.concatenate([direct_modes, image], axis=-1)
    product = jnp.einsum(
        "kpa,kpb->kab",
        weighted.reshape(local_angles, -1, columns),
        right_side.reshape(local_angles, -1, 2 * columns),
        preferred_element_type=jnp.float32,
    )
    gram_terms = complex_blocks(product, snap_count).reshape(local_angles * snap_count, 2 * columns)
    row_count = gram_terms.shape[0] // lax.axis_size("gx")
    row_index = lax.axis_index("gx") * row_count + jnp.arange(row_count, dtype=jnp.int32)
    owner = row_index // snap_count
    selector = (owner[:, None] == jnp.arange(local_angles, dtype=jnp.int32)[None, :]).astype(
        jnp.float32
    )
    own_rows = lax.psum_scatter(gram_terms, "gx", scatter_dimension=0, tiled=True)
    row_energy = jnp.sum(own_rows[:, :columns] ** 2, axis=1)
    energy = lax.psum(jnp.sum(selector * row_energy[:, None], axis=0), "gx")
    mean_sq = energy / (2.0 * snap_count * snap_count)
    row_scale = jnp.sum(selector * lax.rsqrt(mean_sq + epsilon)[None, :], axis=1)
    hankel_gram = own_rows[:, :columns] * row_scale[:, None]
    reduced_operator = own_rows[:, columns:] * row_scale[:, None]
    hankel_norm = jnp.sqrt(mean_sq)
    return (hankel_gram, reduced_operator, hankel_norm)


def gather_small(values, axis):
    count = lax.axis_size(axis)
    copies = jnp.broadcast_to(values[None], (count,) + values.shape)
    return lax.all_to_all(copies, axis, split_axis=0, concat_axis=0, tiled=True)


def permuted_tables(count, wave_index):
    angle_index = jnp.arange(count, dtype=jnp.int32)
    residues = wave_index[:, None] * angle_index[None, :] % count
    phases = 2.0 * math.pi * residues.astype(jnp.float32) / count
    scaling = 1.0 / math.sqrt(count)
    return (
        (jnp.cos(phases) * scaling).astype(jnp.bfloat16),
        (jnp.sin(phases) * scaling).astype(jnp.bfloat16),
    )


def by_wavenumber(direct_snapshots, adjoint_snapshots, quad_weight, mean_velocity, diffusivity):
    local_angles, axial_cells, radial_cells, columns = direct_snapshots.shape
    snap_count = columns // 2
    band_count = lax.axis_size("ka")
    axial_count = lax.axis_size("gx")
    total_angles = local_angles * band_count
    devices = band_count * axial_count
    waves_here = total_angles // devices
    points = axial_cells * radial_cells
    band = points // band_count
    band_index = lax.axis_index("ka")
    axial_index = lax.axis_index("gx")

    row = jnp.arange(total_angles, dtype=jnp.int32)
    chunk = row // waves_here
    owner = (chunk % band_count) * axial_count + chunk // band_count
    wave_index = owner * waves_here + row % waves_here - total_angles // 2
    cos_table, sin_table = permuted_tables(total_angles, wave_index)

    fields = gather_small(jnp.stack([mean_velocity, diffusivity]), "gx")
    fields = jnp.moveaxis(fields, 0, 1).reshape(2, axial_count * axial_cells, radial_cells)

    def gather_angles(snapshots):
        flat = snapshots.reshape(local_angles, points, columns)
        return lax.all_to_all(flat, "ka", split_axis=1, concat_axis=0, tiled=True)

    def transform_all(moved):
        flattened = moved.reshape(total_angles, -1)
        cos_part = jnp.dot(cos_table, flattened, preferred_element_type=jnp.float32).reshape(
            moved.shape
        )
        sin_part = jnp.dot(sin_table, flattened, preferred_element_type=jnp.float32).reshape(
            moved.shape
        )
        return combine_parts(cos_part, sin_part, snap_count)

    def scatter_waves(modes):
        return lax.all_to_all(modes, ("gx", "ka"), split_axis=0, concat_axis=1, tiled=True)

    direct_modes = scatter_waves(transform_all(gather_angles(direct_snapshots)))
    norm_factor = 1.0 / math.sqrt(axial_cells * axial_count * radial_cells)
    plane_weight = (quad_weight * norm_factor).reshape(points)
    band_weight = lax.dynamic_slice_in_dim(plane_weight, band_index * band, band)
    adjoint_modes = transform_all(gather_angles(adjoint_snapshots))
    weighted = (adjoint_modes.astype(jnp.float32) * band_weight[None, :, None]).astype(jnp.bfloat16)
    weighted = scatter_waves(weighted)

    all_axial = axial_cells * axial_count
    field = direct_modes.reshape(waves_here, all_axial, radial_cells, columns)
    field_f32 = field.astype(jnp.float32)
    padded = jnp.pad(field_f32, ((0, 0), (1, 1), (1, 1), (0, 0)))
    forward = padded[:, 2:, 1:-1]
    behind = padded[:, :-2, 1:-1]
    outward = padded[:, 1:-1, 2:]
    inward = padded[:, 1:-1, :-2]
    radius = 0.25 + (jnp.arange(radial_cells, dtype=jnp.float32) + 0.5) / radial_cells
    first_wave = (band_index * axial_count + axial_index) * waves_here
    wavenumber = (
        first_wave + jnp.arange(waves_here, dtype=jnp.int32) - total_angles // 2
    ).astype(jnp.float32) / total_angles
    azimuthal = (wavenumber[:, None] / radius[None, :]) ** 2
    velocity = fields[0][None, :, :, None]
    diffusion = fields[1][None, :, :, None]
    image = (
        -velocity * (forward - behind) * 0.5
        + diffusion
        * (
            forward
            + behind
            + outward
            + inward
            - 4.0 * field_f32
            - azimuthal[:, None, :, None] * field_f32
        )
    ).astype(jnp.bfloat16)
    right_side = jnp.concatenate([field, image], axis=-1)
    product = jnp.einsum(
        "kpa,kpb->kab",
        weighted,
        right_side.reshape(waves_here, -1, 2 * columns),
        preferred_element_type=jnp.float32,
    )
    gram_terms = complex_blocks(product, snap_count)
    energy = jnp.sum(gram_terms[..., :columns] ** 2, axis=(1, 2))
    mean_sq = energy / (2.0 * snap_count * snap_count)
    scales = lax.rsqrt(mean_sq + epsilon)
    hankel_gram = (gram_terms[..., :columns] * scales[:, None, None]).reshape(-1, columns)
    reduced_operator = (gram_terms[..., columns:] * scales[:, None, None]).reshape(-1, columns)
    hankel_norm = gather_small(jnp.sqrt(mean_sq), "gx").reshape(-1)
    return (hankel_gram, reduced_operator, hankel_norm)


def dispatch(direct_snapshots, *rest):
    local_angles, axial_cells, radial_cells, _ = direct_snapshots.shape
    band_count = lax.axis_size("ka")
    devices = band_count * lax.axis_size("gx")
    whole_waves = (local_angles * band_count) % devices == 0
    even_bands = (axial_cells * radial_cells) % band_count == 0
    body = by_wavenumber if whole_waves and even_bands else local
    return body(direct_snapshots, *rest)


def solution(mesh):
    placed = (
        P("ka", "gx", None, None),
        P("ka", "gx", None, None),
        P("gx", None),
        P("gx", None),
        P("gx", None),
    )
    return jax.shard_map(
        dispatch,
        mesh=mesh,
        in_specs=placed,
        out_specs=(P(("ka", "gx"), None), P(("ka", "gx"), None), P("ka")),
        check_vma=False,
    )
```

```python
import math

import jax
import jax.numpy as jnp
from jax import lax
from jax.sharding import PartitionSpec as P

epsilon = 1e-06


def padded_2(cells, sides, width):
    for axis, dim in sides:
        count = lax.axis_size(axis)
        ends = count - 1
        head = lax.slice_in_dim(cells, 0, width, axis=dim)
        tail = lax.slice_in_dim(cells, cells.shape[dim] - width, cells.shape[dim], axis=dim)
        cells = jnp.concatenate(
            [
                lax.ppermute(tail, axis, [(i, (i + 1) % count) for i in range(ends)]),
                cells,
                lax.ppermute(head, axis, [((i + 1) % count, i) for i in range(ends)]),
            ],
            axis=dim,
        )
    return cells


def dft_tables(count):
    wave_index = jnp.arange(count, dtype=jnp.int32) - count // 2
    angle_index = jnp.arange(count, dtype=jnp.int32)
    residues = wave_index[:, None] * angle_index[None, :] % count
    phases = 2.0 * math.pi * residues.astype(jnp.float32) / count
    scaling = 1.0 / math.sqrt(count)
    return (
        (jnp.cos(phases) * scaling).astype(jnp.bfloat16),
        (jnp.sin(phases) * scaling).astype(jnp.bfloat16),
    )


def combine_parts(cos_part, sin_part, half):
    real_part = cos_part[..., :half] + sin_part[..., half:]
    imag_part = cos_part[..., half:] - sin_part[..., :half]
    return jnp.concatenate([real_part, imag_part], axis=-1).astype(jnp.bfloat16)


def complex_blocks(product, half):
    upper_rows = product[..., :half, :]
    lower_rows = product[..., half:, :]
    pieces = []
    for offset in (0, 2 * half):
        pieces.append(
            upper_rows[..., offset : offset + half]
            + lower_rows[..., offset + half : offset + 2 * half]
        )
        pieces.append(
            upper_rows[..., offset + half : offset + 2 * half]
            - lower_rows[..., offset : offset + half]
        )
    return jnp.concatenate(pieces, axis=-1)


def local(direct_snapshots, adjoint_snapshots, quad_weight, mean_velocity, diffusivity):
    local_angles, axial_cells, radial_cells, columns = direct_snapshots.shape
    snap_count = columns // 2
    total_angles = local_angles * lax.axis_size("ka")
    cos_table, sin_table = dft_tables(total_angles)
    first_wave = lax.axis_index("ka") * local_angles
    moved_direct, moved_adjoint = (
        lax.all_to_all(direct_snapshots, "ka", split_axis=2, concat_axis=0, tiled=True),
        lax.all_to_all(adjoint_snapshots, "ka", split_axis=2, concat_axis=0, tiled=True),
    )

    def transform_all(snapshots):
        flattened = snapshots.reshape(total_angles, -1)
        cos_part = jnp.dot(cos_table, flattened, preferred_element_type=jnp.float32).reshape(
            snapshots.shape
        )
        sin_part = jnp.dot(sin_table, flattened, preferred_element_type=jnp.float32).reshape(
            snapshots.shape
        )
        return combine_parts(cos_part, sin_part, snap_count)

    direct_modes, adjoint_modes = (
        lax.all_to_all(transform_all(moved_direct), "ka", split_axis=0, concat_axis=2, tiled=True),
        lax.all_to_all(transform_all(moved_adjoint), "ka", split_axis=0, concat_axis=2, tiled=True),
    )
    padded = padded_2(direct_modes, (("gx", 1),), 1)
    field_f32 = direct_modes.astype(jnp.float32)
    forward = padded[:, 2:].astype(jnp.float32)
    behind = padded[:, :-2].astype(jnp.float32)
    radial_pad = jnp.pad(field_f32, ((0, 0), (0, 0), (1, 1), (0, 0)))
    outward = radial_pad[:, :, 2:]
    inward = radial_pad[:, :, :-2]
    radius = 0.25 + (jnp.arange(radial_cells, dtype=jnp.float32) + 0.5) / radial_cells
    wavenumber = (
        first_wave + jnp.arange(local_angles, dtype=jnp.int32) - total_angles // 2
    ).astype(jnp.float32) / total_angles
    azimuthal = (wavenumber[:, None] / radius[None, :]) ** 2
    velocity = mean_velocity[None, :, :, None]
    diffusion = diffusivity[None, :, :, None]
    image = (
        -velocity * (forward - behind) * 0.5
        + diffusion
        * (
            forward
            + behind
            + outward
            + inward
            - 4.0 * field_f32
            - azimuthal[:, None, :, None] * field_f32
        )
    ).astype(jnp.bfloat16)
    norm_factor = 1.0 / math.sqrt(axial_cells * lax.axis_size("gx") * radial_cells)
    plane_weight = quad_weight * norm_factor
    weighted = (adjoint_modes.astype(jnp.float32) * plane_weight[None, :, :, None]).astype(
        jnp.bfloat16
    )
    right_side = jnp.concatenate([direct_modes, image], axis=-1)
    product = jnp.einsum(
        "kpa,kpb->kab",
        weighted.reshape(local_angles, -1, columns),
        right_side.reshape(local_angles, -1, 2 * columns),
        preferred_element_type=jnp.float32,
    )
    gram_terms = complex_blocks(product, snap_count).reshape(local_angles * snap_count, 2 * columns)
    row_count = gram_terms.shape[0] // lax.axis_size("gx")
    row_index = lax.axis_index("gx") * row_count + jnp.arange(row_count, dtype=jnp.int32)
    owner = row_index // snap_count
    selector = (owner[:, None] == jnp.arange(local_angles, dtype=jnp.int32)[None, :]).astype(
        jnp.float32
    )
    own_rows = lax.psum_scatter(gram_terms, "gx", scatter_dimension=0, tiled=True)
    row_energy = jnp.sum(own_rows[:, :columns] ** 2, axis=1)
    energy = lax.psum(jnp.sum(selector * row_energy[:, None], axis=0), "gx")
    mean_sq = energy / (2.0 * snap_count * snap_count)
    row_scale = jnp.sum(selector * lax.rsqrt(mean_sq + epsilon)[None, :], axis=1)
    hankel_gram = own_rows[:, :columns] * row_scale[:, None]
    reduced_operator = own_rows[:, columns:] * row_scale[:, None]
    hankel_norm = jnp.sqrt(mean_sq)
    return (hankel_gram, reduced_operator, hankel_norm)


def gather_small(values, axis):
    count = lax.axis_size(axis)
    copies = jnp.broadcast_to(values[None], (count,) + values.shape)
    return lax.all_to_all(copies, axis, split_axis=0, concat_axis=0, tiled=True)


def permuted_tables(count, wave_index):
    angle_index = jnp.arange(count, dtype=jnp.int32)
    residues = wave_index[:, None] * angle_index[None, :] % count
    phases = 2.0 * math.pi * residues.astype(jnp.float32) / count
    scaling = 1.0 / math.sqrt(count)
    return (
        (jnp.cos(phases) * scaling).astype(jnp.bfloat16),
        (jnp.sin(phases) * scaling).astype(jnp.bfloat16),
    )


def by_band(direct_snapshots, adjoint_snapshots, quad_weight, mean_velocity, diffusivity):
    local_angles, axial_cells, radial_cells, columns = direct_snapshots.shape
    snap_count = columns // 2
    band_count = lax.axis_size("ka")
    axial_count = lax.axis_size("gx")
    total_angles = local_angles * band_count
    chunk_waves = total_angles // axial_count
    waves_here = chunk_waves // band_count
    band = radial_cells // band_count
    band_index = lax.axis_index("ka")
    axial_index = lax.axis_index("gx")
    all_axial = axial_cells * axial_count

    row = jnp.arange(total_angles, dtype=jnp.int32)
    sub = (row % chunk_waves) // waves_here
    owner = sub * axial_count + row // chunk_waves
    wave_index = owner * waves_here + row % waves_here - total_angles // 2
    cos_table, sin_table = permuted_tables(total_angles, wave_index)

    fields = gather_small(jnp.stack([mean_velocity, diffusivity]), "gx")
    fields = jnp.moveaxis(fields, 0, 1).reshape(2, all_axial, radial_cells)
    fields = lax.dynamic_slice_in_dim(fields, band_index * band, band, axis=2)

    def gather_angles(snapshots):
        split = snapshots.reshape(local_angles, axial_cells, band_count, band, columns)
        moved = lax.all_to_all(split, "ka", split_axis=2, concat_axis=0, tiled=True)
        return moved.reshape(total_angles, axial_cells, band, columns)

    def transform_all(moved):
        flattened = moved.reshape(total_angles, -1)
        cos_part = jnp.dot(cos_table, flattened, preferred_element_type=jnp.float32).reshape(
            moved.shape
        )
        sin_part = jnp.dot(sin_table, flattened, preferred_element_type=jnp.float32).reshape(
            moved.shape
        )
        return combine_parts(cos_part, sin_part, snap_count)

    def gather_axial(modes):
        return lax.all_to_all(modes, "gx", split_axis=0, concat_axis=1, tiled=True)

    field = gather_axial(transform_all(gather_angles(direct_snapshots)))
    norm_factor = 1.0 / math.sqrt(all_axial * radial_cells)
    plane_weight = lax.dynamic_slice_in_dim(quad_weight * norm_factor, band_index * band, band, axis=1)
    adjoint_modes = transform_all(gather_angles(adjoint_snapshots))
    weighted = (adjoint_modes.astype(jnp.float32) * plane_weight[None, :, :, None]).astype(
        jnp.bfloat16
    )
    weighted = gather_axial(weighted)

    field_f32 = field.astype(jnp.float32)
    radial_halo = padded_2(field, (("ka", 2),), 1).astype(jnp.float32)
    outward = radial_halo[:, :, 2:]
    inward = radial_halo[:, :, :-2]
    axial_pad = jnp.pad(field_f32, ((0, 0), (1, 1), (0, 0), (0, 0)))
    forward = axial_pad[:, 2:]
    behind = axial_pad[:, :-2]
    radial_index = (band_index * band + jnp.arange(band, dtype=jnp.int32)).astype(jnp.float32)
    radius = 0.25 + (radial_index + 0.5) / radial_cells
    local_row = jnp.arange(chunk_waves, dtype=jnp.int32)
    local_wave = (
        ((local_row // waves_here) * axial_count + axial_index) * waves_here
        + local_row % waves_here
        - total_angles // 2
    )
    wavenumber = local_wave.astype(jnp.float32) / total_angles
    azimuthal = (wavenumber[:, None] / radius[None, :]) ** 2
    velocity = fields[0][None, :, :, None]
    diffusion = fields[1][None, :, :, None]
    image = (
        -velocity * (forward - behind) * 0.5
        + diffusion
        * (
            forward
            + behind
            + outward
            + inward
            - 4.0 * field_f32
            - azimuthal[:, None, :, None] * field_f32
        )
    ).astype(jnp.bfloat16)
    right_side = jnp.concatenate([field, image], axis=-1)
    product = jnp.einsum(
        "kpa,kpb->kab",
        weighted.reshape(chunk_waves, -1, columns),
        right_side.reshape(chunk_waves, -1, 2 * columns),
        preferred_element_type=jnp.float32,
    )
    partial = complex_blocks(product, snap_count).reshape(band_count, waves_here, snap_count, 2 * columns)
    gram_terms = jnp.sum(lax.all_to_all(partial, "ka", split_axis=0, concat_axis=0, tiled=True), axis=0)
    energy = jnp.sum(gram_terms[..., :columns] ** 2, axis=(1, 2))
    mean_sq = energy / (2.0 * snap_count * snap_count)
    scales = lax.rsqrt(mean_sq + epsilon)
    hankel_gram = (gram_terms[..., :columns] * scales[:, None, None]).reshape(-1, columns)
    reduced_operator = (gram_terms[..., columns:] * scales[:, None, None]).reshape(-1, columns)
    hankel_norm = gather_small(jnp.sqrt(mean_sq), "gx").reshape(-1)
    return (hankel_gram, reduced_operator, hankel_norm)


def dispatch(direct_snapshots, *rest):
    local_angles, _, radial_cells, _ = direct_snapshots.shape
    band_count = lax.axis_size("ka")
    axial_count = lax.axis_size("gx")
    total_angles = local_angles * band_count
    whole_waves = total_angles % (axial_count * band_count) == 0
    even_bands = radial_cells % band_count == 0
    body = by_band if whole_waves and even_bands else local
    return body(direct_snapshots, *rest)


def solution(mesh):
    placed = (
        P("ka", "gx", None, None),
        P("ka", "gx", None, None),
        P("gx", None),
        P("gx", None),
        P("gx", None),
    )
    return jax.shard_map(
        dispatch,
        mesh=mesh,
        in_specs=placed,
        out_specs=(P(("ka", "gx"), None), P(("ka", "gx"), None), P("ka")),
        check_vma=False,
    )
```

```python
import math

import jax
import jax.numpy as jnp
from jax import lax
from jax.sharding import PartitionSpec as P

epsilon = 1e-06


def padded_2(cells, sides, width):
    for axis, dim in sides:
        count = lax.axis_size(axis)
        ends = count - 1
        head = lax.slice_in_dim(cells, 0, width, axis=dim)
        tail = lax.slice_in_dim(cells, cells.shape[dim] - width, cells.shape[dim], axis=dim)
        cells = jnp.concatenate(
            [
                lax.ppermute(tail, axis, [(i, (i + 1) % count) for i in range(ends)]),
                cells,
                lax.ppermute(head, axis, [((i + 1) % count, i) for i in range(ends)]),
            ],
            axis=dim,
        )
    return cells


def gather_small(values, axis):
    count = lax.axis_size(axis)
    copies = jnp.broadcast_to(values[None], (count,) + values.shape)
    return lax.all_to_all(copies, axis, split_axis=0, concat_axis=0, tiled=True)


def dft_tables(count):
    wave_index = jnp.arange(count, dtype=jnp.int32) - count // 2
    angle_index = jnp.arange(count, dtype=jnp.int32)
    residues = wave_index[:, None] * angle_index[None, :] % count
    phases = 2.0 * math.pi * residues.astype(jnp.float32) / count
    scaling = 1.0 / math.sqrt(count)
    return (
        (jnp.cos(phases) * scaling).astype(jnp.bfloat16),
        (jnp.sin(phases) * scaling).astype(jnp.bfloat16),
    )


def combine_parts(cos_part, sin_part, half):
    real_part = cos_part[..., :half] + sin_part[..., half:]
    imag_part = cos_part[..., half:] - sin_part[..., :half]
    return jnp.concatenate([real_part, imag_part], axis=-1).astype(jnp.bfloat16)


def complex_blocks(product, half):
    upper_rows = product[..., :half, :]
    lower_rows = product[..., half:, :]
    pieces = []
    for offset in (0, 2 * half):
        pieces.append(
            upper_rows[..., offset : offset + half]
            + lower_rows[..., offset + half : offset + 2 * half]
        )
        pieces.append(
            upper_rows[..., offset + half : offset + 2 * half]
            - lower_rows[..., offset : offset + half]
        )
    return jnp.concatenate(pieces, axis=-1)


def local(direct_snapshots, adjoint_snapshots, quad_weight, mean_velocity, diffusivity):
    local_angles, axial_cells, radial_cells, columns = direct_snapshots.shape
    snap_count = columns // 2
    total_angles = local_angles * lax.axis_size("ka")
    cos_table, sin_table = dft_tables(total_angles)
    first_wave = lax.axis_index("ka") * local_angles
    moved_direct, moved_adjoint = (
        lax.all_to_all(direct_snapshots, "ka", split_axis=2, concat_axis=0, tiled=True),
        lax.all_to_all(adjoint_snapshots, "ka", split_axis=2, concat_axis=0, tiled=True),
    )

    def transform_all(snapshots):
        flattened = snapshots.reshape(total_angles, -1)
        cos_part = jnp.dot(cos_table, flattened, preferred_element_type=jnp.float32).reshape(
            snapshots.shape
        )
        sin_part = jnp.dot(sin_table, flattened, preferred_element_type=jnp.float32).reshape(
            snapshots.shape
        )
        return combine_parts(cos_part, sin_part, snap_count)

    direct_modes, adjoint_modes = (
        lax.all_to_all(transform_all(moved_direct), "ka", split_axis=0, concat_axis=2, tiled=True),
        lax.all_to_all(transform_all(moved_adjoint), "ka", split_axis=0, concat_axis=2, tiled=True),
    )
    padded = padded_2(direct_modes, (("gx", 1),), 1)
    field_f32 = direct_modes.astype(jnp.float32)
    forward = padded[:, 2:].astype(jnp.float32)
    behind = padded[:, :-2].astype(jnp.float32)
    radial_pad = jnp.pad(field_f32, ((0, 0), (0, 0), (1, 1), (0, 0)))
    outward = radial_pad[:, :, 2:]
    inward = radial_pad[:, :, :-2]
    radius = 0.25 + (jnp.arange(radial_cells, dtype=jnp.float32) + 0.5) / radial_cells
    wavenumber = (
        first_wave + jnp.arange(local_angles, dtype=jnp.int32) - total_angles // 2
    ).astype(jnp.float32) / total_angles
    azimuthal = (wavenumber[:, None] / radius[None, :]) ** 2
    velocity = mean_velocity[None, :, :, None]
    diffusion = diffusivity[None, :, :, None]
    image = (
        -velocity * (forward - behind) * 0.5
        + diffusion
        * (
            forward
            + behind
            + outward
            + inward
            - 4.0 * field_f32
            - azimuthal[:, None, :, None] * field_f32
        )
    ).astype(jnp.bfloat16)
    norm_factor = 1.0 / math.sqrt(axial_cells * lax.axis_size("gx") * radial_cells)
    plane_weight = quad_weight * norm_factor
    weighted = (adjoint_modes.astype(jnp.float32) * plane_weight[None, :, :, None]).astype(
        jnp.bfloat16
    )
    right_side = jnp.concatenate([direct_modes, image], axis=-1)
    product = jnp.einsum(
        "kpa,kpb->kab",
        weighted.reshape(local_angles, -1, columns),
        right_side.reshape(local_angles, -1, 2 * columns),
        preferred_element_type=jnp.float32,
    )
    gram_terms = complex_blocks(product, snap_count).reshape(local_angles * snap_count, 2 * columns)
    row_count = gram_terms.shape[0] // lax.axis_size("gx")
    row_index = lax.axis_index("gx") * row_count + jnp.arange(row_count, dtype=jnp.int32)
    owner = row_index // snap_count
    selector = (owner[:, None] == jnp.arange(local_angles, dtype=jnp.int32)[None, :]).astype(
        jnp.float32
    )
    shares = gram_terms.astype(jnp.bfloat16).reshape(lax.axis_size("gx"), row_count, 2 * columns)
    shares = lax.all_to_all(shares, "gx", split_axis=0, concat_axis=0, tiled=True)
    own_rows = jnp.sum(shares.astype(jnp.float32), axis=0)
    row_energy = jnp.sum(own_rows[:, :columns] ** 2, axis=1)
    energy = jnp.sum(gather_small(jnp.sum(selector * row_energy[:, None], axis=0), "gx"), axis=0)
    mean_sq = energy / (2.0 * snap_count * snap_count)
    row_scale = jnp.sum(selector * lax.rsqrt(mean_sq + epsilon)[None, :], axis=1)
    hankel_gram = own_rows[:, :columns] * row_scale[:, None]
    reduced_operator = own_rows[:, columns:] * row_scale[:, None]
    hankel_norm = jnp.sqrt(mean_sq)
    return (hankel_gram, reduced_operator, hankel_norm)


def solution(mesh):
    placed = (
        P("ka", "gx", None, None),
        P("ka", "gx", None, None),
        P("gx", None),
        P("gx", None),
        P("gx", None),
    )
    return jax.shard_map(
        local,
        mesh=mesh,
        in_specs=placed,
        out_specs=(P(("ka", "gx"), None), P(("ka", "gx"), None), P("ka")),
        check_vma=False,
    )
```

```python
import math

import jax
import jax.numpy as jnp
from jax import lax
from jax.sharding import PartitionSpec as P

epsilon = 1e-06


def padded_2(cells, sides, width):
    for axis, dim in sides:
        count = lax.axis_size(axis)
        ends = count - 1
        head = lax.slice_in_dim(cells, 0, width, axis=dim)
        tail = lax.slice_in_dim(cells, cells.shape[dim] - width, cells.shape[dim], axis=dim)
        cells = jnp.concatenate(
            [
                lax.ppermute(tail, axis, [(i, (i + 1) % count) for i in range(ends)]),
                cells,
                lax.ppermute(head, axis, [((i + 1) % count, i) for i in range(ends)]),
            ],
            axis=dim,
        )
    return cells


def gather_small(values, axis):
    count = lax.axis_size(axis)
    copies = jnp.broadcast_to(values[None], (count,) + values.shape)
    return lax.all_to_all(copies, axis, split_axis=0, concat_axis=0, tiled=True)


def exchange(cells, axis, split_axis):
    count = lax.axis_size(axis)
    here = lax.axis_index(axis)
    width = cells.shape[split_axis] // count
    pieces = []
    for shift in range(count):
        piece = lax.dynamic_slice_in_dim(cells, ((here + shift) % count) * width, width, axis=split_axis)
        if shift:
            piece = lax.ppermute(piece, axis, [(j, (j + shift) % count) for j in range(count)])
        pieces.append(piece)
    return pieces


def in_source_order(pieces, axis, concat_axis):
    count = len(pieces)
    here = lax.axis_index(axis)
    stacked = jnp.stack(pieces)
    ordered = [lax.dynamic_index_in_dim(stacked, (here - source) % count, 0, keepdims=False) for source in range(count)]
    return jnp.concatenate(ordered, axis=concat_axis)


def shifted_tables(count, local_angles, axis):
    here = lax.axis_index(axis)
    blocks = count // local_angles
    wave_index = jnp.arange(count, dtype=jnp.int32) - count // 2
    position = jnp.arange(count, dtype=jnp.int32)
    angle_index = ((here - position // local_angles) % blocks) * local_angles + position % local_angles
    residues = wave_index[:, None] * angle_index[None, :] % count
    phases = 2.0 * math.pi * residues.astype(jnp.float32) / count
    scaling = 1.0 / math.sqrt(count)
    return (
        (jnp.cos(phases) * scaling).astype(jnp.bfloat16),
        (jnp.sin(phases) * scaling).astype(jnp.bfloat16),
    )


def dft_tables(count):
    wave_index = jnp.arange(count, dtype=jnp.int32) - count // 2
    angle_index = jnp.arange(count, dtype=jnp.int32)
    residues = wave_index[:, None] * angle_index[None, :] % count
    phases = 2.0 * math.pi * residues.astype(jnp.float32) / count
    scaling = 1.0 / math.sqrt(count)
    return (
        (jnp.cos(phases) * scaling).astype(jnp.bfloat16),
        (jnp.sin(phases) * scaling).astype(jnp.bfloat16),
    )


def combine_parts(cos_part, sin_part, half):
    real_part = cos_part[..., :half] + sin_part[..., half:]
    imag_part = cos_part[..., half:] - sin_part[..., :half]
    return jnp.concatenate([real_part, imag_part], axis=-1).astype(jnp.bfloat16)


def complex_blocks(product, half):
    upper_rows = product[..., :half, :]
    lower_rows = product[..., half:, :]
    pieces = []
    for offset in (0, 2 * half):
        pieces.append(
            upper_rows[..., offset : offset + half]
            + lower_rows[..., offset + half : offset + 2 * half]
        )
        pieces.append(
            upper_rows[..., offset + half : offset + 2 * half]
            - lower_rows[..., offset : offset + half]
        )
    return jnp.concatenate(pieces, axis=-1)


def local(direct_snapshots, adjoint_snapshots, quad_weight, mean_velocity, diffusivity):
    local_angles, axial_cells, radial_cells, columns = direct_snapshots.shape
    snap_count = columns // 2
    total_angles = local_angles * lax.axis_size("ka")
    cos_table, sin_table = shifted_tables(total_angles, local_angles, "ka")
    first_wave = lax.axis_index("ka") * local_angles
    moved_direct, moved_adjoint = (
        jnp.concatenate(exchange(direct_snapshots, "ka", 2), axis=0),
        jnp.concatenate(exchange(adjoint_snapshots, "ka", 2), axis=0),
    )

    def transform_all(snapshots):
        flattened = snapshots.reshape(total_angles, -1)
        cos_part = jnp.dot(cos_table, flattened, preferred_element_type=jnp.float32).reshape(
            snapshots.shape
        )
        sin_part = jnp.dot(sin_table, flattened, preferred_element_type=jnp.float32).reshape(
            snapshots.shape
        )
        return combine_parts(cos_part, sin_part, snap_count)

    direct_modes, adjoint_modes = (
        in_source_order(exchange(transform_all(moved_direct), "ka", 0), "ka", 2),
        in_source_order(exchange(transform_all(moved_adjoint), "ka", 0), "ka", 2),
    )
    padded = padded_2(direct_modes, (("gx", 1),), 1)
    field_f32 = direct_modes.astype(jnp.float32)
    forward = padded[:, 2:].astype(jnp.float32)
    behind = padded[:, :-2].astype(jnp.float32)
    radial_pad = jnp.pad(field_f32, ((0, 0), (0, 0), (1, 1), (0, 0)))
    outward = radial_pad[:, :, 2:]
    inward = radial_pad[:, :, :-2]
    radius = 0.25 + (jnp.arange(radial_cells, dtype=jnp.float32) + 0.5) / radial_cells
    wavenumber = (
        first_wave + jnp.arange(local_angles, dtype=jnp.int32) - total_angles // 2
    ).astype(jnp.float32) / total_angles
    azimuthal = (wavenumber[:, None] / radius[None, :]) ** 2
    velocity = mean_velocity[None, :, :, None]
    diffusion = diffusivity[None, :, :, None]
    image = (
        -velocity * (forward - behind) * 0.5
        + diffusion
        * (
            forward
            + behind
            + outward
            + inward
            - 4.0 * field_f32
            - azimuthal[:, None, :, None] * field_f32
        )
    ).astype(jnp.bfloat16)
    norm_factor = 1.0 / math.sqrt(axial_cells * lax.axis_size("gx") * radial_cells)
    plane_weight = quad_weight * norm_factor
    weighted = (adjoint_modes.astype(jnp.float32) * plane_weight[None, :, :, None]).astype(
        jnp.bfloat16
    )
    right_side = jnp.concatenate([direct_modes, image], axis=-1)
    product = jnp.einsum(
        "kpa,kpb->kab",
        weighted.reshape(local_angles, -1, columns),
        right_side.reshape(local_angles, -1, 2 * columns),
        preferred_element_type=jnp.float32,
    )
    gram_terms = complex_blocks(product, snap_count).reshape(local_angles * snap_count, 2 * columns)
    row_count = gram_terms.shape[0] // lax.axis_size("gx")
    row_index = lax.axis_index("gx") * row_count + jnp.arange(row_count, dtype=jnp.int32)
    owner = row_index // snap_count
    selector = (owner[:, None] == jnp.arange(local_angles, dtype=jnp.int32)[None, :]).astype(
        jnp.float32
    )
    shares = gram_terms.astype(jnp.bfloat16).reshape(lax.axis_size("gx"), row_count, 2 * columns)
    shares = lax.all_to_all(shares, "gx", split_axis=0, concat_axis=0, tiled=True)
    own_rows = jnp.sum(shares.astype(jnp.float32), axis=0)
    row_energy = jnp.sum(own_rows[:, :columns] ** 2, axis=1)
    energy = jnp.sum(gather_small(jnp.sum(selector * row_energy[:, None], axis=0), "gx"), axis=0)
    mean_sq = energy / (2.0 * snap_count * snap_count)
    row_scale = jnp.sum(selector * lax.rsqrt(mean_sq + epsilon)[None, :], axis=1)
    hankel_gram = own_rows[:, :columns] * row_scale[:, None]
    reduced_operator = own_rows[:, columns:] * row_scale[:, None]
    hankel_norm = jnp.sqrt(mean_sq)
    return (hankel_gram, reduced_operator, hankel_norm)


def solution(mesh):
    placed = (
        P("ka", "gx", None, None),
        P("ka", "gx", None, None),
        P("gx", None),
        P("gx", None),
        P("gx", None),
    )
    return jax.shard_map(
        local,
        mesh=mesh,
        in_specs=placed,
        out_specs=(P(("ka", "gx"), None), P(("ka", "gx"), None), P("ka")),
        check_vma=False,
    )
```

```python
import functools
import math

import jax
import jax.numpy as jnp
from jax import lax
from jax.experimental import pallas as pl
from jax.experimental.pallas import tpu as pltpu
from jax.sharding import PartitionSpec as P

epsilon = 1e-06


def padded_2(cells, sides, width):
    for axis, dim in sides:
        count = lax.axis_size(axis)
        ends = count - 1
        head = lax.slice_in_dim(cells, 0, width, axis=dim)
        tail = lax.slice_in_dim(cells, cells.shape[dim] - width, cells.shape[dim], axis=dim)
        cells = jnp.concatenate(
            [
                lax.ppermute(tail, axis, [(i, (i + 1) % count) for i in range(ends)]),
                cells,
                lax.ppermute(head, axis, [((i + 1) % count, i) for i in range(ends)]),
            ],
            axis=dim,
        )
    return cells


def gather_small(values, axis):
    count = lax.axis_size(axis)
    copies = jnp.broadcast_to(values[None], (count,) + values.shape)
    return lax.all_to_all(copies, axis, split_axis=0, concat_axis=0, tiled=True)


def exchange(cells, axis, split_axis):
    count = lax.axis_size(axis)
    here = lax.axis_index(axis)
    width = cells.shape[split_axis] // count
    pieces = []
    for shift in range(count):
        piece = lax.dynamic_slice_in_dim(cells, ((here + shift) % count) * width, width, axis=split_axis)
        if shift:
            piece = lax.ppermute(piece, axis, [(j, (j + shift) % count) for j in range(count)])
        pieces.append(piece)
    return pieces


def in_source_order(pieces, axis, concat_axis):
    count = len(pieces)
    here = lax.axis_index(axis)
    stacked = jnp.stack(pieces)
    ordered = [lax.dynamic_index_in_dim(stacked, (here - source) % count, 0, keepdims=False) for source in range(count)]
    return jnp.concatenate(ordered, axis=concat_axis)


def shifted_tables(count, local_angles, axis):
    here = lax.axis_index(axis)
    blocks = count // local_angles
    wave_index = jnp.arange(count, dtype=jnp.int32) - count // 2
    position = jnp.arange(count, dtype=jnp.int32)
    angle_index = ((here - position // local_angles) % blocks) * local_angles + position % local_angles
    residues = wave_index[:, None] * angle_index[None, :] % count
    phases = 2.0 * math.pi * residues.astype(jnp.float32) / count
    scaling = 1.0 / math.sqrt(count)
    return (
        (jnp.cos(phases) * scaling).astype(jnp.bfloat16),
        (jnp.sin(phases) * scaling).astype(jnp.bfloat16),
    )


def dft_kernel(*refs, count, weighted):
    table_ref = refs[0]
    piece_refs = refs[1:1 + count]
    rest = refs[1 + count:]
    out_ref = rest[-1]
    width = piece_refs[0].shape[1]
    lane = lax.broadcasted_iota(jnp.int32, (1, width), 1) % 128
    low = lane < 64
    rows = []
    for piece_ref in piece_refs:
        x = piece_ref[...].astype(jnp.float32)
        swapped = jnp.where(low, pltpu.roll(x, width - 64, 1), -pltpu.roll(x, 64, 1))
        rows.append(x)
        rows.append(swapped)
    stacked = jnp.concatenate(rows, axis=0).astype(jnp.bfloat16)
    acc = jnp.dot(table_ref[...], stacked, preferred_element_type=jnp.float32)
    modes = acc.astype(jnp.bfloat16)
    if weighted:
        modes = (modes.astype(jnp.float32) * rest[0][...]).astype(jnp.bfloat16)
    out_ref[...] = modes

def dft(table, pieces, weight=None):
    count = len(pieces)
    angles, total = pieces[0].shape
    waves = table.shape[0]
    block = math.gcd(total, 1024)
    grid = (total // block,)
    in_specs = [pl.BlockSpec((waves, table.shape[1]), lambda j: (0, 0))]
    in_specs += [pl.BlockSpec((angles, block), lambda j: (0, j)) for _ in pieces]
    args = [table, *pieces]
    if weight is not None:
        in_specs.append(pl.BlockSpec((1, block), lambda j: (0, j)))
        args.append(weight)
    return pl.pallas_call(
        functools.partial(dft_kernel, count=count, weighted=weight is not None),
        grid=grid,
        in_specs=in_specs,
        out_specs=pl.BlockSpec((waves, block), lambda j: (0, j)),
        out_shape=jax.ShapeDtypeStruct((waves, total), jnp.bfloat16),
    )(*args)


def piece_tables(count, local_angles, axis):
    here = lax.axis_index(axis)
    blocks = count // local_angles
    wave_index = jnp.arange(count, dtype=jnp.int32) - count // 2
    scaling = 1.0 / math.sqrt(count)
    columns = []
    for shift in range(blocks):
        angle_index = ((here - shift) % blocks) * local_angles + jnp.arange(local_angles, dtype=jnp.int32)
        residues = wave_index[:, None] * angle_index[None, :] % count
        phases = 2.0 * math.pi * residues.astype(jnp.float32) / count
        columns.append((jnp.cos(phases) * scaling).astype(jnp.bfloat16))
        columns.append((jnp.sin(phases) * scaling).astype(jnp.bfloat16))
    return jnp.concatenate(columns, axis=1)


def dft_tables(count):
    wave_index = jnp.arange(count, dtype=jnp.int32) - count // 2
    angle_index = jnp.arange(count, dtype=jnp.int32)
    residues = wave_index[:, None] * angle_index[None, :] % count
    phases = 2.0 * math.pi * residues.astype(jnp.float32) / count
    scaling = 1.0 / math.sqrt(count)
    return (
        (jnp.cos(phases) * scaling).astype(jnp.bfloat16),
        (jnp.sin(phases) * scaling).astype(jnp.bfloat16),
    )


def combine_parts(cos_part, sin_part, half):
    real_part = cos_part[..., :half] + sin_part[..., half:]
    imag_part = cos_part[..., half:] - sin_part[..., :half]
    return jnp.concatenate([real_part, imag_part], axis=-1).astype(jnp.bfloat16)


def complex_blocks(product, half):
    upper_rows = product[..., :half, :]
    lower_rows = product[..., half:, :]
    pieces = []
    for offset in (0, 2 * half):
        pieces.append(
            upper_rows[..., offset : offset + half]
            + lower_rows[..., offset + half : offset + 2 * half]
        )
        pieces.append(
            upper_rows[..., offset + half : offset + 2 * half]
            - lower_rows[..., offset : offset + half]
        )
    return jnp.concatenate(pieces, axis=-1)


def local(direct_snapshots, adjoint_snapshots, quad_weight, mean_velocity, diffusivity):
    local_angles, axial_cells, radial_cells, columns = direct_snapshots.shape
    snap_count = columns // 2
    total_angles = local_angles * lax.axis_size("ka")
    table = piece_tables(total_angles, local_angles, "ka")
    first_wave = lax.axis_index("ka") * local_angles
    band_count = lax.axis_size("ka")
    band = radial_cells // band_count
    lanes = axial_cells * band * columns
    norm_factor = 1.0 / math.sqrt(axial_cells * lax.axis_size("gx") * radial_cells)
    band_weight = lax.dynamic_slice_in_dim(
        quad_weight * norm_factor, lax.axis_index("ka") * band, band, axis=1
    )
    lane_weight = jnp.broadcast_to(band_weight[:, :, None], (axial_cells, band, columns)).reshape(1, lanes)

    def transform_all(snapshots, weight=None):
        pieces = [piece.reshape(local_angles, lanes) for piece in exchange(snapshots, "ka", 2)]
        modes = dft(table, pieces, weight)
        return modes.reshape(total_angles, axial_cells, band, columns)

    direct_modes = in_source_order(exchange(transform_all(direct_snapshots), "ka", 0), "ka", 2)
    weighted = in_source_order(
        exchange(transform_all(adjoint_snapshots, lane_weight), "ka", 0), "ka", 2
    )
    padded = padded_2(direct_modes, (("gx", 1),), 1)
    field_f32 = direct_modes.astype(jnp.float32)
    forward = padded[:, 2:].astype(jnp.float32)
    behind = padded[:, :-2].astype(jnp.float32)
    radial_pad = jnp.pad(field_f32, ((0, 0), (0, 0), (1, 1), (0, 0)))
    outward = radial_pad[:, :, 2:]
    inward = radial_pad[:, :, :-2]
    radius = 0.25 + (jnp.arange(radial_cells, dtype=jnp.float32) + 0.5) / radial_cells
    wavenumber = (
        first_wave + jnp.arange(local_angles, dtype=jnp.int32) - total_angles // 2
    ).astype(jnp.float32) / total_angles
    azimuthal = (wavenumber[:, None] / radius[None, :]) ** 2
    velocity = mean_velocity[None, :, :, None]
    diffusion = diffusivity[None, :, :, None]
    image = (
        -velocity * (forward - behind) * 0.5
        + diffusion
        * (
            forward
            + behind
            + outward
            + inward
            - 4.0 * field_f32
            - azimuthal[:, None, :, None] * field_f32
        )
    ).astype(jnp.bfloat16)
    right_side = jnp.concatenate([direct_modes, image], axis=-1)
    product = jnp.einsum(
        "kpa,kpb->kab",
        weighted.reshape(local_angles, -1, columns),
        right_side.reshape(local_angles, -1, 2 * columns),
        preferred_element_type=jnp.float32,
    )
    gram_terms = complex_blocks(product, snap_count).reshape(local_angles * snap_count, 2 * columns)
    row_count = gram_terms.shape[0] // lax.axis_size("gx")
    row_index = lax.axis_index("gx") * row_count + jnp.arange(row_count, dtype=jnp.int32)
    owner = row_index // snap_count
    selector = (owner[:, None] == jnp.arange(local_angles, dtype=jnp.int32)[None, :]).astype(
        jnp.float32
    )
    shares = gram_terms.astype(jnp.bfloat16).reshape(lax.axis_size("gx"), row_count, 2 * columns)
    shares = lax.all_to_all(shares, "gx", split_axis=0, concat_axis=0, tiled=True)
    own_rows = jnp.sum(shares.astype(jnp.float32), axis=0)
    row_energy = jnp.sum(own_rows[:, :columns] ** 2, axis=1)
    energy = jnp.sum(gather_small(jnp.sum(selector * row_energy[:, None], axis=0), "gx"), axis=0)
    mean_sq = energy / (2.0 * snap_count * snap_count)
    row_scale = jnp.sum(selector * lax.rsqrt(mean_sq + epsilon)[None, :], axis=1)
    hankel_gram = own_rows[:, :columns] * row_scale[:, None]
    reduced_operator = own_rows[:, columns:] * row_scale[:, None]
    hankel_norm = jnp.sqrt(mean_sq)
    return (hankel_gram, reduced_operator, hankel_norm)


def solution(mesh):
    placed = (
        P("ka", "gx", None, None),
        P("ka", "gx", None, None),
        P("gx", None),
        P("gx", None),
        P("gx", None),
    )
    return jax.shard_map(
        local,
        mesh=mesh,
        in_specs=placed,
        out_specs=(P(("ka", "gx"), None), P(("ka", "gx"), None), P("ka")),
        check_vma=False,
    )
```

```python
import functools
import math

import jax
import jax.numpy as jnp
from jax import lax
from jax.experimental import pallas as pl
from jax.experimental.pallas import tpu as pltpu
from jax.sharding import PartitionSpec as P

epsilon = 1e-06


def padded_2(cells, sides, width):
    for axis, dim in sides:
        count = lax.axis_size(axis)
        ends = count - 1
        head = lax.slice_in_dim(cells, 0, width, axis=dim)
        tail = lax.slice_in_dim(cells, cells.shape[dim] - width, cells.shape[dim], axis=dim)
        cells = jnp.concatenate(
            [
                lax.ppermute(tail, axis, [(i, (i + 1) % count) for i in range(ends)]),
                cells,
                lax.ppermute(head, axis, [((i + 1) % count, i) for i in range(ends)]),
            ],
            axis=dim,
        )
    return cells


def gather_small(values, axis):
    count = lax.axis_size(axis)
    copies = jnp.broadcast_to(values[None], (count,) + values.shape)
    return lax.all_to_all(copies, axis, split_axis=0, concat_axis=0, tiled=True)


def exchange(cells, axis, split_axis, offset=0, width=None):
    count = lax.axis_size(axis)
    here = lax.axis_index(axis)
    stride = cells.shape[split_axis] // count
    width = stride if width is None else width
    pieces = []
    for shift in range(count):
        start = ((here + shift) % count) * stride + offset
        piece = lax.dynamic_slice_in_dim(cells, start, width, axis=split_axis)
        if shift:
            piece = lax.ppermute(piece, axis, [(j, (j + shift) % count) for j in range(count)])
        pieces.append(piece)
    return pieces


def in_source_order(pieces, axis, concat_axis):
    count = len(pieces)
    here = lax.axis_index(axis)
    stacked = jnp.stack(pieces)
    ordered = [lax.dynamic_index_in_dim(stacked, (here - source) % count, 0, keepdims=False) for source in range(count)]
    return jnp.concatenate(ordered, axis=concat_axis)


def shifted_tables(count, local_angles, axis):
    here = lax.axis_index(axis)
    blocks = count // local_angles
    wave_index = jnp.arange(count, dtype=jnp.int32) - count // 2
    position = jnp.arange(count, dtype=jnp.int32)
    angle_index = ((here - position // local_angles) % blocks) * local_angles + position % local_angles
    residues = wave_index[:, None] * angle_index[None, :] % count
    phases = 2.0 * math.pi * residues.astype(jnp.float32) / count
    scaling = 1.0 / math.sqrt(count)
    return (
        (jnp.cos(phases) * scaling).astype(jnp.bfloat16),
        (jnp.sin(phases) * scaling).astype(jnp.bfloat16),
    )


def dft_kernel(*refs, count, weighted):
    table_ref = refs[0]
    piece_refs = refs[1:1 + count]
    rest = refs[1 + count:]
    out_ref = rest[-1]
    width = piece_refs[0].shape[1]
    lane = lax.broadcasted_iota(jnp.int32, (1, width), 1) % 128
    low = lane < 64
    rows = []
    for piece_ref in piece_refs:
        x = piece_ref[...].astype(jnp.float32)
        swapped = jnp.where(low, pltpu.roll(x, width - 64, 1), -pltpu.roll(x, 64, 1))
        rows.append(x)
        rows.append(swapped)
    stacked = jnp.concatenate(rows, axis=0).astype(jnp.bfloat16)
    acc = jnp.dot(table_ref[...], stacked, preferred_element_type=jnp.float32)
    modes = acc.astype(jnp.bfloat16)
    if weighted:
        modes = (modes.astype(jnp.float32) * rest[0][...]).astype(jnp.bfloat16)
    out_ref[...] = modes

def dft(table, pieces, weight=None):
    count = len(pieces)
    angles, total = pieces[0].shape
    waves = table.shape[0]
    block = math.gcd(total, 1024)
    grid = (total // block,)
    in_specs = [pl.BlockSpec((waves, table.shape[1]), lambda j: (0, 0))]
    in_specs += [pl.BlockSpec((angles, block), lambda j: (0, j)) for _ in pieces]
    args = [table, *pieces]
    if weight is not None:
        in_specs.append(pl.BlockSpec((1, block), lambda j: (0, j)))
        args.append(weight)
    return pl.pallas_call(
        functools.partial(dft_kernel, count=count, weighted=weight is not None),
        grid=grid,
        in_specs=in_specs,
        out_specs=pl.BlockSpec((waves, block), lambda j: (0, j)),
        out_shape=jax.ShapeDtypeStruct((waves, total), jnp.bfloat16),
    )(*args)


def piece_tables(count, local_angles, axis, wave_order):
    here = lax.axis_index(axis)
    blocks = count // local_angles
    wave_index = wave_order - count // 2
    scaling = 1.0 / math.sqrt(count)
    columns = []
    for shift in range(blocks):
        angle_index = ((here - shift) % blocks) * local_angles + jnp.arange(local_angles, dtype=jnp.int32)
        residues = wave_index[:, None] * angle_index[None, :] % count
        phases = 2.0 * math.pi * residues.astype(jnp.float32) / count
        columns.append((jnp.cos(phases) * scaling).astype(jnp.bfloat16))
        columns.append((jnp.sin(phases) * scaling).astype(jnp.bfloat16))
    return jnp.concatenate(columns, axis=1)


def dft_tables(count):
    wave_index = jnp.arange(count, dtype=jnp.int32) - count // 2
    angle_index = jnp.arange(count, dtype=jnp.int32)
    residues = wave_index[:, None] * angle_index[None, :] % count
    phases = 2.0 * math.pi * residues.astype(jnp.float32) / count
    scaling = 1.0 / math.sqrt(count)
    return (
        (jnp.cos(phases) * scaling).astype(jnp.bfloat16),
        (jnp.sin(phases) * scaling).astype(jnp.bfloat16),
    )


def combine_parts(cos_part, sin_part, half):
    real_part = cos_part[..., :half] + sin_part[..., half:]
    imag_part = cos_part[..., half:] - sin_part[..., :half]
    return jnp.concatenate([real_part, imag_part], axis=-1).astype(jnp.bfloat16)


def complex_blocks(product, half):
    upper_rows = product[..., :half, :]
    lower_rows = product[..., half:, :]
    pieces = []
    for offset in (0, 2 * half):
        pieces.append(
            upper_rows[..., offset : offset + half]
            + lower_rows[..., offset + half : offset + 2 * half]
        )
        pieces.append(
            upper_rows[..., offset + half : offset + 2 * half]
            - lower_rows[..., offset : offset + half]
        )
    return jnp.concatenate(pieces, axis=-1)


def local(direct_snapshots, adjoint_snapshots, quad_weight, mean_velocity, diffusivity):
    local_angles, axial_cells, radial_cells, columns = direct_snapshots.shape
    snap_count = columns // 2
    band_count = lax.axis_size("ka")
    axial_count = lax.axis_size("gx")
    total_angles = local_angles * band_count
    owned = local_angles // axial_count
    halves = 2 if local_angles % axial_count == 0 and owned % 2 == 0 else 1
    half_waves = local_angles // halves
    position = jnp.arange(local_angles, dtype=jnp.int32)
    if halves == 1:
        local_order = position
    else:
        part = owned // halves
        within = position % half_waves
        local_order = (within // part) * owned + (position // half_waves) * part + within % part
    wave_order = (
        jnp.arange(band_count, dtype=jnp.int32)[:, None] * local_angles + local_order[None, :]
    ).reshape(total_angles)
    table = piece_tables(total_angles, local_angles, "ka", wave_order)
    first_wave = lax.axis_index("ka") * local_angles
    band = radial_cells // band_count
    lanes = axial_cells * band * columns
    norm_factor = 1.0 / math.sqrt(axial_cells * axial_count * radial_cells)
    band_weight = lax.dynamic_slice_in_dim(
        quad_weight * norm_factor, lax.axis_index("ka") * band, band, axis=1
    )
    lane_weight = jnp.broadcast_to(band_weight[:, :, None], (axial_cells, band, columns)).reshape(1, lanes)

    def transform_all(snapshots, weight=None):
        pieces = [piece.reshape(local_angles, lanes) for piece in exchange(snapshots, "ka", 2)]
        modes = dft(table, pieces, weight)
        return modes.reshape(total_angles, axial_cells, band, columns)

    direct_all = transform_all(direct_snapshots)
    weighted_all = transform_all(adjoint_snapshots, lane_weight)
    radius = 0.25 + (jnp.arange(radial_cells, dtype=jnp.float32) + 0.5) / radial_cells
    velocity = mean_velocity[None, :, :, None]
    diffusion = diffusivity[None, :, :, None]
    row_count = local_angles * snap_count // axial_count
    half_rows = row_count // halves
    own_parts = []
    for half in range(halves):
        offset = half * half_waves
        direct_modes = in_source_order(exchange(direct_all, "ka", 0, offset, half_waves), "ka", 2)
        weighted = in_source_order(exchange(weighted_all, "ka", 0, offset, half_waves), "ka", 2)
        padded = padded_2(direct_modes, (("gx", 1),), 1)
        field_f32 = direct_modes.astype(jnp.float32)
        forward = padded[:, 2:].astype(jnp.float32)
        behind = padded[:, :-2].astype(jnp.float32)
        radial_pad = jnp.pad(field_f32, ((0, 0), (0, 0), (1, 1), (0, 0)))
        outward = radial_pad[:, :, 2:]
        inward = radial_pad[:, :, :-2]
        wavenumber = (
            first_wave + local_order[offset : offset + half_waves] - total_angles // 2
        ).astype(jnp.float32) / total_angles
        azimuthal = (wavenumber[:, None] / radius[None, :]) ** 2
        image = (
            -velocity * (forward - behind) * 0.5
            + diffusion
            * (
                forward
                + behind
                + outward
                + inward
                - 4.0 * field_f32
                - azimuthal[:, None, :, None] * field_f32
            )
        ).astype(jnp.bfloat16)
        right_side = jnp.concatenate([direct_modes, image], axis=-1)
        product = jnp.einsum(
            "kpa,kpb->kab",
            weighted.reshape(half_waves, -1, columns),
            right_side.reshape(half_waves, -1, 2 * columns),
            preferred_element_type=jnp.float32,
        )
        gram_terms = complex_blocks(product, snap_count).reshape(half_waves * snap_count, 2 * columns)
        shares = gram_terms.astype(jnp.bfloat16).reshape(axial_count, half_rows, 2 * columns)
        shares = lax.all_to_all(shares, "gx", split_axis=0, concat_axis=0, tiled=True)
        own_parts.append(jnp.sum(shares.astype(jnp.float32), axis=0))
    own_rows = jnp.concatenate(own_parts, axis=0)
    row_index = lax.axis_index("gx") * row_count + jnp.arange(row_count, dtype=jnp.int32)
    owner = row_index // snap_count
    selector = (owner[:, None] == jnp.arange(local_angles, dtype=jnp.int32)[None, :]).astype(
        jnp.float32
    )
    row_energy = jnp.sum(own_rows[:, :columns] ** 2, axis=1)
    energy = jnp.sum(gather_small(jnp.sum(selector * row_energy[:, None], axis=0), "gx"), axis=0)
    mean_sq = energy / (2.0 * snap_count * snap_count)
    row_scale = jnp.sum(selector * lax.rsqrt(mean_sq + epsilon)[None, :], axis=1)
    hankel_gram = own_rows[:, :columns] * row_scale[:, None]
    reduced_operator = own_rows[:, columns:] * row_scale[:, None]
    hankel_norm = jnp.sqrt(mean_sq)
    return (hankel_gram, reduced_operator, hankel_norm)


def solution(mesh):
    placed = (
        P("ka", "gx", None, None),
        P("ka", "gx", None, None),
        P("gx", None),
        P("gx", None),
        P("gx", None),
    )
    return jax.shard_map(
        local,
        mesh=mesh,
        in_specs=placed,
        out_specs=(P(("ka", "gx"), None), P(("ka", "gx"), None), P("ka")),
        check_vma=False,
    )
```

```python
import functools
import math

import jax
import jax.numpy as jnp
from jax import lax
from jax.experimental import pallas as pl
from jax.experimental.pallas import tpu as pltpu
from jax.sharding import PartitionSpec as P

epsilon = 1e-06


def padded_2(cells, sides, width):
    for axis, dim in sides:
        count = lax.axis_size(axis)
        ends = count - 1
        head = lax.slice_in_dim(cells, 0, width, axis=dim)
        tail = lax.slice_in_dim(cells, cells.shape[dim] - width, cells.shape[dim], axis=dim)
        cells = jnp.concatenate(
            [
                lax.ppermute(tail, axis, [(i, (i + 1) % count) for i in range(ends)]),
                cells,
                lax.ppermute(head, axis, [((i + 1) % count, i) for i in range(ends)]),
            ],
            axis=dim,
        )
    return cells


def gather_small(values, axis):
    count = lax.axis_size(axis)
    copies = jnp.broadcast_to(values[None], (count,) + values.shape)
    return lax.all_to_all(copies, axis, split_axis=0, concat_axis=0, tiled=True)


def exchange(cells, axis, split_axis):
    count = lax.axis_size(axis)
    here = lax.axis_index(axis)
    width = cells.shape[split_axis] // count
    pieces = []
    for shift in range(count):
        piece = lax.dynamic_slice_in_dim(cells, ((here + shift) % count) * width, width, axis=split_axis)
        if shift:
            piece = lax.ppermute(piece, axis, [(j, (j + shift) % count) for j in range(count)])
        pieces.append(piece)
    return pieces


def in_source_order(pieces, axis, concat_axis):
    count = len(pieces)
    here = lax.axis_index(axis)
    stacked = jnp.stack(pieces)
    ordered = [lax.dynamic_index_in_dim(stacked, (here - source) % count, 0, keepdims=False) for source in range(count)]
    return jnp.concatenate(ordered, axis=concat_axis)


def shifted_tables(count, local_angles, axis):
    here = lax.axis_index(axis)
    blocks = count // local_angles
    wave_index = jnp.arange(count, dtype=jnp.int32) - count // 2
    position = jnp.arange(count, dtype=jnp.int32)
    angle_index = ((here - position // local_angles) % blocks) * local_angles + position % local_angles
    residues = wave_index[:, None] * angle_index[None, :] % count
    phases = 2.0 * math.pi * residues.astype(jnp.float32) / count
    scaling = 1.0 / math.sqrt(count)
    return (
        (jnp.cos(phases) * scaling).astype(jnp.bfloat16),
        (jnp.sin(phases) * scaling).astype(jnp.bfloat16),
    )


def dft_kernel(*refs, count, weighted):
    table_ref = refs[0]
    piece_refs = refs[1:1 + count]
    rest = refs[1 + count:]
    out_ref = rest[-1]
    width = piece_refs[0].shape[1]
    lane = lax.broadcasted_iota(jnp.int32, (1, width), 1) % 128
    low = lane < 64
    packed = piece_refs[0].shape[0] % 16 == 0
    rows = []
    for piece_ref in piece_refs:
        x = piece_ref[...]
        if not packed:
            x = x.astype(jnp.float32)
        swapped = jnp.where(low, pltpu.roll(x, width - 64, 1), -pltpu.roll(x, 64, 1))
        rows.append(x)
        rows.append(swapped)
    stacked = jnp.concatenate(rows, axis=0).astype(jnp.bfloat16)
    acc = jnp.dot(table_ref[...], stacked, preferred_element_type=jnp.float32)
    modes = acc.astype(jnp.bfloat16)
    if weighted:
        modes = (modes.astype(jnp.float32) * rest[0][...]).astype(jnp.bfloat16)
    out_ref[...] = modes

def dft(table, pieces, weight=None):
    count = len(pieces)
    angles, total = pieces[0].shape
    waves = table.shape[0]
    block = math.gcd(total, 4096)
    grid = (total // block,)
    in_specs = [pl.BlockSpec((waves, table.shape[1]), lambda j: (0, 0))]
    in_specs += [pl.BlockSpec((angles, block), lambda j: (0, j)) for _ in pieces]
    args = [table, *pieces]
    if weight is not None:
        in_specs.append(pl.BlockSpec((1, block), lambda j: (0, j)))
        args.append(weight)
    return pl.pallas_call(
        functools.partial(dft_kernel, count=count, weighted=weight is not None),
        grid=grid,
        in_specs=in_specs,
        out_specs=pl.BlockSpec((waves, block), lambda j: (0, j)),
        out_shape=jax.ShapeDtypeStruct((waves, total), jnp.bfloat16),
    )(*args)


def piece_tables(count, local_angles, axis):
    here = lax.axis_index(axis)
    blocks = count // local_angles
    wave_index = jnp.arange(count, dtype=jnp.int32) - count // 2
    scaling = 1.0 / math.sqrt(count)
    columns = []
    for shift in range(blocks):
        angle_index = ((here - shift) % blocks) * local_angles + jnp.arange(local_angles, dtype=jnp.int32)
        residues = wave_index[:, None] * angle_index[None, :] % count
        phases = 2.0 * math.pi * residues.astype(jnp.float32) / count
        columns.append((jnp.cos(phases) * scaling).astype(jnp.bfloat16))
        columns.append((jnp.sin(phases) * scaling).astype(jnp.bfloat16))
    return jnp.concatenate(columns, axis=1)


def dft_tables(count):
    wave_index = jnp.arange(count, dtype=jnp.int32) - count // 2
    angle_index = jnp.arange(count, dtype=jnp.int32)
    residues = wave_index[:, None] * angle_index[None, :] % count
    phases = 2.0 * math.pi * residues.astype(jnp.float32) / count
    scaling = 1.0 / math.sqrt(count)
    return (
        (jnp.cos(phases) * scaling).astype(jnp.bfloat16),
        (jnp.sin(phases) * scaling).astype(jnp.bfloat16),
    )


def combine_parts(cos_part, sin_part, half):
    real_part = cos_part[..., :half] + sin_part[..., half:]
    imag_part = cos_part[..., half:] - sin_part[..., :half]
    return jnp.concatenate([real_part, imag_part], axis=-1).astype(jnp.bfloat16)


def complex_blocks(product, half):
    upper_rows = product[..., :half, :]
    lower_rows = product[..., half:, :]
    pieces = []
    for offset in (0, 2 * half):
        pieces.append(
            upper_rows[..., offset : offset + half]
            + lower_rows[..., offset + half : offset + 2 * half]
        )
        pieces.append(
            upper_rows[..., offset + half : offset + 2 * half]
            - lower_rows[..., offset : offset + half]
        )
    return jnp.concatenate(pieces, axis=-1)


def local(direct_snapshots, adjoint_snapshots, quad_weight, mean_velocity, diffusivity):
    local_angles, axial_cells, radial_cells, columns = direct_snapshots.shape
    snap_count = columns // 2
    total_angles = local_angles * lax.axis_size("ka")
    table = piece_tables(total_angles, local_angles, "ka")
    first_wave = lax.axis_index("ka") * local_angles
    band_count = lax.axis_size("ka")
    band = radial_cells // band_count
    lanes = axial_cells * band * columns
    norm_factor = 1.0 / math.sqrt(axial_cells * lax.axis_size("gx") * radial_cells)
    band_weight = lax.dynamic_slice_in_dim(
        quad_weight * norm_factor, lax.axis_index("ka") * band, band, axis=1
    )
    lane_weight = jnp.broadcast_to(band_weight[:, :, None], (axial_cells, band, columns)).reshape(1, lanes)

    def transform_all(snapshots, weight=None):
        pieces = [piece.reshape(local_angles, lanes) for piece in exchange(snapshots, "ka", 2)]
        modes = dft(table, pieces, weight)
        return modes.reshape(total_angles, axial_cells, band, columns)

    direct_modes = in_source_order(exchange(transform_all(direct_snapshots), "ka", 0), "ka", 2)
    weighted = in_source_order(
        exchange(transform_all(adjoint_snapshots, lane_weight), "ka", 0), "ka", 2
    )
    padded = padded_2(direct_modes, (("gx", 1),), 1)
    field_f32 = direct_modes.astype(jnp.float32)
    forward = padded[:, 2:].astype(jnp.float32)
    behind = padded[:, :-2].astype(jnp.float32)
    radial_pad = jnp.pad(field_f32, ((0, 0), (0, 0), (1, 1), (0, 0)))
    outward = radial_pad[:, :, 2:]
    inward = radial_pad[:, :, :-2]
    radius = 0.25 + (jnp.arange(radial_cells, dtype=jnp.float32) + 0.5) / radial_cells
    wavenumber = (
        first_wave + jnp.arange(local_angles, dtype=jnp.int32) - total_angles // 2
    ).astype(jnp.float32) / total_angles
    azimuthal = (wavenumber[:, None] / radius[None, :]) ** 2
    velocity = mean_velocity[None, :, :, None]
    diffusion = diffusivity[None, :, :, None]
    image = (
        -velocity * (forward - behind) * 0.5
        + diffusion
        * (
            forward
            + behind
            + outward
            + inward
            - 4.0 * field_f32
            - azimuthal[:, None, :, None] * field_f32
        )
    ).astype(jnp.bfloat16)
    right_side = jnp.concatenate([direct_modes, image], axis=-1)
    product = jnp.einsum(
        "kpa,kpb->kab",
        weighted.reshape(local_angles, -1, columns),
        right_side.reshape(local_angles, -1, 2 * columns),
        preferred_element_type=jnp.float32,
    )
    gram_terms = complex_blocks(product, snap_count).reshape(local_angles * snap_count, 2 * columns)
    row_count = gram_terms.shape[0] // lax.axis_size("gx")
    row_index = lax.axis_index("gx") * row_count + jnp.arange(row_count, dtype=jnp.int32)
    owner = row_index // snap_count
    selector = (owner[:, None] == jnp.arange(local_angles, dtype=jnp.int32)[None, :]).astype(
        jnp.float32
    )
    shares = gram_terms.astype(jnp.bfloat16).reshape(lax.axis_size("gx"), row_count, 2 * columns)
    shares = lax.all_to_all(shares, "gx", split_axis=0, concat_axis=0, tiled=True)
    own_rows = jnp.sum(shares.astype(jnp.float32), axis=0)
    row_energy = jnp.sum(own_rows[:, :columns] ** 2, axis=1)
    energy = jnp.sum(gather_small(jnp.sum(selector * row_energy[:, None], axis=0), "gx"), axis=0)
    mean_sq = energy / (2.0 * snap_count * snap_count)
    row_scale = jnp.sum(selector * lax.rsqrt(mean_sq + epsilon)[None, :], axis=1)
    hankel_gram = own_rows[:, :columns] * row_scale[:, None]
    reduced_operator = own_rows[:, columns:] * row_scale[:, None]
    hankel_norm = jnp.sqrt(mean_sq)
    return (hankel_gram, reduced_operator, hankel_norm)


def solution(mesh):
    placed = (
        P("ka", "gx", None, None),
        P("ka", "gx", None, None),
        P("gx", None),
        P("gx", None),
        P("gx", None),
    )
    return jax.shard_map(
        local,
        mesh=mesh,
        in_specs=placed,
        out_specs=(P(("ka", "gx"), None), P(("ka", "gx"), None), P("ka")),
        check_vma=False,
    )
```

```python
import functools
import math

import jax
import jax.numpy as jnp
from jax import lax
from jax.experimental import pallas as pl
from jax.experimental.pallas import tpu as pltpu
from jax.sharding import PartitionSpec as P

epsilon = 1e-06


def padded_2(cells, sides, width):
    for axis, dim in sides:
        count = lax.axis_size(axis)
        ends = count - 1
        head = lax.slice_in_dim(cells, 0, width, axis=dim)
        tail = lax.slice_in_dim(cells, cells.shape[dim] - width, cells.shape[dim], axis=dim)
        cells = jnp.concatenate(
            [
                lax.ppermute(tail, axis, [(i, (i + 1) % count) for i in range(ends)]),
                cells,
                lax.ppermute(head, axis, [((i + 1) % count, i) for i in range(ends)]),
            ],
            axis=dim,
        )
    return cells


def gather_small(values, axis):
    count = lax.axis_size(axis)
    copies = jnp.broadcast_to(values[None], (count,) + values.shape)
    return lax.all_to_all(copies, axis, split_axis=0, concat_axis=0, tiled=True)


def exchange(cells, axis, split_axis):
    count = lax.axis_size(axis)
    here = lax.axis_index(axis)
    width = cells.shape[split_axis] // count
    pieces = []
    for shift in range(count):
        piece = lax.dynamic_slice_in_dim(cells, ((here + shift) % count) * width, width, axis=split_axis)
        if shift:
            piece = lax.ppermute(piece, axis, [(j, (j + shift) % count) for j in range(count)])
        pieces.append(piece)
    return pieces


def in_source_order(pieces, axis, concat_axis):
    count = len(pieces)
    here = lax.axis_index(axis)
    stacked = jnp.stack(pieces)
    ordered = [lax.dynamic_index_in_dim(stacked, (here - source) % count, 0, keepdims=False) for source in range(count)]
    return jnp.concatenate(ordered, axis=concat_axis)


def shifted_tables(count, local_angles, axis):
    here = lax.axis_index(axis)
    blocks = count // local_angles
    wave_index = jnp.arange(count, dtype=jnp.int32) - count // 2
    position = jnp.arange(count, dtype=jnp.int32)
    angle_index = ((here - position // local_angles) % blocks) * local_angles + position % local_angles
    residues = wave_index[:, None] * angle_index[None, :] % count
    phases = 2.0 * math.pi * residues.astype(jnp.float32) / count
    scaling = 1.0 / math.sqrt(count)
    return (
        (jnp.cos(phases) * scaling).astype(jnp.bfloat16),
        (jnp.sin(phases) * scaling).astype(jnp.bfloat16),
    )


def dft_kernel(*refs, count, weighted):
    table_ref = refs[0]
    piece_refs = refs[1:1 + count]
    rest = refs[1 + count:]
    out_ref = rest[-1]
    width = piece_refs[0].shape[1]
    lane = lax.broadcasted_iota(jnp.int32, (1, width), 1) % 128
    low = lane < 64
    packed = piece_refs[0].shape[0] % 16 == 0
    rows = []
    for piece_ref in piece_refs:
        x = piece_ref[...]
        if not packed:
            x = x.astype(jnp.float32)
        swapped = jnp.where(low, pltpu.roll(x, width - 64, 1), -pltpu.roll(x, 64, 1))
        rows.append(x)
        rows.append(swapped)
    stacked = jnp.concatenate(rows, axis=0).astype(jnp.bfloat16)
    acc = jnp.dot(table_ref[...], stacked, preferred_element_type=jnp.float32)
    modes = acc.astype(jnp.bfloat16)
    if weighted:
        modes = (modes.astype(jnp.float32) * rest[0][...]).astype(jnp.bfloat16)
    out_ref[...] = modes

def dft(table, pieces, weight=None):
    count = len(pieces)
    angles, total = pieces[0].shape
    waves = table.shape[0]
    block = math.gcd(total, 4096)
    grid = (total // block,)
    in_specs = [pl.BlockSpec((waves, table.shape[1]), lambda j: (0, 0))]
    in_specs += [pl.BlockSpec((angles, block), lambda j: (0, j)) for _ in pieces]
    args = [table, *pieces]
    if weight is not None:
        in_specs.append(pl.BlockSpec((1, block), lambda j: (0, j)))
        args.append(weight)
    return pl.pallas_call(
        functools.partial(dft_kernel, count=count, weighted=weight is not None),
        grid=grid,
        in_specs=in_specs,
        out_specs=pl.BlockSpec((waves, block), lambda j: (0, j)),
        out_shape=jax.ShapeDtypeStruct((waves, total), jnp.bfloat16),
    )(*args)


def piece_tables(count, local_angles, axis, wave_order=None):
    here = lax.axis_index(axis)
    blocks = count // local_angles
    if wave_order is None:
        wave_order = jnp.arange(count, dtype=jnp.int32)
    wave_index = wave_order - count // 2
    scaling = 1.0 / math.sqrt(count)
    columns = []
    for shift in range(blocks):
        angle_index = ((here - shift) % blocks) * local_angles + jnp.arange(local_angles, dtype=jnp.int32)
        residues = wave_index[:, None] * angle_index[None, :] % count
        phases = 2.0 * math.pi * residues.astype(jnp.float32) / count
        columns.append((jnp.cos(phases) * scaling).astype(jnp.bfloat16))
        columns.append((jnp.sin(phases) * scaling).astype(jnp.bfloat16))
    return jnp.concatenate(columns, axis=1)


def dft_tables(count):
    wave_index = jnp.arange(count, dtype=jnp.int32) - count // 2
    angle_index = jnp.arange(count, dtype=jnp.int32)
    residues = wave_index[:, None] * angle_index[None, :] % count
    phases = 2.0 * math.pi * residues.astype(jnp.float32) / count
    scaling = 1.0 / math.sqrt(count)
    return (
        (jnp.cos(phases) * scaling).astype(jnp.bfloat16),
        (jnp.sin(phases) * scaling).astype(jnp.bfloat16),
    )


def combine_parts(cos_part, sin_part, half):
    real_part = cos_part[..., :half] + sin_part[..., half:]
    imag_part = cos_part[..., half:] - sin_part[..., :half]
    return jnp.concatenate([real_part, imag_part], axis=-1).astype(jnp.bfloat16)


def complex_blocks(product, half):
    upper_rows = product[..., :half, :]
    lower_rows = product[..., half:, :]
    pieces = []
    for offset in (0, 2 * half):
        pieces.append(
            upper_rows[..., offset : offset + half]
            + lower_rows[..., offset + half : offset + 2 * half]
        )
        pieces.append(
            upper_rows[..., offset + half : offset + 2 * half]
            - lower_rows[..., offset : offset + half]
        )
    return jnp.concatenate(pieces, axis=-1)


def local(direct_snapshots, adjoint_snapshots, quad_weight, mean_velocity, diffusivity):
    local_angles, axial_cells, radial_cells, columns = direct_snapshots.shape
    snap_count = columns // 2
    total_angles = local_angles * lax.axis_size("ka")
    table = piece_tables(total_angles, local_angles, "ka")
    first_wave = lax.axis_index("ka") * local_angles
    band_count = lax.axis_size("ka")
    band = radial_cells // band_count
    lanes = axial_cells * band * columns
    norm_factor = 1.0 / math.sqrt(axial_cells * lax.axis_size("gx") * radial_cells)
    band_weight = lax.dynamic_slice_in_dim(
        quad_weight * norm_factor, lax.axis_index("ka") * band, band, axis=1
    )
    lane_weight = jnp.broadcast_to(band_weight[:, :, None], (axial_cells, band, columns)).reshape(1, lanes)

    def transform_all(snapshots, weight=None):
        pieces = [piece.reshape(local_angles, lanes) for piece in exchange(snapshots, "ka", 2)]
        modes = dft(table, pieces, weight)
        return modes.reshape(total_angles, axial_cells, band, columns)

    direct_modes = in_source_order(exchange(transform_all(direct_snapshots), "ka", 0), "ka", 2)
    weighted = in_source_order(
        exchange(transform_all(adjoint_snapshots, lane_weight), "ka", 0), "ka", 2
    )
    padded = padded_2(direct_modes, (("gx", 1),), 1)
    field_f32 = direct_modes.astype(jnp.float32)
    forward = padded[:, 2:].astype(jnp.float32)
    behind = padded[:, :-2].astype(jnp.float32)
    radial_pad = jnp.pad(field_f32, ((0, 0), (0, 0), (1, 1), (0, 0)))
    outward = radial_pad[:, :, 2:]
    inward = radial_pad[:, :, :-2]
    radius = 0.25 + (jnp.arange(radial_cells, dtype=jnp.float32) + 0.5) / radial_cells
    wavenumber = (
        first_wave + jnp.arange(local_angles, dtype=jnp.int32) - total_angles // 2
    ).astype(jnp.float32) / total_angles
    azimuthal = (wavenumber[:, None] / radius[None, :]) ** 2
    velocity = mean_velocity[None, :, :, None]
    diffusion = diffusivity[None, :, :, None]
    image = (
        -velocity * (forward - behind) * 0.5
        + diffusion
        * (
            forward
            + behind
            + outward
            + inward
            - 4.0 * field_f32
            - azimuthal[:, None, :, None] * field_f32
        )
    ).astype(jnp.bfloat16)
    right_side = jnp.concatenate([direct_modes, image], axis=-1)
    product = jnp.einsum(
        "kpa,kpb->kab",
        weighted.reshape(local_angles, -1, columns),
        right_side.reshape(local_angles, -1, 2 * columns),
        preferred_element_type=jnp.float32,
    )
    gram_terms = complex_blocks(product, snap_count).reshape(local_angles * snap_count, 2 * columns)
    row_count = gram_terms.shape[0] // lax.axis_size("gx")
    row_index = lax.axis_index("gx") * row_count + jnp.arange(row_count, dtype=jnp.int32)
    owner = row_index // snap_count
    selector = (owner[:, None] == jnp.arange(local_angles, dtype=jnp.int32)[None, :]).astype(
        jnp.float32
    )
    shares = gram_terms.astype(jnp.bfloat16).reshape(lax.axis_size("gx"), row_count, 2 * columns)
    shares = lax.all_to_all(shares, "gx", split_axis=0, concat_axis=0, tiled=True)
    own_rows = jnp.sum(shares.astype(jnp.float32), axis=0)
    row_energy = jnp.sum(own_rows[:, :columns] ** 2, axis=1)
    energy = jnp.sum(gather_small(jnp.sum(selector * row_energy[:, None], axis=0), "gx"), axis=0)
    mean_sq = energy / (2.0 * snap_count * snap_count)
    row_scale = jnp.sum(selector * lax.rsqrt(mean_sq + epsilon)[None, :], axis=1)
    hankel_gram = own_rows[:, :columns] * row_scale[:, None]
    reduced_operator = own_rows[:, columns:] * row_scale[:, None]
    hankel_norm = jnp.sqrt(mean_sq)
    return (hankel_gram, reduced_operator, hankel_norm)


def core_pairs(cells, partner_pairs):
    return lax.ppermute(cells, "ka", partner_pairs)


def by_chip(direct_snapshots, adjoint_snapshots, quad_weight, mean_velocity, diffusivity):
    local_angles, axial_cells, radial_cells, columns = direct_snapshots.shape
    snap_count = columns // 2
    band_count = lax.axis_size("ka")
    axial_count = lax.axis_size("gx")
    total_angles = local_angles * band_count
    band_index = lax.axis_index("ka")
    core = band_index % 2
    side = band_index // 2
    band = radial_cells // band_count
    lanes = axial_cells * band * columns
    half = total_angles // 2
    row = jnp.arange(total_angles, dtype=jnp.int32)
    wave_order = (((row % half) // local_angles) * 2 + row // half) * local_angles + row % local_angles
    table = piece_tables(total_angles, local_angles, "ka", wave_order)
    norm_factor = 1.0 / math.sqrt(axial_cells * axial_count * radial_cells)
    band_weight = lax.dynamic_slice_in_dim(quad_weight * norm_factor, band_index * band, band, axis=1)
    lane_weight = jnp.broadcast_to(band_weight[:, :, None], (axial_cells, band, columns)).reshape(1, lanes)
    across_cores = [(0, 1), (1, 0), (2, 3), (3, 2)]

    def transform_all(snapshots, weight=None):
        pieces = [piece.reshape(local_angles, lanes) for piece in exchange(snapshots, "ka", 2)]
        modes = dft(table, pieces, weight).reshape(2, half, axial_cells, band, columns)
        kept = lax.dynamic_index_in_dim(modes, core, 0, keepdims=False)
        sent = lax.dynamic_index_in_dim(modes, 1 - core, 0, keepdims=False)
        stacked = jnp.stack([kept, core_pairs(sent, across_cores)])
        lower = lax.dynamic_index_in_dim(stacked, core, 0, keepdims=False)
        upper = lax.dynamic_index_in_dim(stacked, 1 - core, 0, keepdims=False)
        return jnp.concatenate([lower, upper], axis=2)

    field = transform_all(direct_snapshots)
    weighted = transform_all(adjoint_snapshots, lane_weight)
    span = 2 * band
    up_pairs = [(0, 2), (1, 3)]
    down_pairs = [(2, 0), (3, 1)]
    below = core_pairs(field[:, :, span - 1 :], up_pairs)
    above = core_pairs(field[:, :, :1], down_pairs)
    radial_halo = jnp.concatenate([below, field, above], axis=2).astype(jnp.float32)
    outward = radial_halo[:, :, 2:]
    inward = radial_halo[:, :, :-2]
    padded = padded_2(field, (("gx", 1),), 1)
    field_f32 = field.astype(jnp.float32)
    forward = padded[:, 2:].astype(jnp.float32)
    behind = padded[:, :-2].astype(jnp.float32)
    first_radial = side * span
    radial_index = (first_radial + jnp.arange(span, dtype=jnp.int32)).astype(jnp.float32)
    radius = 0.25 + (radial_index + 0.5) / radial_cells
    local_row = jnp.arange(half, dtype=jnp.int32)
    wave = ((local_row // local_angles) * 2 + core) * local_angles + local_row % local_angles
    wavenumber = (wave - total_angles // 2).astype(jnp.float32) / total_angles
    azimuthal = (wavenumber[:, None] / radius[None, :]) ** 2
    velocity = lax.dynamic_slice_in_dim(mean_velocity, first_radial, span, axis=1)[None, :, :, None]
    diffusion = lax.dynamic_slice_in_dim(diffusivity, first_radial, span, axis=1)[None, :, :, None]
    image = (
        -velocity * (forward - behind) * 0.5
        + diffusion
        * (
            forward
            + behind
            + outward
            + inward
            - 4.0 * field_f32
            - azimuthal[:, None, :, None] * field_f32
        )
    ).astype(jnp.bfloat16)
    right_side = jnp.concatenate([field, image], axis=-1)
    product = jnp.einsum(
        "kpa,kpb->kab",
        weighted.reshape(half, -1, columns),
        right_side.reshape(half, -1, 2 * columns),
        preferred_element_type=jnp.float32,
    )
    gram_terms = complex_blocks(product, snap_count).reshape(2, local_angles * snap_count, 2 * columns)
    mine = lax.dynamic_index_in_dim(gram_terms, side, 0, keepdims=False)
    theirs = lax.dynamic_index_in_dim(gram_terms, 1 - side, 0, keepdims=False).astype(jnp.bfloat16)
    across_sides = [(0, 2), (1, 3), (2, 0), (3, 1)]
    summed = mine + core_pairs(theirs, across_sides).astype(jnp.float32)
    row_count = local_angles * snap_count // axial_count
    shares = summed.astype(jnp.bfloat16).reshape(axial_count, row_count, 2 * columns)
    shares = lax.all_to_all(shares, "gx", split_axis=0, concat_axis=0, tiled=True)
    own_rows = jnp.sum(shares.astype(jnp.float32), axis=0)
    row_index = lax.axis_index("gx") * row_count + jnp.arange(row_count, dtype=jnp.int32)
    owner = row_index // snap_count
    selector = (owner[:, None] == jnp.arange(local_angles, dtype=jnp.int32)[None, :]).astype(
        jnp.float32
    )
    row_energy = jnp.sum(own_rows[:, :columns] ** 2, axis=1)
    energy = jnp.sum(gather_small(jnp.sum(selector * row_energy[:, None], axis=0), "gx"), axis=0)
    mean_sq = energy / (2.0 * snap_count * snap_count)
    row_scale = jnp.sum(selector * lax.rsqrt(mean_sq + epsilon)[None, :], axis=1)
    hankel_gram = own_rows[:, :columns] * row_scale[:, None]
    reduced_operator = own_rows[:, columns:] * row_scale[:, None]
    hankel_norm = jnp.sqrt(mean_sq)
    return (hankel_gram, reduced_operator, hankel_norm)


def dispatch(direct_snapshots, *rest):
    local_angles, _, radial_cells, _ = direct_snapshots.shape
    fits = lax.axis_size("ka") == 4 and radial_cells % 4 == 0
    body = by_chip if fits else local
    return body(direct_snapshots, *rest)


def solution(mesh):
    placed = (
        P("ka", "gx", None, None),
        P("ka", "gx", None, None),
        P("gx", None),
        P("gx", None),
        P("gx", None),
    )
    return jax.shard_map(
        dispatch,
        mesh=mesh,
        in_specs=placed,
        out_specs=(P(("ka", "gx"), None), P(("ka", "gx"), None), P("ka")),
        check_vma=False,
    )
```

```python
import functools
import math

import jax
import jax.numpy as jnp
from jax import lax
from jax.experimental import pallas as pl
from jax.experimental.pallas import tpu as pltpu
from jax.sharding import PartitionSpec as P

epsilon = 1e-06


def padded_2(cells, sides, width):
    for axis, dim in sides:
        count = lax.axis_size(axis)
        ends = count - 1
        head = lax.slice_in_dim(cells, 0, width, axis=dim)
        tail = lax.slice_in_dim(cells, cells.shape[dim] - width, cells.shape[dim], axis=dim)
        cells = jnp.concatenate(
            [
                lax.ppermute(tail, axis, [(i, (i + 1) % count) for i in range(ends)]),
                cells,
                lax.ppermute(head, axis, [((i + 1) % count, i) for i in range(ends)]),
            ],
            axis=dim,
        )
    return cells


def gather_small(values, axis):
    count = lax.axis_size(axis)
    copies = jnp.broadcast_to(values[None], (count,) + values.shape)
    return lax.all_to_all(copies, axis, split_axis=0, concat_axis=0, tiled=True)


def exchange(cells, axis, split_axis, offset=0, width=None):
    count = lax.axis_size(axis)
    here = lax.axis_index(axis)
    stride = cells.shape[split_axis] // count
    width = stride if width is None else width
    pieces = []
    for shift in range(count):
        start = ((here + shift) % count) * stride + offset
        piece = lax.dynamic_slice_in_dim(cells, start, width, axis=split_axis)
        if shift:
            piece = lax.ppermute(piece, axis, [(j, (j + shift) % count) for j in range(count)])
        pieces.append(piece)
    return pieces


def in_source_order(pieces, axis, concat_axis):
    count = len(pieces)
    here = lax.axis_index(axis)
    stacked = jnp.stack(pieces)
    ordered = [lax.dynamic_index_in_dim(stacked, (here - source) % count, 0, keepdims=False) for source in range(count)]
    return jnp.concatenate(ordered, axis=concat_axis)


def shifted_tables(count, local_angles, axis):
    here = lax.axis_index(axis)
    blocks = count // local_angles
    wave_index = jnp.arange(count, dtype=jnp.int32) - count // 2
    position = jnp.arange(count, dtype=jnp.int32)
    angle_index = ((here - position // local_angles) % blocks) * local_angles + position % local_angles
    residues = wave_index[:, None] * angle_index[None, :] % count
    phases = 2.0 * math.pi * residues.astype(jnp.float32) / count
    scaling = 1.0 / math.sqrt(count)
    return (
        (jnp.cos(phases) * scaling).astype(jnp.bfloat16),
        (jnp.sin(phases) * scaling).astype(jnp.bfloat16),
    )


def dft_kernel(*refs, count, weighted):
    table_ref = refs[0]
    piece_refs = refs[1:1 + count]
    rest = refs[1 + count:]
    out_ref = rest[-1]
    width = piece_refs[0].shape[1]
    lane = lax.broadcasted_iota(jnp.int32, (1, width), 1) % 128
    low = lane < 64
    packed = piece_refs[0].shape[0] % 16 == 0
    rows = []
    for piece_ref in piece_refs:
        x = piece_ref[...]
        if not packed:
            x = x.astype(jnp.float32)
        swapped = jnp.where(low, pltpu.roll(x, width - 64, 1), -pltpu.roll(x, 64, 1))
        rows.append(x)
        rows.append(swapped)
    stacked = jnp.concatenate(rows, axis=0).astype(jnp.bfloat16)
    acc = jnp.dot(table_ref[...], stacked, preferred_element_type=jnp.float32)
    modes = acc.astype(jnp.bfloat16)
    if weighted:
        modes = (modes.astype(jnp.float32) * rest[0][...]).astype(jnp.bfloat16)
    out_ref[...] = modes

def dft(table, pieces, weight=None):
    count = len(pieces)
    angles, total = pieces[0].shape
    waves = table.shape[0]
    block = math.gcd(total, 4096)
    grid = (total // block,)
    in_specs = [pl.BlockSpec((waves, table.shape[1]), lambda j: (0, 0))]
    in_specs += [pl.BlockSpec((angles, block), lambda j: (0, j)) for _ in pieces]
    args = [table, *pieces]
    if weight is not None:
        in_specs.append(pl.BlockSpec((1, block), lambda j: (0, j)))
        args.append(weight)
    return pl.pallas_call(
        functools.partial(dft_kernel, count=count, weighted=weight is not None),
        grid=grid,
        in_specs=in_specs,
        out_specs=pl.BlockSpec((waves, block), lambda j: (0, j)),
        out_shape=jax.ShapeDtypeStruct((waves, total), jnp.bfloat16),
    )(*args)


def piece_tables(count, local_angles, axis, wave_order):
    here = lax.axis_index(axis)
    blocks = count // local_angles
    wave_index = wave_order - count // 2
    scaling = 1.0 / math.sqrt(count)
    columns = []
    for shift in range(blocks):
        angle_index = ((here - shift) % blocks) * local_angles + jnp.arange(local_angles, dtype=jnp.int32)
        residues = wave_index[:, None] * angle_index[None, :] % count
        phases = 2.0 * math.pi * residues.astype(jnp.float32) / count
        columns.append((jnp.cos(phases) * scaling).astype(jnp.bfloat16))
        columns.append((jnp.sin(phases) * scaling).astype(jnp.bfloat16))
    return jnp.concatenate(columns, axis=1)


def dft_tables(count):
    wave_index = jnp.arange(count, dtype=jnp.int32) - count // 2
    angle_index = jnp.arange(count, dtype=jnp.int32)
    residues = wave_index[:, None] * angle_index[None, :] % count
    phases = 2.0 * math.pi * residues.astype(jnp.float32) / count
    scaling = 1.0 / math.sqrt(count)
    return (
        (jnp.cos(phases) * scaling).astype(jnp.bfloat16),
        (jnp.sin(phases) * scaling).astype(jnp.bfloat16),
    )


def combine_parts(cos_part, sin_part, half):
    real_part = cos_part[..., :half] + sin_part[..., half:]
    imag_part = cos_part[..., half:] - sin_part[..., :half]
    return jnp.concatenate([real_part, imag_part], axis=-1).astype(jnp.bfloat16)


def complex_blocks(product, half):
    upper_rows = product[..., :half, :]
    lower_rows = product[..., half:, :]
    pieces = []
    for offset in (0, 2 * half):
        pieces.append(
            upper_rows[..., offset : offset + half]
            + lower_rows[..., offset + half : offset + 2 * half]
        )
        pieces.append(
            upper_rows[..., offset + half : offset + 2 * half]
            - lower_rows[..., offset : offset + half]
        )
    return jnp.concatenate(pieces, axis=-1)


def local(direct_snapshots, adjoint_snapshots, quad_weight, mean_velocity, diffusivity):
    local_angles, axial_cells, radial_cells, columns = direct_snapshots.shape
    snap_count = columns // 2
    band_count = lax.axis_size("ka")
    axial_count = lax.axis_size("gx")
    total_angles = local_angles * band_count
    owned = local_angles // axial_count
    halves = 2 if local_angles % axial_count == 0 and owned % 2 == 0 else 1
    half_waves = local_angles // halves
    position = jnp.arange(local_angles, dtype=jnp.int32)
    if halves == 1:
        local_order = position
    else:
        part = owned // halves
        within = position % half_waves
        local_order = (within // part) * owned + (position // half_waves) * part + within % part
    wave_order = (
        jnp.arange(band_count, dtype=jnp.int32)[:, None] * local_angles + local_order[None, :]
    ).reshape(total_angles)
    table = piece_tables(total_angles, local_angles, "ka", wave_order)
    first_wave = lax.axis_index("ka") * local_angles
    band = radial_cells // band_count
    lanes = axial_cells * band * columns
    norm_factor = 1.0 / math.sqrt(axial_cells * axial_count * radial_cells)
    band_weight = lax.dynamic_slice_in_dim(
        quad_weight * norm_factor, lax.axis_index("ka") * band, band, axis=1
    )
    lane_weight = jnp.broadcast_to(band_weight[:, :, None], (axial_cells, band, columns)).reshape(1, lanes)

    def transform_all(snapshots, weight=None):
        pieces = [piece.reshape(local_angles, lanes) for piece in exchange(snapshots, "ka", 2)]
        modes = dft(table, pieces, weight)
        return modes.reshape(total_angles, axial_cells, band, columns)

    direct_all = transform_all(direct_snapshots)
    weighted_all = transform_all(adjoint_snapshots, lane_weight)
    radius = 0.25 + (jnp.arange(radial_cells, dtype=jnp.float32) + 0.5) / radial_cells
    velocity = mean_velocity[None, :, :, None]
    diffusion = diffusivity[None, :, :, None]
    row_count = local_angles * snap_count // axial_count
    half_rows = row_count // halves
    own_parts = []
    for half in range(halves):
        offset = half * half_waves
        direct_modes = in_source_order(exchange(direct_all, "ka", 0, offset, half_waves), "ka", 2)
        weighted = in_source_order(exchange(weighted_all, "ka", 0, offset, half_waves), "ka", 2)
        padded = padded_2(direct_modes, (("gx", 1),), 1)
        field_f32 = direct_modes.astype(jnp.float32)
        forward = padded[:, 2:].astype(jnp.float32)
        behind = padded[:, :-2].astype(jnp.float32)
        radial_pad = jnp.pad(field_f32, ((0, 0), (0, 0), (1, 1), (0, 0)))
        outward = radial_pad[:, :, 2:]
        inward = radial_pad[:, :, :-2]
        wavenumber = (
            first_wave + local_order[offset : offset + half_waves] - total_angles // 2
        ).astype(jnp.float32) / total_angles
        azimuthal = (wavenumber[:, None] / radius[None, :]) ** 2
        image = (
            -velocity * (forward - behind) * 0.5
            + diffusion
            * (
                forward
                + behind
                + outward
                + inward
                - 4.0 * field_f32
                - azimuthal[:, None, :, None] * field_f32
            )
        ).astype(jnp.bfloat16)
        right_side = jnp.concatenate([direct_modes, image], axis=-1)
        product = jnp.einsum(
            "kpa,kpb->kab",
            weighted.reshape(half_waves, -1, columns),
            right_side.reshape(half_waves, -1, 2 * columns),
            preferred_element_type=jnp.float32,
        )
        gram_terms = complex_blocks(product, snap_count).reshape(half_waves * snap_count, 2 * columns)
        shares = gram_terms.astype(jnp.bfloat16).reshape(axial_count, half_rows, 2 * columns)
        if half + 1 < halves:
            shares, direct_all, weighted_all = lax.optimization_barrier((shares, direct_all, weighted_all))
        shares = lax.all_to_all(shares, "gx", split_axis=0, concat_axis=0, tiled=True)
        own_parts.append(jnp.sum(shares.astype(jnp.float32), axis=0))
    own_rows = jnp.concatenate(own_parts, axis=0)
    row_index = lax.axis_index("gx") * row_count + jnp.arange(row_count, dtype=jnp.int32)
    owner = row_index // snap_count
    selector = (owner[:, None] == jnp.arange(local_angles, dtype=jnp.int32)[None, :]).astype(
        jnp.float32
    )
    row_energy = jnp.sum(own_rows[:, :columns] ** 2, axis=1)
    energy = jnp.sum(gather_small(jnp.sum(selector * row_energy[:, None], axis=0), "gx"), axis=0)
    mean_sq = energy / (2.0 * snap_count * snap_count)
    row_scale = jnp.sum(selector * lax.rsqrt(mean_sq + epsilon)[None, :], axis=1)
    hankel_gram = own_rows[:, :columns] * row_scale[:, None]
    reduced_operator = own_rows[:, columns:] * row_scale[:, None]
    hankel_norm = jnp.sqrt(mean_sq)
    return (hankel_gram, reduced_operator, hankel_norm)


def solution(mesh):
    placed = (
        P("ka", "gx", None, None),
        P("ka", "gx", None, None),
        P("gx", None),
        P("gx", None),
        P("gx", None),
    )
    return jax.shard_map(
        local,
        mesh=mesh,
        in_specs=placed,
        out_specs=(P(("ka", "gx"), None), P(("ka", "gx"), None), P("ka")),
        check_vma=False,
    )
```

```python
import functools
import math

import jax
import jax.numpy as jnp
from jax import lax
from jax.experimental import pallas as pl
from jax.experimental.pallas import tpu as pltpu
from jax.sharding import PartitionSpec as P

epsilon = 1e-06


def padded_2(cells, sides, width):
    for axis, dim in sides:
        count = lax.axis_size(axis)
        ends = count - 1
        head = lax.slice_in_dim(cells, 0, width, axis=dim)
        tail = lax.slice_in_dim(cells, cells.shape[dim] - width, cells.shape[dim], axis=dim)
        cells = jnp.concatenate(
            [
                lax.ppermute(tail, axis, [(i, (i + 1) % count) for i in range(ends)]),
                cells,
                lax.ppermute(head, axis, [((i + 1) % count, i) for i in range(ends)]),
            ],
            axis=dim,
        )
    return cells


def gather_small(values, axis):
    count = lax.axis_size(axis)
    copies = jnp.broadcast_to(values[None], (count,) + values.shape)
    return lax.all_to_all(copies, axis, split_axis=0, concat_axis=0, tiled=True)


def exchange(cells, axis, split_axis, offset=0, width=None):
    count = lax.axis_size(axis)
    here = lax.axis_index(axis)
    stride = cells.shape[split_axis] // count
    width = stride if width is None else width
    pieces = []
    for shift in range(count):
        start = ((here + shift) % count) * stride + offset
        piece = lax.dynamic_slice_in_dim(cells, start, width, axis=split_axis)
        if shift:
            piece = lax.ppermute(piece, axis, [(j, (j + shift) % count) for j in range(count)])
        pieces.append(piece)
    return pieces


def in_source_order(pieces, axis, concat_axis):
    count = len(pieces)
    here = lax.axis_index(axis)
    stacked = jnp.stack(pieces)
    ordered = [lax.dynamic_index_in_dim(stacked, (here - source) % count, 0, keepdims=False) for source in range(count)]
    return jnp.concatenate(ordered, axis=concat_axis)


def shifted_tables(count, local_angles, axis):
    here = lax.axis_index(axis)
    blocks = count // local_angles
    wave_index = jnp.arange(count, dtype=jnp.int32) - count // 2
    position = jnp.arange(count, dtype=jnp.int32)
    angle_index = ((here - position // local_angles) % blocks) * local_angles + position % local_angles
    residues = wave_index[:, None] * angle_index[None, :] % count
    phases = 2.0 * math.pi * residues.astype(jnp.float32) / count
    scaling = 1.0 / math.sqrt(count)
    return (
        (jnp.cos(phases) * scaling).astype(jnp.bfloat16),
        (jnp.sin(phases) * scaling).astype(jnp.bfloat16),
    )


def dft_kernel(*refs, count, weighted):
    table_ref = refs[0]
    piece_refs = refs[1:1 + count]
    rest = refs[1 + count:]
    out_ref = rest[-1]
    width = piece_refs[0].shape[1]
    lane = lax.broadcasted_iota(jnp.int32, (1, width), 1) % 128
    low = lane < 64
    packed = piece_refs[0].shape[0] % 16 == 0
    rows = []
    for piece_ref in piece_refs:
        x = piece_ref[...]
        if not packed:
            x = x.astype(jnp.float32)
        swapped = jnp.where(low, pltpu.roll(x, width - 64, 1), -pltpu.roll(x, 64, 1))
        rows.append(x)
        rows.append(swapped)
    stacked = jnp.concatenate(rows, axis=0).astype(jnp.bfloat16)
    acc = jnp.dot(table_ref[...], stacked, preferred_element_type=jnp.float32)
    modes = acc.astype(jnp.bfloat16)
    if weighted:
        modes = (modes.astype(jnp.float32) * rest[0][...]).astype(jnp.bfloat16)
    out_ref[...] = modes

def dft(table, pieces, weight=None):
    count = len(pieces)
    angles, total = pieces[0].shape
    waves = table.shape[0]
    block = math.gcd(total, 4096)
    grid = (total // block,)
    in_specs = [pl.BlockSpec((waves, table.shape[1]), lambda j: (0, 0))]
    in_specs += [pl.BlockSpec((angles, block), lambda j: (0, j)) for _ in pieces]
    args = [table, *pieces]
    if weight is not None:
        in_specs.append(pl.BlockSpec((1, block), lambda j: (0, j)))
        args.append(weight)
    return pl.pallas_call(
        functools.partial(dft_kernel, count=count, weighted=weight is not None),
        grid=grid,
        in_specs=in_specs,
        out_specs=pl.BlockSpec((waves, block), lambda j: (0, j)),
        out_shape=jax.ShapeDtypeStruct((waves, total), jnp.bfloat16),
    )(*args)


def piece_tables(count, local_angles, axis, wave_order):
    here = lax.axis_index(axis)
    blocks = count // local_angles
    wave_index = wave_order - count // 2
    scaling = 1.0 / math.sqrt(count)
    columns = []
    for shift in range(blocks):
        angle_index = ((here - shift) % blocks) * local_angles + jnp.arange(local_angles, dtype=jnp.int32)
        residues = wave_index[:, None] * angle_index[None, :] % count
        phases = 2.0 * math.pi * residues.astype(jnp.float32) / count
        columns.append((jnp.cos(phases) * scaling).astype(jnp.bfloat16))
        columns.append((jnp.sin(phases) * scaling).astype(jnp.bfloat16))
    return jnp.concatenate(columns, axis=1)


def dft_tables(count):
    wave_index = jnp.arange(count, dtype=jnp.int32) - count // 2
    angle_index = jnp.arange(count, dtype=jnp.int32)
    residues = wave_index[:, None] * angle_index[None, :] % count
    phases = 2.0 * math.pi * residues.astype(jnp.float32) / count
    scaling = 1.0 / math.sqrt(count)
    return (
        (jnp.cos(phases) * scaling).astype(jnp.bfloat16),
        (jnp.sin(phases) * scaling).astype(jnp.bfloat16),
    )


def combine_parts(cos_part, sin_part, half):
    real_part = cos_part[..., :half] + sin_part[..., half:]
    imag_part = cos_part[..., half:] - sin_part[..., :half]
    return jnp.concatenate([real_part, imag_part], axis=-1).astype(jnp.bfloat16)


def complex_blocks(product, half):
    upper_rows = product[..., :half, :]
    lower_rows = product[..., half:, :]
    pieces = []
    for offset in (0, 2 * half):
        pieces.append(
            upper_rows[..., offset : offset + half]
            + lower_rows[..., offset + half : offset + 2 * half]
        )
        pieces.append(
            upper_rows[..., offset + half : offset + 2 * half]
            - lower_rows[..., offset : offset + half]
        )
    return jnp.concatenate(pieces, axis=-1)


def local(direct_snapshots, adjoint_snapshots, quad_weight, mean_velocity, diffusivity):
    local_angles, axial_cells, radial_cells, columns = direct_snapshots.shape
    snap_count = columns // 2
    band_count = lax.axis_size("ka")
    axial_count = lax.axis_size("gx")
    total_angles = local_angles * band_count
    owned = local_angles // axial_count
    halves = 2 if local_angles % axial_count == 0 and owned % 2 == 0 else 1
    half_waves = local_angles // halves
    position = jnp.arange(local_angles, dtype=jnp.int32)
    if halves == 1:
        local_order = position
    else:
        part = owned // halves
        within = position % half_waves
        local_order = (within // part) * owned + (position // half_waves) * part + within % part
    wave_order = (
        jnp.arange(band_count, dtype=jnp.int32)[:, None] * local_angles + local_order[None, :]
    ).reshape(total_angles)
    table = piece_tables(total_angles, local_angles, "ka", wave_order)
    first_wave = lax.axis_index("ka") * local_angles
    band = radial_cells // band_count
    lanes = axial_cells * band * columns
    norm_factor = 1.0 / math.sqrt(axial_cells * axial_count * radial_cells)
    band_weight = lax.dynamic_slice_in_dim(
        quad_weight * norm_factor, lax.axis_index("ka") * band, band, axis=1
    )
    lane_weight = jnp.broadcast_to(band_weight[:, :, None], (axial_cells, band, columns)).reshape(1, lanes)

    def transform_all(snapshots, weight=None):
        pieces = [piece.reshape(local_angles, lanes) for piece in exchange(snapshots, "ka", 2)]
        modes = dft(table, pieces, weight)
        return modes.reshape(total_angles, axial_cells, band, columns)

    direct_all = transform_all(direct_snapshots)
    weighted_all = transform_all(adjoint_snapshots, lane_weight)
    radius = 0.25 + (jnp.arange(radial_cells, dtype=jnp.float32) + 0.5) / radial_cells
    velocity = mean_velocity[None, :, :, None]
    diffusion = diffusivity[None, :, :, None]
    row_count = local_angles * snap_count // axial_count
    half_rows = row_count // halves
    own_parts = []
    for half in range(halves):
        offset = half * half_waves
        direct_modes = in_source_order(exchange(direct_all, "ka", 0, offset, half_waves), "ka", 2)
        weighted = in_source_order(exchange(weighted_all, "ka", 0, offset, half_waves), "ka", 2)
        if half + 1 < halves:
            direct_modes, weighted, direct_all, weighted_all = lax.optimization_barrier(
                (direct_modes, weighted, direct_all, weighted_all)
            )
        padded = padded_2(direct_modes, (("gx", 1),), 1)
        field_f32 = direct_modes.astype(jnp.float32)
        forward = padded[:, 2:].astype(jnp.float32)
        behind = padded[:, :-2].astype(jnp.float32)
        radial_pad = jnp.pad(field_f32, ((0, 0), (0, 0), (1, 1), (0, 0)))
        outward = radial_pad[:, :, 2:]
        inward = radial_pad[:, :, :-2]
        wavenumber = (
            first_wave + local_order[offset : offset + half_waves] - total_angles // 2
        ).astype(jnp.float32) / total_angles
        azimuthal = (wavenumber[:, None] / radius[None, :]) ** 2
        image = (
            -velocity * (forward - behind) * 0.5
            + diffusion
            * (
                forward
                + behind
                + outward
                + inward
                - 4.0 * field_f32
                - azimuthal[:, None, :, None] * field_f32
            )
        ).astype(jnp.bfloat16)
        right_side = jnp.concatenate([direct_modes, image], axis=-1)
        product = jnp.einsum(
            "kpa,kpb->kab",
            weighted.reshape(half_waves, -1, columns),
            right_side.reshape(half_waves, -1, 2 * columns),
            preferred_element_type=jnp.float32,
        )
        gram_terms = complex_blocks(product, snap_count).reshape(half_waves * snap_count, 2 * columns)
        shares = gram_terms.astype(jnp.bfloat16).reshape(axial_count, half_rows, 2 * columns)
        shares = lax.all_to_all(shares, "gx", split_axis=0, concat_axis=0, tiled=True)
        own_parts.append(jnp.sum(shares.astype(jnp.float32), axis=0))
    own_rows = jnp.concatenate(own_parts, axis=0)
    row_index = lax.axis_index("gx") * row_count + jnp.arange(row_count, dtype=jnp.int32)
    owner = row_index // snap_count
    selector = (owner[:, None] == jnp.arange(local_angles, dtype=jnp.int32)[None, :]).astype(
        jnp.float32
    )
    row_energy = jnp.sum(own_rows[:, :columns] ** 2, axis=1)
    energy = jnp.sum(gather_small(jnp.sum(selector * row_energy[:, None], axis=0), "gx"), axis=0)
    mean_sq = energy / (2.0 * snap_count * snap_count)
    row_scale = jnp.sum(selector * lax.rsqrt(mean_sq + epsilon)[None, :], axis=1)
    hankel_gram = own_rows[:, :columns] * row_scale[:, None]
    reduced_operator = own_rows[:, columns:] * row_scale[:, None]
    hankel_norm = jnp.sqrt(mean_sq)
    return (hankel_gram, reduced_operator, hankel_norm)


def solution(mesh):
    placed = (
        P("ka", "gx", None, None),
        P("ka", "gx", None, None),
        P("gx", None),
        P("gx", None),
        P("gx", None),
    )
    return jax.shard_map(
        local,
        mesh=mesh,
        in_specs=placed,
        out_specs=(P(("ka", "gx"), None), P(("ka", "gx"), None), P("ka")),
        check_vma=False,
    )
```

```python
import functools
import math

import jax
import jax.numpy as jnp
from jax import lax
from jax.experimental import pallas as pl
from jax.experimental.pallas import tpu as pltpu
from jax.sharding import PartitionSpec as P

epsilon = 1e-06


def padded_2(cells, sides, width):
    for axis, dim in sides:
        count = lax.axis_size(axis)
        ends = count - 1
        head = lax.slice_in_dim(cells, 0, width, axis=dim)
        tail = lax.slice_in_dim(cells, cells.shape[dim] - width, cells.shape[dim], axis=dim)
        cells = jnp.concatenate(
            [
                lax.ppermute(tail, axis, [(i, (i + 1) % count) for i in range(ends)]),
                cells,
                lax.ppermute(head, axis, [((i + 1) % count, i) for i in range(ends)]),
            ],
            axis=dim,
        )
    return cells


def gather_small(values, axis):
    count = lax.axis_size(axis)
    copies = jnp.broadcast_to(values[None], (count,) + values.shape)
    return lax.all_to_all(copies, axis, split_axis=0, concat_axis=0, tiled=True)


def exchange(cells, axis, split_axis):
    count = lax.axis_size(axis)
    here = lax.axis_index(axis)
    width = cells.shape[split_axis] // count
    pieces = []
    for shift in range(count):
        piece = lax.dynamic_slice_in_dim(cells, ((here + shift) % count) * width, width, axis=split_axis)
        if shift:
            piece = lax.ppermute(piece, axis, [(j, (j + shift) % count) for j in range(count)])
        pieces.append(piece)
    return pieces


def in_source_order(pieces, axis, concat_axis):
    count = len(pieces)
    here = lax.axis_index(axis)
    stacked = jnp.stack(pieces)
    ordered = [lax.dynamic_index_in_dim(stacked, (here - source) % count, 0, keepdims=False) for source in range(count)]
    return jnp.concatenate(ordered, axis=concat_axis)


def shifted_tables(count, local_angles, axis):
    here = lax.axis_index(axis)
    blocks = count // local_angles
    wave_index = jnp.arange(count, dtype=jnp.int32) - count // 2
    position = jnp.arange(count, dtype=jnp.int32)
    angle_index = ((here - position // local_angles) % blocks) * local_angles + position % local_angles
    residues = wave_index[:, None] * angle_index[None, :] % count
    phases = 2.0 * math.pi * residues.astype(jnp.float32) / count
    scaling = 1.0 / math.sqrt(count)
    return (
        (jnp.cos(phases) * scaling).astype(jnp.bfloat16),
        (jnp.sin(phases) * scaling).astype(jnp.bfloat16),
    )


def dft_kernel(*refs, count, weighted):
    table_ref = refs[0]
    piece_refs = refs[1:1 + count]
    rest = refs[1 + count:]
    out_ref = rest[-1]
    width = piece_refs[0].shape[1]
    lane = lax.broadcasted_iota(jnp.int32, (1, width), 1) % 128
    low = lane < 64
    packed = piece_refs[0].shape[0] % 16 == 0
    rows = []
    for piece_ref in piece_refs:
        x = piece_ref[...]
        if not packed:
            x = x.astype(jnp.float32)
        swapped = jnp.where(low, pltpu.roll(x, width - 64, 1), -pltpu.roll(x, 64, 1))
        rows.append(x)
        rows.append(swapped)
    stacked = jnp.concatenate(rows, axis=0).astype(jnp.bfloat16)
    acc = jnp.dot(table_ref[...], stacked, preferred_element_type=jnp.float32)
    modes = acc.astype(jnp.bfloat16)
    if weighted:
        modes = (modes.astype(jnp.float32) * rest[0][...]).astype(jnp.bfloat16)
    out_ref[...] = modes

def dft(table, pieces, weight=None):
    count = len(pieces)
    angles, total = pieces[0].shape
    waves = table.shape[0]
    block = math.gcd(total, 4096)
    grid = (total // block,)
    in_specs = [pl.BlockSpec((waves, table.shape[1]), lambda j: (0, 0))]
    in_specs += [pl.BlockSpec((angles, block), lambda j: (0, j)) for _ in pieces]
    args = [table, *pieces]
    if weight is not None:
        in_specs.append(pl.BlockSpec((1, block), lambda j: (0, j)))
        args.append(weight)
    return pl.pallas_call(
        functools.partial(dft_kernel, count=count, weighted=weight is not None),
        grid=grid,
        in_specs=in_specs,
        out_specs=pl.BlockSpec((waves, block), lambda j: (0, j)),
        out_shape=jax.ShapeDtypeStruct((waves, total), jnp.bfloat16),
    )(*args)


def piece_tables(count, local_angles, axis):
    here = lax.axis_index(axis)
    blocks = count // local_angles
    wave_index = jnp.arange(count, dtype=jnp.int32) - count // 2
    scaling = 1.0 / math.sqrt(count)
    columns = []
    for shift in range(blocks):
        angle_index = ((here - shift) % blocks) * local_angles + jnp.arange(local_angles, dtype=jnp.int32)
        residues = wave_index[:, None] * angle_index[None, :] % count
        phases = 2.0 * math.pi * residues.astype(jnp.float32) / count
        columns.append((jnp.cos(phases) * scaling).astype(jnp.bfloat16))
        columns.append((jnp.sin(phases) * scaling).astype(jnp.bfloat16))
    return jnp.concatenate(columns, axis=1)


def dft_tables(count):
    wave_index = jnp.arange(count, dtype=jnp.int32) - count // 2
    angle_index = jnp.arange(count, dtype=jnp.int32)
    residues = wave_index[:, None] * angle_index[None, :] % count
    phases = 2.0 * math.pi * residues.astype(jnp.float32) / count
    scaling = 1.0 / math.sqrt(count)
    return (
        (jnp.cos(phases) * scaling).astype(jnp.bfloat16),
        (jnp.sin(phases) * scaling).astype(jnp.bfloat16),
    )


def combine_parts(cos_part, sin_part, half):
    real_part = cos_part[..., :half] + sin_part[..., half:]
    imag_part = cos_part[..., half:] - sin_part[..., :half]
    return jnp.concatenate([real_part, imag_part], axis=-1).astype(jnp.bfloat16)


def complex_blocks(product, half):
    upper_rows = product[..., :half, :]
    lower_rows = product[..., half:, :]
    pieces = []
    for offset in (0, 2 * half):
        pieces.append(
            upper_rows[..., offset : offset + half]
            + lower_rows[..., offset + half : offset + 2 * half]
        )
        pieces.append(
            upper_rows[..., offset + half : offset + 2 * half]
            - lower_rows[..., offset : offset + half]
        )
    return jnp.concatenate(pieces, axis=-1)


def local(direct_snapshots, adjoint_snapshots, quad_weight, mean_velocity, diffusivity):
    local_angles, axial_cells, radial_cells, columns = direct_snapshots.shape
    snap_count = columns // 2
    total_angles = local_angles * lax.axis_size("ka")
    table = piece_tables(total_angles, local_angles, "ka")
    first_wave = lax.axis_index("ka") * local_angles
    band_count = lax.axis_size("ka")
    band = radial_cells // band_count
    lanes = axial_cells * band * columns
    norm_factor = 1.0 / math.sqrt(axial_cells * lax.axis_size("gx") * radial_cells)
    band_weight = lax.dynamic_slice_in_dim(
        quad_weight * norm_factor, lax.axis_index("ka") * band, band, axis=1
    )
    lane_weight = jnp.broadcast_to(band_weight[:, :, None], (axial_cells, band, columns)).reshape(1, lanes)

    def transform_all(snapshots, weight=None):
        pieces = [piece.reshape(local_angles, lanes) for piece in exchange(snapshots, "ka", 2)]
        modes = dft(table, pieces, weight)
        return modes.reshape(total_angles, axial_cells, band, columns)

    direct_modes = in_source_order(exchange(transform_all(direct_snapshots), "ka", 0), "ka", 2)
    weighted = in_source_order(
        exchange(transform_all(adjoint_snapshots, lane_weight), "ka", 0), "ka", 2
    )
    padded = padded_2(direct_modes, (("gx", 1),), 1)
    field_f32 = direct_modes.astype(jnp.float32)
    forward = padded[:, 2:].astype(jnp.float32)
    behind = padded[:, :-2].astype(jnp.float32)
    radial_pad = jnp.pad(field_f32, ((0, 0), (0, 0), (1, 1), (0, 0)))
    outward = radial_pad[:, :, 2:]
    inward = radial_pad[:, :, :-2]
    radius = 0.25 + (jnp.arange(radial_cells, dtype=jnp.float32) + 0.5) / radial_cells
    wavenumber = (
        first_wave + jnp.arange(local_angles, dtype=jnp.int32) - total_angles // 2
    ).astype(jnp.float32) / total_angles
    azimuthal = (wavenumber[:, None] / radius[None, :]) ** 2
    velocity = mean_velocity[None, :, :, None]
    diffusion = diffusivity[None, :, :, None]
    image = (
        -velocity * (forward - behind) * 0.5
        + diffusion
        * (
            forward
            + behind
            + outward
            + inward
            - 4.0 * field_f32
            - azimuthal[:, None, :, None] * field_f32
        )
    ).astype(jnp.bfloat16)
    right_side = jnp.concatenate([direct_modes, image], axis=-1)
    product = jnp.einsum(
        "kpa,kpb->kab",
        weighted.reshape(local_angles, -1, columns),
        right_side.reshape(local_angles, -1, 2 * columns),
        preferred_element_type=jnp.float32,
    )
    gram_terms = complex_blocks(product, snap_count).reshape(local_angles * snap_count, 2 * columns)
    row_count = gram_terms.shape[0] // lax.axis_size("gx")
    row_index = lax.axis_index("gx") * row_count + jnp.arange(row_count, dtype=jnp.int32)
    owner = row_index // snap_count
    selector = (owner[:, None] == jnp.arange(local_angles, dtype=jnp.int32)[None, :]).astype(
        jnp.float32
    )
    shares = gram_terms.astype(jnp.bfloat16).reshape(lax.axis_size("gx"), row_count, 2 * columns)

    def reduce_rows(part):
        part = lax.all_to_all(part, "gx", split_axis=0, concat_axis=0, tiled=True)
        return jnp.sum(part.astype(jnp.float32), axis=0)

    own_hankel = reduce_rows(shares[..., :columns])
    row_energy = jnp.sum(own_hankel**2, axis=1)
    energy = jnp.sum(selector * row_energy[:, None], axis=0)
    axial_count = lax.axis_size("gx")
    energy = energy + sum(
        lax.ppermute(energy, "gx", [(j, (j + shift) % axial_count) for j in range(axial_count)])
        for shift in range(1, axial_count)
    )
    own_operator = reduce_rows(shares[..., columns:])
    mean_sq = energy / (2.0 * snap_count * snap_count)
    row_scale = jnp.sum(selector * lax.rsqrt(mean_sq + epsilon)[None, :], axis=1)
    hankel_gram = own_hankel * row_scale[:, None]
    reduced_operator = own_operator * row_scale[:, None]
    hankel_norm = jnp.sqrt(mean_sq)
    return (hankel_gram, reduced_operator, hankel_norm)


def solution(mesh):
    placed = (
        P("ka", "gx", None, None),
        P("ka", "gx", None, None),
        P("gx", None),
        P("gx", None),
        P("gx", None),
    )
    return jax.shard_map(
        local,
        mesh=mesh,
        in_specs=placed,
        out_specs=(P(("ka", "gx"), None), P(("ka", "gx"), None), P("ka")),
        check_vma=False,
    )
```

```python
import functools
import math

import jax
import jax.numpy as jnp
from jax import lax
from jax.experimental import pallas as pl
from jax.experimental.pallas import tpu as pltpu
from jax.sharding import PartitionSpec as P

epsilon = 1e-06


def padded_2(cells, sides, width):
    for axis, dim in sides:
        count = lax.axis_size(axis)
        ends = count - 1
        head = lax.slice_in_dim(cells, 0, width, axis=dim)
        tail = lax.slice_in_dim(cells, cells.shape[dim] - width, cells.shape[dim], axis=dim)
        cells = jnp.concatenate(
            [
                lax.ppermute(tail, axis, [(i, (i + 1) % count) for i in range(ends)]),
                cells,
                lax.ppermute(head, axis, [((i + 1) % count, i) for i in range(ends)]),
            ],
            axis=dim,
        )
    return cells


def gather_small(values, axis):
    count = lax.axis_size(axis)
    copies = jnp.broadcast_to(values[None], (count,) + values.shape)
    return lax.all_to_all(copies, axis, split_axis=0, concat_axis=0, tiled=True)


def exchange(cells, axis, split_axis):
    count = lax.axis_size(axis)
    here = lax.axis_index(axis)
    width = cells.shape[split_axis] // count
    pieces = []
    for shift in range(count):
        piece = lax.dynamic_slice_in_dim(cells, ((here + shift) % count) * width, width, axis=split_axis)
        if shift:
            piece = lax.ppermute(piece, axis, [(j, (j + shift) % count) for j in range(count)])
        pieces.append(piece)
    return pieces


def in_source_order(pieces, axis, concat_axis):
    count = len(pieces)
    here = lax.axis_index(axis)
    stacked = jnp.stack(pieces)
    ordered = [lax.dynamic_index_in_dim(stacked, (here - source) % count, 0, keepdims=False) for source in range(count)]
    return jnp.concatenate(ordered, axis=concat_axis)


def shifted_tables(count, local_angles, axis):
    here = lax.axis_index(axis)
    blocks = count // local_angles
    wave_index = jnp.arange(count, dtype=jnp.int32) - count // 2
    position = jnp.arange(count, dtype=jnp.int32)
    angle_index = ((here - position // local_angles) % blocks) * local_angles + position % local_angles
    residues = wave_index[:, None] * angle_index[None, :] % count
    phases = 2.0 * math.pi * residues.astype(jnp.float32) / count
    scaling = 1.0 / math.sqrt(count)
    return (
        (jnp.cos(phases) * scaling).astype(jnp.bfloat16),
        (jnp.sin(phases) * scaling).astype(jnp.bfloat16),
    )


def dft_kernel(*refs, count, weighted):
    table_ref = refs[0]
    piece_refs = refs[1:1 + count]
    rest = refs[1 + count:]
    out_ref = rest[-1]
    width = piece_refs[0].shape[1]
    lane = lax.broadcasted_iota(jnp.int32, (1, width), 1) % 128
    low = lane < 64
    packed = piece_refs[0].shape[0] % 16 == 0
    rows = []
    for piece_ref in piece_refs:
        x = piece_ref[...]
        if not packed:
            x = x.astype(jnp.float32)
        swapped = jnp.where(low, pltpu.roll(x, width - 64, 1), -pltpu.roll(x, 64, 1))
        rows.append(x)
        rows.append(swapped)
    stacked = jnp.concatenate(rows, axis=0).astype(jnp.bfloat16)
    acc = jnp.dot(table_ref[...], stacked, preferred_element_type=jnp.float32)
    modes = acc.astype(jnp.bfloat16)
    if weighted:
        modes = (modes.astype(jnp.float32) * rest[0][...]).astype(jnp.bfloat16)
    out_ref[...] = modes

def dft(table, pieces, weight=None):
    count = len(pieces)
    angles, total = pieces[0].shape
    waves = table.shape[0]
    block = math.gcd(total, 4096)
    grid = (total // block,)
    in_specs = [pl.BlockSpec((waves, table.shape[1]), lambda j: (0, 0))]
    in_specs += [pl.BlockSpec((angles, block), lambda j: (0, j)) for _ in pieces]
    args = [table, *pieces]
    if weight is not None:
        in_specs.append(pl.BlockSpec((1, block), lambda j: (0, j)))
        args.append(weight)
    return pl.pallas_call(
        functools.partial(dft_kernel, count=count, weighted=weight is not None),
        grid=grid,
        in_specs=in_specs,
        out_specs=pl.BlockSpec((waves, block), lambda j: (0, j)),
        out_shape=jax.ShapeDtypeStruct((waves, total), jnp.bfloat16),
    )(*args)


def piece_tables(count, local_angles, axis):
    here = lax.axis_index(axis)
    blocks = count // local_angles
    wave_index = jnp.arange(count, dtype=jnp.int32) - count // 2
    scaling = 1.0 / math.sqrt(count)
    columns = []
    for shift in range(blocks):
        angle_index = ((here - shift) % blocks) * local_angles + jnp.arange(local_angles, dtype=jnp.int32)
        residues = wave_index[:, None] * angle_index[None, :] % count
        phases = 2.0 * math.pi * residues.astype(jnp.float32) / count
        columns.append((jnp.cos(phases) * scaling).astype(jnp.bfloat16))
        columns.append((jnp.sin(phases) * scaling).astype(jnp.bfloat16))
    return jnp.concatenate(columns, axis=1)


def dft_tables(count):
    wave_index = jnp.arange(count, dtype=jnp.int32) - count // 2
    angle_index = jnp.arange(count, dtype=jnp.int32)
    residues = wave_index[:, None] * angle_index[None, :] % count
    phases = 2.0 * math.pi * residues.astype(jnp.float32) / count
    scaling = 1.0 / math.sqrt(count)
    return (
        (jnp.cos(phases) * scaling).astype(jnp.bfloat16),
        (jnp.sin(phases) * scaling).astype(jnp.bfloat16),
    )


def combine_parts(cos_part, sin_part, half):
    real_part = cos_part[..., :half] + sin_part[..., half:]
    imag_part = cos_part[..., half:] - sin_part[..., :half]
    return jnp.concatenate([real_part, imag_part], axis=-1).astype(jnp.bfloat16)


def complex_blocks(product, half):
    upper_rows = product[..., :half, :]
    lower_rows = product[..., half:, :]
    pieces = []
    for offset in (0, 2 * half):
        pieces.append(
            upper_rows[..., offset : offset + half]
            + lower_rows[..., offset + half : offset + 2 * half]
        )
        pieces.append(
            upper_rows[..., offset + half : offset + 2 * half]
            - lower_rows[..., offset : offset + half]
        )
    return jnp.concatenate(pieces, axis=-1)


def local(direct_snapshots, adjoint_snapshots, quad_weight, mean_velocity, diffusivity):
    local_angles, axial_cells, radial_cells, columns = direct_snapshots.shape
    snap_count = columns // 2
    total_angles = local_angles * lax.axis_size("ka")
    table = piece_tables(total_angles, local_angles, "ka")
    first_wave = lax.axis_index("ka") * local_angles
    band_count = lax.axis_size("ka")
    band = radial_cells // band_count
    lanes = axial_cells * band * columns
    norm_factor = 1.0 / math.sqrt(axial_cells * lax.axis_size("gx") * radial_cells)
    band_weight = lax.dynamic_slice_in_dim(
        quad_weight * norm_factor, lax.axis_index("ka") * band, band, axis=1
    )
    lane_weight = jnp.broadcast_to(band_weight[:, :, None], (axial_cells, band, columns)).reshape(1, lanes)

    def transform_all(snapshots, weight=None):
        pieces = [piece.reshape(local_angles, lanes) for piece in exchange(snapshots, "ka", 2)]
        modes = dft(table, pieces, weight)
        return modes.reshape(total_angles, axial_cells, band, columns)

    direct_modes = in_source_order(exchange(transform_all(direct_snapshots), "ka", 0), "ka", 2)
    weighted = in_source_order(
        exchange(transform_all(adjoint_snapshots, lane_weight), "ka", 0), "ka", 2
    )
    padded = padded_2(direct_modes, (("gx", 1),), 1)
    field_f32 = direct_modes.astype(jnp.float32)
    forward = padded[:, 2:].astype(jnp.float32)
    behind = padded[:, :-2].astype(jnp.float32)
    radial_pad = jnp.pad(field_f32, ((0, 0), (0, 0), (1, 1), (0, 0)))
    outward = radial_pad[:, :, 2:]
    inward = radial_pad[:, :, :-2]
    radius = 0.25 + (jnp.arange(radial_cells, dtype=jnp.float32) + 0.5) / radial_cells
    wavenumber = (
        first_wave + jnp.arange(local_angles, dtype=jnp.int32) - total_angles // 2
    ).astype(jnp.float32) / total_angles
    azimuthal = (wavenumber[:, None] / radius[None, :]) ** 2
    velocity = mean_velocity[None, :, :, None]
    diffusion = diffusivity[None, :, :, None]
    image = (
        -velocity * (forward - behind) * 0.5
        + diffusion
        * (
            forward
            + behind
            + outward
            + inward
            - 4.0 * field_f32
            - azimuthal[:, None, :, None] * field_f32
        )
    ).astype(jnp.bfloat16)
    right_side = jnp.concatenate([direct_modes, image], axis=-1)
    product = jnp.einsum(
        "kpa,kpb->kab",
        weighted.reshape(local_angles, -1, columns),
        right_side.reshape(local_angles, -1, 2 * columns),
        preferred_element_type=jnp.float32,
    )
    gram_terms = complex_blocks(product, snap_count).reshape(local_angles * snap_count, 2 * columns)
    row_count = gram_terms.shape[0] // lax.axis_size("gx")
    row_index = lax.axis_index("gx") * row_count + jnp.arange(row_count, dtype=jnp.int32)
    owner = row_index // snap_count
    selector = (owner[:, None] == jnp.arange(local_angles, dtype=jnp.int32)[None, :]).astype(
        jnp.float32
    )
    shares = gram_terms.astype(jnp.bfloat16).reshape(lax.axis_size("gx"), row_count, 2 * columns)
    own_rows = sum(piece.astype(jnp.float32) for piece in exchange(shares, "gx", 0))[0]
    row_energy = jnp.sum(own_rows[:, :columns] ** 2, axis=1)
    energy = jnp.sum(gather_small(jnp.sum(selector * row_energy[:, None], axis=0), "gx"), axis=0)
    mean_sq = energy / (2.0 * snap_count * snap_count)
    row_scale = jnp.sum(selector * lax.rsqrt(mean_sq + epsilon)[None, :], axis=1)
    hankel_gram = own_rows[:, :columns] * row_scale[:, None]
    reduced_operator = own_rows[:, columns:] * row_scale[:, None]
    hankel_norm = jnp.sqrt(mean_sq)
    return (hankel_gram, reduced_operator, hankel_norm)


def solution(mesh):
    placed = (
        P("ka", "gx", None, None),
        P("ka", "gx", None, None),
        P("gx", None),
        P("gx", None),
        P("gx", None),
    )
    return jax.shard_map(
        local,
        mesh=mesh,
        in_specs=placed,
        out_specs=(P(("ka", "gx"), None), P(("ka", "gx"), None), P("ka")),
        check_vma=False,
    )
```

```python
import functools
import math

import jax
import jax.numpy as jnp
from jax import lax
from jax.experimental import pallas as pl
from jax.experimental.pallas import tpu as pltpu
from jax.sharding import PartitionSpec as P

epsilon = 1e-06


def padded_2(cells, sides, width):
    for axis, dim in sides:
        count = lax.axis_size(axis)
        ends = count - 1
        head = lax.slice_in_dim(cells, 0, width, axis=dim)
        tail = lax.slice_in_dim(cells, cells.shape[dim] - width, cells.shape[dim], axis=dim)
        cells = jnp.concatenate(
            [
                lax.ppermute(tail, axis, [(i, (i + 1) % count) for i in range(ends)]),
                cells,
                lax.ppermute(head, axis, [((i + 1) % count, i) for i in range(ends)]),
            ],
            axis=dim,
        )
    return cells


def gather_small(values, axis):
    count = lax.axis_size(axis)
    copies = jnp.broadcast_to(values[None], (count,) + values.shape)
    return lax.all_to_all(copies, axis, split_axis=0, concat_axis=0, tiled=True)


def exchange(cells, axis, split_axis):
    count = lax.axis_size(axis)
    here = lax.axis_index(axis)
    width = cells.shape[split_axis] // count
    pieces = []
    for shift in range(count):
        piece = lax.dynamic_slice_in_dim(cells, ((here + shift) % count) * width, width, axis=split_axis)
        if shift:
            piece = lax.ppermute(piece, axis, [(j, (j + shift) % count) for j in range(count)])
        pieces.append(piece)
    return pieces


def in_source_order(pieces, axis, concat_axis):
    count = len(pieces)
    here = lax.axis_index(axis)
    stacked = jnp.stack(pieces)
    ordered = [lax.dynamic_index_in_dim(stacked, (here - source) % count, 0, keepdims=False) for source in range(count)]
    return jnp.concatenate(ordered, axis=concat_axis)


def shifted_tables(count, local_angles, axis):
    here = lax.axis_index(axis)
    blocks = count // local_angles
    wave_index = jnp.arange(count, dtype=jnp.int32) - count // 2
    position = jnp.arange(count, dtype=jnp.int32)
    angle_index = ((here - position // local_angles) % blocks) * local_angles + position % local_angles
    residues = wave_index[:, None] * angle_index[None, :] % count
    phases = 2.0 * math.pi * residues.astype(jnp.float32) / count
    scaling = 1.0 / math.sqrt(count)
    return (
        (jnp.cos(phases) * scaling).astype(jnp.bfloat16),
        (jnp.sin(phases) * scaling).astype(jnp.bfloat16),
    )


def dft_kernel(*refs, count, weighted):
    table_ref = refs[0]
    piece_refs = refs[1:1 + count]
    rest = refs[1 + count:]
    out_ref = rest[-1]
    width = piece_refs[0].shape[1]
    lane = lax.broadcasted_iota(jnp.int32, (1, width), 1) % 128
    low = lane < 64
    packed = piece_refs[0].shape[0] % 16 == 0
    rows = []
    for piece_ref in piece_refs:
        x = piece_ref[...]
        if not packed:
            x = x.astype(jnp.float32)
        swapped = jnp.where(low, pltpu.roll(x, width - 64, 1), -pltpu.roll(x, 64, 1))
        rows.append(x)
        rows.append(swapped)
    stacked = jnp.concatenate(rows, axis=0).astype(jnp.bfloat16)
    acc = jnp.dot(table_ref[...], stacked, preferred_element_type=jnp.float32)
    modes = acc.astype(jnp.bfloat16)
    if weighted:
        modes = (modes.astype(jnp.float32) * rest[0][...]).astype(jnp.bfloat16)
    out_ref[...] = modes

def dft(table, pieces, weight=None):
    count = len(pieces)
    angles, total = pieces[0].shape
    waves = table.shape[0]
    block = math.gcd(total, 4096)
    grid = (total // block,)
    in_specs = [pl.BlockSpec((waves, table.shape[1]), lambda j: (0, 0))]
    in_specs += [pl.BlockSpec((angles, block), lambda j: (0, j)) for _ in pieces]
    args = [table, *pieces]
    if weight is not None:
        in_specs.append(pl.BlockSpec((1, block), lambda j: (0, j)))
        args.append(weight)
    return pl.pallas_call(
        functools.partial(dft_kernel, count=count, weighted=weight is not None),
        grid=grid,
        in_specs=in_specs,
        out_specs=pl.BlockSpec((waves, block), lambda j: (0, j)),
        out_shape=jax.ShapeDtypeStruct((waves, total), jnp.bfloat16),
    )(*args)


def piece_tables(count, local_angles, axis):
    here = lax.axis_index(axis)
    blocks = count // local_angles
    wave_index = jnp.arange(count, dtype=jnp.int32) - count // 2
    scaling = 1.0 / math.sqrt(count)
    columns = []
    for shift in range(blocks):
        angle_index = ((here - shift) % blocks) * local_angles + jnp.arange(local_angles, dtype=jnp.int32)
        residues = wave_index[:, None] * angle_index[None, :] % count
        phases = 2.0 * math.pi * residues.astype(jnp.float32) / count
        columns.append((jnp.cos(phases) * scaling).astype(jnp.bfloat16))
        columns.append((jnp.sin(phases) * scaling).astype(jnp.bfloat16))
    return jnp.concatenate(columns, axis=1)


def dft_tables(count):
    wave_index = jnp.arange(count, dtype=jnp.int32) - count // 2
    angle_index = jnp.arange(count, dtype=jnp.int32)
    residues = wave_index[:, None] * angle_index[None, :] % count
    phases = 2.0 * math.pi * residues.astype(jnp.float32) / count
    scaling = 1.0 / math.sqrt(count)
    return (
        (jnp.cos(phases) * scaling).astype(jnp.bfloat16),
        (jnp.sin(phases) * scaling).astype(jnp.bfloat16),
    )


def combine_parts(cos_part, sin_part, half):
    real_part = cos_part[..., :half] + sin_part[..., half:]
    imag_part = cos_part[..., half:] - sin_part[..., :half]
    return jnp.concatenate([real_part, imag_part], axis=-1).astype(jnp.bfloat16)


def complex_blocks(product, half):
    upper_rows = product[..., :half, :]
    lower_rows = product[..., half:, :]
    pieces = []
    for offset in (0, 2 * half):
        pieces.append(
            upper_rows[..., offset : offset + half]
            + lower_rows[..., offset + half : offset + 2 * half]
        )
        pieces.append(
            upper_rows[..., offset + half : offset + 2 * half]
            - lower_rows[..., offset : offset + half]
        )
    return jnp.concatenate(pieces, axis=-1)


def local(direct_snapshots, adjoint_snapshots, quad_weight, mean_velocity, diffusivity):
    local_angles, axial_cells, radial_cells, columns = direct_snapshots.shape
    snap_count = columns // 2
    total_angles = local_angles * lax.axis_size("ka")
    table = piece_tables(total_angles, local_angles, "ka")
    first_wave = lax.axis_index("ka") * local_angles
    band_count = lax.axis_size("ka")
    band = radial_cells // band_count
    lanes = axial_cells * band * columns
    norm_factor = 1.0 / math.sqrt(axial_cells * lax.axis_size("gx") * radial_cells)
    band_weight = lax.dynamic_slice_in_dim(
        quad_weight * norm_factor, lax.axis_index("ka") * band, band, axis=1
    )
    lane_weight = jnp.broadcast_to(band_weight[:, :, None], (axial_cells, band, columns)).reshape(1, lanes)

    def transform_all(snapshots, weight=None):
        pieces = [piece.reshape(local_angles, lanes) for piece in exchange(snapshots, "ka", 2)]
        modes = dft(table, pieces, weight)
        return modes.reshape(total_angles, axial_cells, band, columns)

    direct_modes = in_source_order(exchange(transform_all(direct_snapshots), "ka", 0), "ka", 2)
    weighted = in_source_order(
        exchange(transform_all(adjoint_snapshots, lane_weight), "ka", 0), "ka", 2
    )
    padded = padded_2(direct_modes, (("gx", 1),), 1)
    field_f32 = direct_modes.astype(jnp.float32)
    forward = padded[:, 2:].astype(jnp.float32)
    behind = padded[:, :-2].astype(jnp.float32)
    radial_pad = jnp.pad(field_f32, ((0, 0), (0, 0), (1, 1), (0, 0)))
    outward = radial_pad[:, :, 2:]
    inward = radial_pad[:, :, :-2]
    radius = 0.25 + (jnp.arange(radial_cells, dtype=jnp.float32) + 0.5) / radial_cells
    wavenumber = (
        first_wave + jnp.arange(local_angles, dtype=jnp.int32) - total_angles // 2
    ).astype(jnp.float32) / total_angles
    azimuthal = (wavenumber[:, None] / radius[None, :]) ** 2
    velocity = mean_velocity[None, :, :, None]
    diffusion = diffusivity[None, :, :, None]
    image = (
        -velocity * (forward - behind) * 0.5
        + diffusion
        * (
            forward
            + behind
            + outward
            + inward
            - 4.0 * field_f32
            - azimuthal[:, None, :, None] * field_f32
        )
    ).astype(jnp.bfloat16)
    right_side = jnp.concatenate([direct_modes, image], axis=-1)
    product = jnp.einsum(
        "kpa,kpb->kab",
        weighted.reshape(local_angles, -1, columns),
        right_side.reshape(local_angles, -1, 2 * columns),
        preferred_element_type=jnp.float32,
    )
    gram_terms = complex_blocks(product, snap_count).reshape(local_angles * snap_count, 2 * columns)
    row_count = gram_terms.shape[0] // lax.axis_size("gx")
    row_index = lax.axis_index("gx") * row_count + jnp.arange(row_count, dtype=jnp.int32)
    owner = row_index // snap_count
    selector = (owner[:, None] == jnp.arange(local_angles, dtype=jnp.int32)[None, :]).astype(
        jnp.float32
    )
    shares = gram_terms.astype(jnp.bfloat16).reshape(lax.axis_size("gx"), row_count, 2 * columns)
    own_rows = sum(piece.astype(jnp.float32) for piece in exchange(shares, "gx", 0))[0]
    row_energy = jnp.sum(own_rows[:, :columns] ** 2, axis=1)
    partial_energy = jnp.sum(selector * row_energy[:, None], axis=0)
    copies = jnp.broadcast_to(partial_energy, (lax.axis_size("gx"), local_angles))
    energy = sum(exchange(copies, "gx", 0))[0]
    mean_sq = energy / (2.0 * snap_count * snap_count)
    row_scale = jnp.sum(selector * lax.rsqrt(mean_sq + epsilon)[None, :], axis=1)
    hankel_gram = own_rows[:, :columns] * row_scale[:, None]
    reduced_operator = own_rows[:, columns:] * row_scale[:, None]
    hankel_norm = jnp.sqrt(mean_sq)
    return (hankel_gram, reduced_operator, hankel_norm)


def solution(mesh):
    placed = (
        P("ka", "gx", None, None),
        P("ka", "gx", None, None),
        P("gx", None),
        P("gx", None),
        P("gx", None),
    )
    return jax.shard_map(
        local,
        mesh=mesh,
        in_specs=placed,
        out_specs=(P(("ka", "gx"), None), P(("ka", "gx"), None), P("ka")),
        check_vma=False,
    )
```

```python
import functools
import math

import jax
import jax.numpy as jnp
from jax import lax
from jax.experimental import pallas as pl
from jax.experimental.pallas import tpu as pltpu
from jax.sharding import PartitionSpec as P

epsilon = 1e-06


def padded_2(cells, sides, width):
    for axis, dim in sides:
        count = lax.axis_size(axis)
        ends = count - 1
        head = lax.slice_in_dim(cells, 0, width, axis=dim)
        tail = lax.slice_in_dim(cells, cells.shape[dim] - width, cells.shape[dim], axis=dim)
        cells = jnp.concatenate(
            [
                lax.ppermute(tail, axis, [(i, (i + 1) % count) for i in range(ends)]),
                cells,
                lax.ppermute(head, axis, [((i + 1) % count, i) for i in range(ends)]),
            ],
            axis=dim,
        )
    return cells


def gather_small(values, axis):
    count = lax.axis_size(axis)
    copies = jnp.broadcast_to(values[None], (count,) + values.shape)
    return lax.all_to_all(copies, axis, split_axis=0, concat_axis=0, tiled=True)


def exchange(cells, axis, split_axis):
    count = lax.axis_size(axis)
    here = lax.axis_index(axis)
    width = cells.shape[split_axis] // count
    pieces = []
    for shift in range(count):
        piece = lax.dynamic_slice_in_dim(cells, ((here + shift) % count) * width, width, axis=split_axis)
        if shift:
            piece = lax.ppermute(piece, axis, [(j, (j + shift) % count) for j in range(count)])
        pieces.append(piece)
    return pieces


def in_source_order(pieces, axis, concat_axis):
    count = len(pieces)
    here = lax.axis_index(axis)
    stacked = jnp.stack(pieces)
    ordered = [lax.dynamic_index_in_dim(stacked, (here - source) % count, 0, keepdims=False) for source in range(count)]
    return jnp.concatenate(ordered, axis=concat_axis)


def shifted_tables(count, local_angles, axis):
    here = lax.axis_index(axis)
    blocks = count // local_angles
    wave_index = jnp.arange(count, dtype=jnp.int32) - count // 2
    position = jnp.arange(count, dtype=jnp.int32)
    angle_index = ((here - position // local_angles) % blocks) * local_angles + position % local_angles
    residues = wave_index[:, None] * angle_index[None, :] % count
    phases = 2.0 * math.pi * residues.astype(jnp.float32) / count
    scaling = 1.0 / math.sqrt(count)
    return (
        (jnp.cos(phases) * scaling).astype(jnp.bfloat16),
        (jnp.sin(phases) * scaling).astype(jnp.bfloat16),
    )


def dft_kernel(*refs, count, weighted):
    table_ref = refs[0]
    piece_refs = refs[1:1 + count]
    rest = refs[1 + count:]
    out_ref = rest[-1]
    width = piece_refs[0].shape[1]
    lane = lax.broadcasted_iota(jnp.int32, (1, width), 1) % 128
    low = lane < 64
    packed = piece_refs[0].shape[0] % 16 == 0
    rows = []
    for piece_ref in piece_refs:
        x = piece_ref[...]
        if not packed:
            x = x.astype(jnp.float32)
        swapped = jnp.where(low, pltpu.roll(x, width - 64, 1), -pltpu.roll(x, 64, 1))
        rows.append(x)
        rows.append(swapped)
    stacked = jnp.concatenate(rows, axis=0).astype(jnp.bfloat16)
    acc = jnp.dot(table_ref[...], stacked, preferred_element_type=jnp.float32)
    modes = acc.astype(jnp.bfloat16)
    if weighted:
        modes = (modes.astype(jnp.float32) * rest[0][...]).astype(jnp.bfloat16)
    out_ref[...] = modes

def dft(table, pieces, weight=None):
    count = len(pieces)
    angles, total = pieces[0].shape
    waves = table.shape[0]
    block = math.gcd(total, 4096)
    grid = (total // block,)
    in_specs = [pl.BlockSpec((waves, table.shape[1]), lambda j: (0, 0))]
    in_specs += [pl.BlockSpec((angles, block), lambda j: (0, j)) for _ in pieces]
    args = [table, *pieces]
    if weight is not None:
        in_specs.append(pl.BlockSpec((1, block), lambda j: (0, j)))
        args.append(weight)
    return pl.pallas_call(
        functools.partial(dft_kernel, count=count, weighted=weight is not None),
        grid=grid,
        in_specs=in_specs,
        out_specs=pl.BlockSpec((waves, block), lambda j: (0, j)),
        out_shape=jax.ShapeDtypeStruct((waves, total), jnp.bfloat16),
    )(*args)


def piece_tables(count, local_angles, axis):
    here = lax.axis_index(axis)
    blocks = count // local_angles
    wave_index = jnp.arange(count, dtype=jnp.int32) - count // 2
    scaling = 1.0 / math.sqrt(count)
    columns = []
    for shift in range(blocks):
        angle_index = ((here - shift) % blocks) * local_angles + jnp.arange(local_angles, dtype=jnp.int32)
        residues = wave_index[:, None] * angle_index[None, :] % count
        phases = 2.0 * math.pi * residues.astype(jnp.float32) / count
        columns.append((jnp.cos(phases) * scaling).astype(jnp.bfloat16))
        columns.append((jnp.sin(phases) * scaling).astype(jnp.bfloat16))
    return jnp.concatenate(columns, axis=1)


def dft_tables(count):
    wave_index = jnp.arange(count, dtype=jnp.int32) - count // 2
    angle_index = jnp.arange(count, dtype=jnp.int32)
    residues = wave_index[:, None] * angle_index[None, :] % count
    phases = 2.0 * math.pi * residues.astype(jnp.float32) / count
    scaling = 1.0 / math.sqrt(count)
    return (
        (jnp.cos(phases) * scaling).astype(jnp.bfloat16),
        (jnp.sin(phases) * scaling).astype(jnp.bfloat16),
    )


def combine_parts(cos_part, sin_part, half):
    real_part = cos_part[..., :half] + sin_part[..., half:]
    imag_part = cos_part[..., half:] - sin_part[..., :half]
    return jnp.concatenate([real_part, imag_part], axis=-1).astype(jnp.bfloat16)


def complex_blocks(product, half):
    upper_rows = product[..., :half, :]
    lower_rows = product[..., half:, :]
    pieces = []
    for offset in (0, 2 * half):
        pieces.append(
            upper_rows[..., offset : offset + half]
            + lower_rows[..., offset + half : offset + 2 * half]
        )
        pieces.append(
            upper_rows[..., offset + half : offset + 2 * half]
            - lower_rows[..., offset : offset + half]
        )
    return jnp.concatenate(pieces, axis=-1)


def local(direct_snapshots, adjoint_snapshots, quad_weight, mean_velocity, diffusivity):
    local_angles, axial_cells, radial_cells, columns = direct_snapshots.shape
    snap_count = columns // 2
    total_angles = local_angles * lax.axis_size("ka")
    table = piece_tables(total_angles, local_angles, "ka")
    first_wave = lax.axis_index("ka") * local_angles
    band_count = lax.axis_size("ka")
    band = radial_cells // band_count
    lanes = axial_cells * band * columns
    norm_factor = 1.0 / math.sqrt(axial_cells * lax.axis_size("gx") * radial_cells)
    band_weight = lax.dynamic_slice_in_dim(
        quad_weight * norm_factor, lax.axis_index("ka") * band, band, axis=1
    )
    lane_weight = jnp.broadcast_to(band_weight[:, :, None], (axial_cells, band, columns)).reshape(1, lanes)

    def transform_all(snapshots, weight=None):
        pieces = [piece.reshape(local_angles, lanes) for piece in exchange(snapshots, "ka", 2)]
        modes = dft(table, pieces, weight)
        return modes.reshape(total_angles, axial_cells, band, columns)

    direct_modes = in_source_order(exchange(transform_all(direct_snapshots), "ka", 0), "ka", 2)
    weighted_all = transform_all(adjoint_snapshots, lane_weight)
    direct_modes, weighted_all = lax.optimization_barrier((direct_modes, weighted_all))
    weighted = in_source_order(exchange(weighted_all, "ka", 0), "ka", 2)
    padded = padded_2(direct_modes, (("gx", 1),), 1)
    field_f32 = direct_modes.astype(jnp.float32)
    forward = padded[:, 2:].astype(jnp.float32)
    behind = padded[:, :-2].astype(jnp.float32)
    radial_pad = jnp.pad(field_f32, ((0, 0), (0, 0), (1, 1), (0, 0)))
    outward = radial_pad[:, :, 2:]
    inward = radial_pad[:, :, :-2]
    radius = 0.25 + (jnp.arange(radial_cells, dtype=jnp.float32) + 0.5) / radial_cells
    wavenumber = (
        first_wave + jnp.arange(local_angles, dtype=jnp.int32) - total_angles // 2
    ).astype(jnp.float32) / total_angles
    azimuthal = (wavenumber[:, None] / radius[None, :]) ** 2
    velocity = mean_velocity[None, :, :, None]
    diffusion = diffusivity[None, :, :, None]
    image = (
        -velocity * (forward - behind) * 0.5
        + diffusion
        * (
            forward
            + behind
            + outward
            + inward
            - 4.0 * field_f32
            - azimuthal[:, None, :, None] * field_f32
        )
    ).astype(jnp.bfloat16)
    right_side = jnp.concatenate([direct_modes, image], axis=-1)
    product = jnp.einsum(
        "kpa,kpb->kab",
        weighted.reshape(local_angles, -1, columns),
        right_side.reshape(local_angles, -1, 2 * columns),
        preferred_element_type=jnp.float32,
    )
    gram_terms = complex_blocks(product, snap_count).reshape(local_angles * snap_count, 2 * columns)
    row_count = gram_terms.shape[0] // lax.axis_size("gx")
    row_index = lax.axis_index("gx") * row_count + jnp.arange(row_count, dtype=jnp.int32)
    owner = row_index // snap_count
    selector = (owner[:, None] == jnp.arange(local_angles, dtype=jnp.int32)[None, :]).astype(
        jnp.float32
    )
    shares = gram_terms.astype(jnp.bfloat16).reshape(lax.axis_size("gx"), row_count, 2 * columns)
    own_rows = sum(piece.astype(jnp.float32) for piece in exchange(shares, "gx", 0))[0]
    row_energy = jnp.sum(own_rows[:, :columns] ** 2, axis=1)
    energy = jnp.sum(gather_small(jnp.sum(selector * row_energy[:, None], axis=0), "gx"), axis=0)
    mean_sq = energy / (2.0 * snap_count * snap_count)
    row_scale = jnp.sum(selector * lax.rsqrt(mean_sq + epsilon)[None, :], axis=1)
    hankel_gram = own_rows[:, :columns] * row_scale[:, None]
    reduced_operator = own_rows[:, columns:] * row_scale[:, None]
    hankel_norm = jnp.sqrt(mean_sq)
    return (hankel_gram, reduced_operator, hankel_norm)


def solution(mesh):
    placed = (
        P("ka", "gx", None, None),
        P("ka", "gx", None, None),
        P("gx", None),
        P("gx", None),
        P("gx", None),
    )
    return jax.shard_map(
        local,
        mesh=mesh,
        in_specs=placed,
        out_specs=(P(("ka", "gx"), None), P(("ka", "gx"), None), P("ka")),
        check_vma=False,
    )
```

```python
import functools
import math

import jax
import jax.numpy as jnp
from jax import lax
from jax.experimental import pallas as pl
from jax.experimental.pallas import tpu as pltpu
from jax.sharding import PartitionSpec as P

epsilon = 1e-06


def padded_2(cells, sides, width):
    for axis, dim in sides:
        count = lax.axis_size(axis)
        ends = count - 1
        head = lax.slice_in_dim(cells, 0, width, axis=dim)
        tail = lax.slice_in_dim(cells, cells.shape[dim] - width, cells.shape[dim], axis=dim)
        cells = jnp.concatenate(
            [
                lax.ppermute(tail, axis, [(i, (i + 1) % count) for i in range(ends)]),
                cells,
                lax.ppermute(head, axis, [((i + 1) % count, i) for i in range(ends)]),
            ],
            axis=dim,
        )
    return cells


def gather_small(values, axis):
    count = lax.axis_size(axis)
    copies = jnp.broadcast_to(values[None], (count,) + values.shape)
    return lax.all_to_all(copies, axis, split_axis=0, concat_axis=0, tiled=True)


def exchange(cells, axis, split_axis, far_first=False):
    count = lax.axis_size(axis)
    here = lax.axis_index(axis)
    width = cells.shape[split_axis] // count
    shifts = list(range(count))
    if far_first:
        shifts = [0] + sorted(range(1, count), key=lambda shift: -min(shift, count - shift))
    pieces = []
    for shift in shifts:
        piece = lax.dynamic_slice_in_dim(cells, ((here + shift) % count) * width, width, axis=split_axis)
        if shift:
            piece = lax.ppermute(piece, axis, [(j, (j + shift) % count) for j in range(count)])
        pieces.append(piece)
    return pieces


def in_source_order(pieces, axis, concat_axis):
    count = len(pieces)
    here = lax.axis_index(axis)
    stacked = jnp.stack(pieces)
    ordered = [lax.dynamic_index_in_dim(stacked, (here - source) % count, 0, keepdims=False) for source in range(count)]
    return jnp.concatenate(ordered, axis=concat_axis)


def shifted_tables(count, local_angles, axis):
    here = lax.axis_index(axis)
    blocks = count // local_angles
    wave_index = jnp.arange(count, dtype=jnp.int32) - count // 2
    position = jnp.arange(count, dtype=jnp.int32)
    angle_index = ((here - position // local_angles) % blocks) * local_angles + position % local_angles
    residues = wave_index[:, None] * angle_index[None, :] % count
    phases = 2.0 * math.pi * residues.astype(jnp.float32) / count
    scaling = 1.0 / math.sqrt(count)
    return (
        (jnp.cos(phases) * scaling).astype(jnp.bfloat16),
        (jnp.sin(phases) * scaling).astype(jnp.bfloat16),
    )


def dft_kernel(*refs, count, weighted):
    table_ref = refs[0]
    piece_refs = refs[1:1 + count]
    rest = refs[1 + count:]
    out_ref = rest[-1]
    width = piece_refs[0].shape[1]
    lane = lax.broadcasted_iota(jnp.int32, (1, width), 1) % 128
    low = lane < 64
    packed = piece_refs[0].shape[0] % 16 == 0
    rows = []
    for piece_ref in piece_refs:
        x = piece_ref[...]
        if not packed:
            x = x.astype(jnp.float32)
        swapped = jnp.where(low, pltpu.roll(x, width - 64, 1), -pltpu.roll(x, 64, 1))
        rows.append(x)
        rows.append(swapped)
    stacked = jnp.concatenate(rows, axis=0).astype(jnp.bfloat16)
    acc = jnp.dot(table_ref[...], stacked, preferred_element_type=jnp.float32)
    modes = acc.astype(jnp.bfloat16)
    if weighted:
        modes = (modes.astype(jnp.float32) * rest[0][...]).astype(jnp.bfloat16)
    out_ref[...] = modes

def dft(table, pieces, weight=None):
    count = len(pieces)
    angles, total = pieces[0].shape
    waves = table.shape[0]
    block = math.gcd(total, 4096)
    grid = (total // block,)
    in_specs = [pl.BlockSpec((waves, table.shape[1]), lambda j: (0, 0))]
    in_specs += [pl.BlockSpec((angles, block), lambda j: (0, j)) for _ in pieces]
    args = [table, *pieces]
    if weight is not None:
        in_specs.append(pl.BlockSpec((1, block), lambda j: (0, j)))
        args.append(weight)
    return pl.pallas_call(
        functools.partial(dft_kernel, count=count, weighted=weight is not None),
        grid=grid,
        in_specs=in_specs,
        out_specs=pl.BlockSpec((waves, block), lambda j: (0, j)),
        out_shape=jax.ShapeDtypeStruct((waves, total), jnp.bfloat16),
    )(*args)


def piece_tables(count, local_angles, axis):
    here = lax.axis_index(axis)
    blocks = count // local_angles
    wave_index = jnp.arange(count, dtype=jnp.int32) - count // 2
    scaling = 1.0 / math.sqrt(count)
    columns = []
    for shift in range(blocks):
        angle_index = ((here - shift) % blocks) * local_angles + jnp.arange(local_angles, dtype=jnp.int32)
        residues = wave_index[:, None] * angle_index[None, :] % count
        phases = 2.0 * math.pi * residues.astype(jnp.float32) / count
        columns.append((jnp.cos(phases) * scaling).astype(jnp.bfloat16))
        columns.append((jnp.sin(phases) * scaling).astype(jnp.bfloat16))
    return jnp.concatenate(columns, axis=1)


def dft_tables(count):
    wave_index = jnp.arange(count, dtype=jnp.int32) - count // 2
    angle_index = jnp.arange(count, dtype=jnp.int32)
    residues = wave_index[:, None] * angle_index[None, :] % count
    phases = 2.0 * math.pi * residues.astype(jnp.float32) / count
    scaling = 1.0 / math.sqrt(count)
    return (
        (jnp.cos(phases) * scaling).astype(jnp.bfloat16),
        (jnp.sin(phases) * scaling).astype(jnp.bfloat16),
    )


def combine_parts(cos_part, sin_part, half):
    real_part = cos_part[..., :half] + sin_part[..., half:]
    imag_part = cos_part[..., half:] - sin_part[..., :half]
    return jnp.concatenate([real_part, imag_part], axis=-1).astype(jnp.bfloat16)


def complex_blocks(product, half):
    upper_rows = product[..., :half, :]
    lower_rows = product[..., half:, :]
    pieces = []
    for offset in (0, 2 * half):
        pieces.append(
            upper_rows[..., offset : offset + half]
            + lower_rows[..., offset + half : offset + 2 * half]
        )
        pieces.append(
            upper_rows[..., offset + half : offset + 2 * half]
            - lower_rows[..., offset : offset + half]
        )
    return jnp.concatenate(pieces, axis=-1)


def local(direct_snapshots, adjoint_snapshots, quad_weight, mean_velocity, diffusivity):
    local_angles, axial_cells, radial_cells, columns = direct_snapshots.shape
    snap_count = columns // 2
    total_angles = local_angles * lax.axis_size("ka")
    table = piece_tables(total_angles, local_angles, "ka")
    first_wave = lax.axis_index("ka") * local_angles
    band_count = lax.axis_size("ka")
    band = radial_cells // band_count
    lanes = axial_cells * band * columns
    norm_factor = 1.0 / math.sqrt(axial_cells * lax.axis_size("gx") * radial_cells)
    band_weight = lax.dynamic_slice_in_dim(
        quad_weight * norm_factor, lax.axis_index("ka") * band, band, axis=1
    )
    lane_weight = jnp.broadcast_to(band_weight[:, :, None], (axial_cells, band, columns)).reshape(1, lanes)

    def transform_all(snapshots, weight=None):
        pieces = [piece.reshape(local_angles, lanes) for piece in exchange(snapshots, "ka", 2)]
        modes = dft(table, pieces, weight)
        return modes.reshape(total_angles, axial_cells, band, columns)

    direct_modes = in_source_order(exchange(transform_all(direct_snapshots), "ka", 0), "ka", 2)
    weighted = in_source_order(
        exchange(transform_all(adjoint_snapshots, lane_weight), "ka", 0), "ka", 2
    )
    padded = padded_2(direct_modes, (("gx", 1),), 1)
    field_f32 = direct_modes.astype(jnp.float32)
    forward = padded[:, 2:].astype(jnp.float32)
    behind = padded[:, :-2].astype(jnp.float32)
    radial_pad = jnp.pad(field_f32, ((0, 0), (0, 0), (1, 1), (0, 0)))
    outward = radial_pad[:, :, 2:]
    inward = radial_pad[:, :, :-2]
    radius = 0.25 + (jnp.arange(radial_cells, dtype=jnp.float32) + 0.5) / radial_cells
    wavenumber = (
        first_wave + jnp.arange(local_angles, dtype=jnp.int32) - total_angles // 2
    ).astype(jnp.float32) / total_angles
    azimuthal = (wavenumber[:, None] / radius[None, :]) ** 2
    velocity = mean_velocity[None, :, :, None]
    diffusion = diffusivity[None, :, :, None]
    image = (
        -velocity * (forward - behind) * 0.5
        + diffusion
        * (
            forward
            + behind
            + outward
            + inward
            - 4.0 * field_f32
            - azimuthal[:, None, :, None] * field_f32
        )
    ).astype(jnp.bfloat16)
    right_side = jnp.concatenate([direct_modes, image], axis=-1)
    product = jnp.einsum(
        "kpa,kpb->kab",
        weighted.reshape(local_angles, -1, columns),
        right_side.reshape(local_angles, -1, 2 * columns),
        preferred_element_type=jnp.float32,
    )
    gram_terms = complex_blocks(product, snap_count).reshape(local_angles * snap_count, 2 * columns)
    row_count = gram_terms.shape[0] // lax.axis_size("gx")
    row_index = lax.axis_index("gx") * row_count + jnp.arange(row_count, dtype=jnp.int32)
    owner = row_index // snap_count
    selector = (owner[:, None] == jnp.arange(local_angles, dtype=jnp.int32)[None, :]).astype(
        jnp.float32
    )
    shares = gram_terms.astype(jnp.bfloat16).reshape(lax.axis_size("gx"), row_count, 2 * columns)
    own_rows = sum(piece.astype(jnp.float32) for piece in exchange(shares, "gx", 0, True))[0]
    row_energy = jnp.sum(own_rows[:, :columns] ** 2, axis=1)
    energy = jnp.sum(gather_small(jnp.sum(selector * row_energy[:, None], axis=0), "gx"), axis=0)
    mean_sq = energy / (2.0 * snap_count * snap_count)
    row_scale = jnp.sum(selector * lax.rsqrt(mean_sq + epsilon)[None, :], axis=1)
    hankel_gram = own_rows[:, :columns] * row_scale[:, None]
    reduced_operator = own_rows[:, columns:] * row_scale[:, None]
    hankel_norm = jnp.sqrt(mean_sq)
    return (hankel_gram, reduced_operator, hankel_norm)


def solution(mesh):
    placed = (
        P("ka", "gx", None, None),
        P("ka", "gx", None, None),
        P("gx", None),
        P("gx", None),
        P("gx", None),
    )
    return jax.shard_map(
        local,
        mesh=mesh,
        in_specs=placed,
        out_specs=(P(("ka", "gx"), None), P(("ka", "gx"), None), P("ka")),
        check_vma=False,
    )
```

```python
import functools
import math

import jax
import jax.numpy as jnp
from jax import lax
from jax.experimental import pallas as pl
from jax.experimental.pallas import tpu as pltpu
from jax.sharding import PartitionSpec as P

epsilon = 1e-06


def padded_2(cells, sides, width):
    for axis, dim in sides:
        count = lax.axis_size(axis)
        ends = count - 1
        head = lax.slice_in_dim(cells, 0, width, axis=dim)
        tail = lax.slice_in_dim(cells, cells.shape[dim] - width, cells.shape[dim], axis=dim)
        cells = jnp.concatenate(
            [
                lax.ppermute(tail, axis, [(i, (i + 1) % count) for i in range(ends)]),
                cells,
                lax.ppermute(head, axis, [((i + 1) % count, i) for i in range(ends)]),
            ],
            axis=dim,
        )
    return cells


def gather_small(values, axis):
    count = lax.axis_size(axis)
    copies = jnp.broadcast_to(values[None], (count,) + values.shape)
    return lax.all_to_all(copies, axis, split_axis=0, concat_axis=0, tiled=True)


def exchange(cells, axis, split_axis, far_first=False):
    count = lax.axis_size(axis)
    here = lax.axis_index(axis)
    width = cells.shape[split_axis] // count
    shifts = list(range(count))
    if far_first:
        shifts = [0] + sorted(range(1, count), key=lambda shift: -min(shift, count - shift))
    pieces = [None] * count
    for shift in shifts:
        piece = lax.dynamic_slice_in_dim(cells, ((here + shift) % count) * width, width, axis=split_axis)
        if shift:
            piece = lax.ppermute(piece, axis, [(j, (j + shift) % count) for j in range(count)])
        pieces[shift] = piece
    return pieces


def in_source_order(pieces, axis, concat_axis):
    count = len(pieces)
    here = lax.axis_index(axis)
    stacked = jnp.stack(pieces)
    ordered = [lax.dynamic_index_in_dim(stacked, (here - source) % count, 0, keepdims=False) for source in range(count)]
    return jnp.concatenate(ordered, axis=concat_axis)


def shifted_tables(count, local_angles, axis):
    here = lax.axis_index(axis)
    blocks = count // local_angles
    wave_index = jnp.arange(count, dtype=jnp.int32) - count // 2
    position = jnp.arange(count, dtype=jnp.int32)
    angle_index = ((here - position // local_angles) % blocks) * local_angles + position % local_angles
    residues = wave_index[:, None] * angle_index[None, :] % count
    phases = 2.0 * math.pi * residues.astype(jnp.float32) / count
    scaling = 1.0 / math.sqrt(count)
    return (
        (jnp.cos(phases) * scaling).astype(jnp.bfloat16),
        (jnp.sin(phases) * scaling).astype(jnp.bfloat16),
    )


def dft_kernel(*refs, count, weighted):
    table_ref = refs[0]
    piece_refs = refs[1:1 + count]
    rest = refs[1 + count:]
    out_ref = rest[-1]
    width = piece_refs[0].shape[1]
    lane = lax.broadcasted_iota(jnp.int32, (1, width), 1) % 128
    low = lane < 64
    packed = piece_refs[0].shape[0] % 16 == 0
    rows = []
    for piece_ref in piece_refs:
        x = piece_ref[...]
        if not packed:
            x = x.astype(jnp.float32)
        swapped = jnp.where(low, pltpu.roll(x, width - 64, 1), -pltpu.roll(x, 64, 1))
        rows.append(x)
        rows.append(swapped)
    stacked = jnp.concatenate(rows, axis=0).astype(jnp.bfloat16)
    acc = jnp.dot(table_ref[...], stacked, preferred_element_type=jnp.float32)
    modes = acc.astype(jnp.bfloat16)
    if weighted:
        modes = (modes.astype(jnp.float32) * rest[0][...]).astype(jnp.bfloat16)
    out_ref[...] = modes

def dft(table, pieces, weight=None):
    count = len(pieces)
    angles, total = pieces[0].shape
    waves = table.shape[0]
    block = math.gcd(total, 4096)
    grid = (total // block,)
    in_specs = [pl.BlockSpec((waves, table.shape[1]), lambda j: (0, 0))]
    in_specs += [pl.BlockSpec((angles, block), lambda j: (0, j)) for _ in pieces]
    args = [table, *pieces]
    if weight is not None:
        in_specs.append(pl.BlockSpec((1, block), lambda j: (0, j)))
        args.append(weight)
    return pl.pallas_call(
        functools.partial(dft_kernel, count=count, weighted=weight is not None),
        grid=grid,
        in_specs=in_specs,
        out_specs=pl.BlockSpec((waves, block), lambda j: (0, j)),
        out_shape=jax.ShapeDtypeStruct((waves, total), jnp.bfloat16),
    )(*args)


def piece_tables(count, local_angles, axis):
    here = lax.axis_index(axis)
    blocks = count // local_angles
    wave_index = jnp.arange(count, dtype=jnp.int32) - count // 2
    scaling = 1.0 / math.sqrt(count)
    columns = []
    for shift in range(blocks):
        angle_index = ((here - shift) % blocks) * local_angles + jnp.arange(local_angles, dtype=jnp.int32)
        residues = wave_index[:, None] * angle_index[None, :] % count
        phases = 2.0 * math.pi * residues.astype(jnp.float32) / count
        columns.append((jnp.cos(phases) * scaling).astype(jnp.bfloat16))
        columns.append((jnp.sin(phases) * scaling).astype(jnp.bfloat16))
    return jnp.concatenate(columns, axis=1)


def dft_tables(count):
    wave_index = jnp.arange(count, dtype=jnp.int32) - count // 2
    angle_index = jnp.arange(count, dtype=jnp.int32)
    residues = wave_index[:, None] * angle_index[None, :] % count
    phases = 2.0 * math.pi * residues.astype(jnp.float32) / count
    scaling = 1.0 / math.sqrt(count)
    return (
        (jnp.cos(phases) * scaling).astype(jnp.bfloat16),
        (jnp.sin(phases) * scaling).astype(jnp.bfloat16),
    )


def combine_parts(cos_part, sin_part, half):
    real_part = cos_part[..., :half] + sin_part[..., half:]
    imag_part = cos_part[..., half:] - sin_part[..., :half]
    return jnp.concatenate([real_part, imag_part], axis=-1).astype(jnp.bfloat16)


def complex_blocks(product, half):
    upper_rows = product[..., :half, :]
    lower_rows = product[..., half:, :]
    pieces = []
    for offset in (0, 2 * half):
        pieces.append(
            upper_rows[..., offset : offset + half]
            + lower_rows[..., offset + half : offset + 2 * half]
        )
        pieces.append(
            upper_rows[..., offset + half : offset + 2 * half]
            - lower_rows[..., offset : offset + half]
        )
    return jnp.concatenate(pieces, axis=-1)


def local(direct_snapshots, adjoint_snapshots, quad_weight, mean_velocity, diffusivity):
    local_angles, axial_cells, radial_cells, columns = direct_snapshots.shape
    snap_count = columns // 2
    total_angles = local_angles * lax.axis_size("ka")
    table = piece_tables(total_angles, local_angles, "ka")
    first_wave = lax.axis_index("ka") * local_angles
    band_count = lax.axis_size("ka")
    band = radial_cells // band_count
    lanes = axial_cells * band * columns
    norm_factor = 1.0 / math.sqrt(axial_cells * lax.axis_size("gx") * radial_cells)
    band_weight = lax.dynamic_slice_in_dim(
        quad_weight * norm_factor, lax.axis_index("ka") * band, band, axis=1
    )
    lane_weight = jnp.broadcast_to(band_weight[:, :, None], (axial_cells, band, columns)).reshape(1, lanes)

    def transform_all(snapshots, weight=None):
        pieces = [piece.reshape(local_angles, lanes) for piece in exchange(snapshots, "ka", 2, True)]
        modes = dft(table, pieces, weight)
        return modes.reshape(total_angles, axial_cells, band, columns)

    direct_modes = in_source_order(exchange(transform_all(direct_snapshots), "ka", 0, True), "ka", 2)
    weighted = in_source_order(
        exchange(transform_all(adjoint_snapshots, lane_weight), "ka", 0, True), "ka", 2
    )
    padded = padded_2(direct_modes, (("gx", 1),), 1)
    field_f32 = direct_modes.astype(jnp.float32)
    forward = padded[:, 2:].astype(jnp.float32)
    behind = padded[:, :-2].astype(jnp.float32)
    radial_pad = jnp.pad(field_f32, ((0, 0), (0, 0), (1, 1), (0, 0)))
    outward = radial_pad[:, :, 2:]
    inward = radial_pad[:, :, :-2]
    radius = 0.25 + (jnp.arange(radial_cells, dtype=jnp.float32) + 0.5) / radial_cells
    wavenumber = (
        first_wave + jnp.arange(local_angles, dtype=jnp.int32) - total_angles // 2
    ).astype(jnp.float32) / total_angles
    azimuthal = (wavenumber[:, None] / radius[None, :]) ** 2
    velocity = mean_velocity[None, :, :, None]
    diffusion = diffusivity[None, :, :, None]
    image = (
        -velocity * (forward - behind) * 0.5
        + diffusion
        * (
            forward
            + behind
            + outward
            + inward
            - 4.0 * field_f32
            - azimuthal[:, None, :, None] * field_f32
        )
    ).astype(jnp.bfloat16)
    right_side = jnp.concatenate([direct_modes, image], axis=-1)
    product = jnp.einsum(
        "kpa,kpb->kab",
        weighted.reshape(local_angles, -1, columns),
        right_side.reshape(local_angles, -1, 2 * columns),
        preferred_element_type=jnp.float32,
    )
    gram_terms = complex_blocks(product, snap_count).reshape(local_angles * snap_count, 2 * columns)
    row_count = gram_terms.shape[0] // lax.axis_size("gx")
    row_index = lax.axis_index("gx") * row_count + jnp.arange(row_count, dtype=jnp.int32)
    owner = row_index // snap_count
    selector = (owner[:, None] == jnp.arange(local_angles, dtype=jnp.int32)[None, :]).astype(
        jnp.float32
    )
    shares = gram_terms.astype(jnp.bfloat16).reshape(lax.axis_size("gx"), row_count, 2 * columns)
    own_rows = sum(piece.astype(jnp.float32) for piece in exchange(shares, "gx", 0, True))[0]
    row_energy = jnp.sum(own_rows[:, :columns] ** 2, axis=1)
    energy = jnp.sum(gather_small(jnp.sum(selector * row_energy[:, None], axis=0), "gx"), axis=0)
    mean_sq = energy / (2.0 * snap_count * snap_count)
    row_scale = jnp.sum(selector * lax.rsqrt(mean_sq + epsilon)[None, :], axis=1)
    hankel_gram = own_rows[:, :columns] * row_scale[:, None]
    reduced_operator = own_rows[:, columns:] * row_scale[:, None]
    hankel_norm = jnp.sqrt(mean_sq)
    return (hankel_gram, reduced_operator, hankel_norm)


def solution(mesh):
    placed = (
        P("ka", "gx", None, None),
        P("ka", "gx", None, None),
        P("gx", None),
        P("gx", None),
        P("gx", None),
    )
    return jax.shard_map(
        local,
        mesh=mesh,
        in_specs=placed,
        out_specs=(P(("ka", "gx"), None), P(("ka", "gx"), None), P("ka")),
        check_vma=False,
    )
```

```python
import functools
import math

import jax
import jax.numpy as jnp
from jax import lax
from jax.experimental import pallas as pl
from jax.experimental.pallas import tpu as pltpu
from jax.sharding import PartitionSpec as P

epsilon = 1e-06


def padded_2(cells, sides, width):
    for axis, dim in sides:
        count = lax.axis_size(axis)
        ends = count - 1
        head = lax.slice_in_dim(cells, 0, width, axis=dim)
        tail = lax.slice_in_dim(cells, cells.shape[dim] - width, cells.shape[dim], axis=dim)
        cells = jnp.concatenate(
            [
                lax.ppermute(tail, axis, [(i, (i + 1) % count) for i in range(ends)]),
                cells,
                lax.ppermute(head, axis, [((i + 1) % count, i) for i in range(ends)]),
            ],
            axis=dim,
        )
    return cells


def gather_small(values, axis):
    count = lax.axis_size(axis)
    copies = jnp.broadcast_to(values[None], (count,) + values.shape)
    return lax.all_to_all(copies, axis, split_axis=0, concat_axis=0, tiled=True)


def exchange(cells, axis, split_axis, far_first=False):
    count = lax.axis_size(axis)
    here = lax.axis_index(axis)
    width = cells.shape[split_axis] // count
    shifts = list(range(count))
    if far_first:
        shifts = [0] + sorted(range(1, count), key=lambda shift: -min(shift, count - shift))
    pieces = []
    for shift in shifts:
        piece = lax.dynamic_slice_in_dim(cells, ((here + shift) % count) * width, width, axis=split_axis)
        if shift:
            piece = lax.ppermute(piece, axis, [(j, (j + shift) % count) for j in range(count)])
        pieces.append(piece)
    return pieces


def in_source_order(pieces, axis, concat_axis):
    count = len(pieces)
    here = lax.axis_index(axis)
    stacked = jnp.stack(pieces)
    ordered = [lax.dynamic_index_in_dim(stacked, (here - source) % count, 0, keepdims=False) for source in range(count)]
    return jnp.concatenate(ordered, axis=concat_axis)


def shifted_tables(count, local_angles, axis):
    here = lax.axis_index(axis)
    blocks = count // local_angles
    wave_index = jnp.arange(count, dtype=jnp.int32) - count // 2
    position = jnp.arange(count, dtype=jnp.int32)
    angle_index = ((here - position // local_angles) % blocks) * local_angles + position % local_angles
    residues = wave_index[:, None] * angle_index[None, :] % count
    phases = 2.0 * math.pi * residues.astype(jnp.float32) / count
    scaling = 1.0 / math.sqrt(count)
    return (
        (jnp.cos(phases) * scaling).astype(jnp.bfloat16),
        (jnp.sin(phases) * scaling).astype(jnp.bfloat16),
    )


def dft_kernel(*refs, count, weighted):
    table_ref = refs[0]
    piece_refs = refs[1:1 + count]
    rest = refs[1 + count:]
    out_ref = rest[-1]
    width = piece_refs[0].shape[1]
    lane = lax.broadcasted_iota(jnp.int32, (1, width), 1) % 128
    low = lane < 64
    packed = piece_refs[0].shape[0] % 16 == 0
    rows = []
    for piece_ref in piece_refs:
        x = piece_ref[...]
        if not packed:
            x = x.astype(jnp.float32)
        swapped = jnp.where(low, pltpu.roll(x, width - 64, 1), -pltpu.roll(x, 64, 1))
        rows.append(x)
        rows.append(swapped)
    stacked = jnp.concatenate(rows, axis=0).astype(jnp.bfloat16)
    acc = jnp.dot(table_ref[...], stacked, preferred_element_type=jnp.float32)
    modes = acc.astype(jnp.bfloat16)
    if weighted:
        modes = (modes.astype(jnp.float32) * rest[0][...]).astype(jnp.bfloat16)
    out_ref[...] = modes

def dft(table, pieces, weight=None):
    count = len(pieces)
    angles, total = pieces[0].shape
    waves = table.shape[0]
    block = math.gcd(total, 4096)
    grid = (total // block,)
    in_specs = [pl.BlockSpec((waves, table.shape[1]), lambda j: (0, 0))]
    in_specs += [pl.BlockSpec((angles, block), lambda j: (0, j)) for _ in pieces]
    args = [table, *pieces]
    if weight is not None:
        in_specs.append(pl.BlockSpec((1, block), lambda j: (0, j)))
        args.append(weight)
    return pl.pallas_call(
        functools.partial(dft_kernel, count=count, weighted=weight is not None),
        grid=grid,
        in_specs=in_specs,
        out_specs=pl.BlockSpec((waves, block), lambda j: (0, j)),
        out_shape=jax.ShapeDtypeStruct((waves, total), jnp.bfloat16),
    )(*args)


def piece_tables(count, local_angles, axis):
    here = lax.axis_index(axis)
    blocks = count // local_angles
    wave_index = jnp.arange(count, dtype=jnp.int32) - count // 2
    scaling = 1.0 / math.sqrt(count)
    columns = []
    for shift in range(blocks):
        angle_index = ((here - shift) % blocks) * local_angles + jnp.arange(local_angles, dtype=jnp.int32)
        residues = wave_index[:, None] * angle_index[None, :] % count
        phases = 2.0 * math.pi * residues.astype(jnp.float32) / count
        columns.append((jnp.cos(phases) * scaling).astype(jnp.bfloat16))
        columns.append((jnp.sin(phases) * scaling).astype(jnp.bfloat16))
    return jnp.concatenate(columns, axis=1)


def dft_tables(count):
    wave_index = jnp.arange(count, dtype=jnp.int32) - count // 2
    angle_index = jnp.arange(count, dtype=jnp.int32)
    residues = wave_index[:, None] * angle_index[None, :] % count
    phases = 2.0 * math.pi * residues.astype(jnp.float32) / count
    scaling = 1.0 / math.sqrt(count)
    return (
        (jnp.cos(phases) * scaling).astype(jnp.bfloat16),
        (jnp.sin(phases) * scaling).astype(jnp.bfloat16),
    )


def combine_parts(cos_part, sin_part, half):
    real_part = cos_part[..., :half] + sin_part[..., half:]
    imag_part = cos_part[..., half:] - sin_part[..., :half]
    return jnp.concatenate([real_part, imag_part], axis=-1).astype(jnp.bfloat16)


def complex_blocks(product, half):
    upper_rows = product[..., :half, :]
    lower_rows = product[..., half:, :]
    pieces = []
    for offset in (0, 2 * half):
        pieces.append(
            upper_rows[..., offset : offset + half]
            + lower_rows[..., offset + half : offset + 2 * half]
        )
        pieces.append(
            upper_rows[..., offset + half : offset + 2 * half]
            - lower_rows[..., offset : offset + half]
        )
    return jnp.concatenate(pieces, axis=-1)


def local(direct_snapshots, adjoint_snapshots, quad_weight, mean_velocity, diffusivity):
    local_angles, axial_cells, radial_cells, columns = direct_snapshots.shape
    snap_count = columns // 2
    total_angles = local_angles * lax.axis_size("ka")
    table = piece_tables(total_angles, local_angles, "ka")
    first_wave = lax.axis_index("ka") * local_angles
    band_count = lax.axis_size("ka")
    band = radial_cells // band_count
    lanes = axial_cells * band * columns
    norm_factor = 1.0 / math.sqrt(axial_cells * lax.axis_size("gx") * radial_cells)
    band_weight = lax.dynamic_slice_in_dim(
        quad_weight * norm_factor, lax.axis_index("ka") * band, band, axis=1
    )
    lane_weight = jnp.broadcast_to(band_weight[:, :, None], (axial_cells, band, columns)).reshape(1, lanes)

    def transform_all(snapshots, weight=None):
        pieces = [piece.reshape(local_angles, lanes) for piece in exchange(snapshots, "ka", 2)]
        modes = dft(table, pieces, weight)
        return modes.reshape(total_angles, axial_cells, band, columns)

    direct_modes = lax.all_to_all(
        transform_all(direct_snapshots), "ka", split_axis=0, concat_axis=2, tiled=True
    )
    weighted = lax.all_to_all(
        transform_all(adjoint_snapshots, lane_weight), "ka", split_axis=0, concat_axis=2, tiled=True
    )
    padded = padded_2(direct_modes, (("gx", 1),), 1)
    field_f32 = direct_modes.astype(jnp.float32)
    forward = padded[:, 2:].astype(jnp.float32)
    behind = padded[:, :-2].astype(jnp.float32)
    radial_pad = jnp.pad(field_f32, ((0, 0), (0, 0), (1, 1), (0, 0)))
    outward = radial_pad[:, :, 2:]
    inward = radial_pad[:, :, :-2]
    radius = 0.25 + (jnp.arange(radial_cells, dtype=jnp.float32) + 0.5) / radial_cells
    wavenumber = (
        first_wave + jnp.arange(local_angles, dtype=jnp.int32) - total_angles // 2
    ).astype(jnp.float32) / total_angles
    azimuthal = (wavenumber[:, None] / radius[None, :]) ** 2
    velocity = mean_velocity[None, :, :, None]
    diffusion = diffusivity[None, :, :, None]
    image = (
        -velocity * (forward - behind) * 0.5
        + diffusion
        * (
            forward
            + behind
            + outward
            + inward
            - 4.0 * field_f32
            - azimuthal[:, None, :, None] * field_f32
        )
    ).astype(jnp.bfloat16)
    right_side = jnp.concatenate([direct_modes, image], axis=-1)
    product = jnp.einsum(
        "kpa,kpb->kab",
        weighted.reshape(local_angles, -1, columns),
        right_side.reshape(local_angles, -1, 2 * columns),
        preferred_element_type=jnp.float32,
    )
    gram_terms = complex_blocks(product, snap_count).reshape(local_angles * snap_count, 2 * columns)
    row_count = gram_terms.shape[0] // lax.axis_size("gx")
    row_index = lax.axis_index("gx") * row_count + jnp.arange(row_count, dtype=jnp.int32)
    owner = row_index // snap_count
    selector = (owner[:, None] == jnp.arange(local_angles, dtype=jnp.int32)[None, :]).astype(
        jnp.float32
    )
    shares = gram_terms.astype(jnp.bfloat16).reshape(lax.axis_size("gx"), row_count, 2 * columns)
    own_rows = sum(piece.astype(jnp.float32) for piece in exchange(shares, "gx", 0, True))[0]
    row_energy = jnp.sum(own_rows[:, :columns] ** 2, axis=1)
    energy = jnp.sum(gather_small(jnp.sum(selector * row_energy[:, None], axis=0), "gx"), axis=0)
    mean_sq = energy / (2.0 * snap_count * snap_count)
    row_scale = jnp.sum(selector * lax.rsqrt(mean_sq + epsilon)[None, :], axis=1)
    hankel_gram = own_rows[:, :columns] * row_scale[:, None]
    reduced_operator = own_rows[:, columns:] * row_scale[:, None]
    hankel_norm = jnp.sqrt(mean_sq)
    return (hankel_gram, reduced_operator, hankel_norm)


def solution(mesh):
    placed = (
        P("ka", "gx", None, None),
        P("ka", "gx", None, None),
        P("gx", None),
        P("gx", None),
        P("gx", None),
    )
    return jax.shard_map(
        local,
        mesh=mesh,
        in_specs=placed,
        out_specs=(P(("ka", "gx"), None), P(("ka", "gx"), None), P("ka")),
        check_vma=False,
    )
```

```python
import functools
import math

import jax
import jax.numpy as jnp
from jax import lax
from jax.experimental import pallas as pl
from jax.experimental.pallas import tpu as pltpu
from jax.sharding import PartitionSpec as P

epsilon = 1e-06


def padded_2(cells, sides, width):
    for axis, dim in sides:
        count = lax.axis_size(axis)
        ends = count - 1
        head = lax.slice_in_dim(cells, 0, width, axis=dim)
        tail = lax.slice_in_dim(cells, cells.shape[dim] - width, cells.shape[dim], axis=dim)
        cells = jnp.concatenate(
            [
                lax.ppermute(tail, axis, [(i, (i + 1) % count) for i in range(ends)]),
                cells,
                lax.ppermute(head, axis, [((i + 1) % count, i) for i in range(ends)]),
            ],
            axis=dim,
        )
    return cells


def gather_small(values, axis):
    count = lax.axis_size(axis)
    copies = jnp.broadcast_to(values[None], (count,) + values.shape)
    return lax.all_to_all(copies, axis, split_axis=0, concat_axis=0, tiled=True)


def exchange(cells, axis, split_axis, far_first=False):
    count = lax.axis_size(axis)
    here = lax.axis_index(axis)
    width = cells.shape[split_axis] // count
    shifts = list(range(count))
    if far_first:
        shifts = [0] + sorted(range(1, count), key=lambda shift: -min(shift, count - shift))
    pieces = []
    for shift in shifts:
        piece = lax.dynamic_slice_in_dim(cells, ((here + shift) % count) * width, width, axis=split_axis)
        if shift:
            piece = lax.ppermute(piece, axis, [(j, (j + shift) % count) for j in range(count)])
        pieces.append(piece)
    return pieces


def in_source_order(pieces, axis, concat_axis):
    count = len(pieces)
    here = lax.axis_index(axis)
    stacked = jnp.stack(pieces)
    ordered = [lax.dynamic_index_in_dim(stacked, (here - source) % count, 0, keepdims=False) for source in range(count)]
    return jnp.concatenate(ordered, axis=concat_axis)


def shifted_tables(count, local_angles, axis):
    here = lax.axis_index(axis)
    blocks = count // local_angles
    wave_index = jnp.arange(count, dtype=jnp.int32) - count // 2
    position = jnp.arange(count, dtype=jnp.int32)
    angle_index = ((here - position // local_angles) % blocks) * local_angles + position % local_angles
    residues = wave_index[:, None] * angle_index[None, :] % count
    phases = 2.0 * math.pi * residues.astype(jnp.float32) / count
    scaling = 1.0 / math.sqrt(count)
    return (
        (jnp.cos(phases) * scaling).astype(jnp.bfloat16),
        (jnp.sin(phases) * scaling).astype(jnp.bfloat16),
    )


def dft_kernel(*refs, count, weighted):
    table_ref = refs[0]
    piece_refs = refs[1:1 + count]
    rest = refs[1 + count:]
    out_ref = rest[-1]
    width = piece_refs[0].shape[1]
    lane = lax.broadcasted_iota(jnp.int32, (1, width), 1) % 128
    low = lane < 64
    packed = piece_refs[0].shape[0] % 16 == 0
    rows = []
    for piece_ref in piece_refs:
        x = piece_ref[...]
        if not packed:
            x = x.astype(jnp.float32)
        swapped = jnp.where(low, pltpu.roll(x, width - 64, 1), -pltpu.roll(x, 64, 1))
        rows.append(x)
        rows.append(swapped)
    stacked = jnp.concatenate(rows, axis=0).astype(jnp.bfloat16)
    acc = jnp.dot(table_ref[...], stacked, preferred_element_type=jnp.float32)
    modes = acc.astype(jnp.bfloat16)
    if weighted:
        modes = (modes.astype(jnp.float32) * rest[0][...]).astype(jnp.bfloat16)
    out_ref[...] = modes

def dft(table, pieces, weight=None):
    count = len(pieces)
    angles, total = pieces[0].shape
    waves = table.shape[0]
    block = math.gcd(total, 4096)
    grid = (total // block,)
    in_specs = [pl.BlockSpec((waves, table.shape[1]), lambda j: (0, 0))]
    in_specs += [pl.BlockSpec((angles, block), lambda j: (0, j)) for _ in pieces]
    args = [table, *pieces]
    if weight is not None:
        in_specs.append(pl.BlockSpec((1, block), lambda j: (0, j)))
        args.append(weight)
    return pl.pallas_call(
        functools.partial(dft_kernel, count=count, weighted=weight is not None),
        grid=grid,
        in_specs=in_specs,
        out_specs=pl.BlockSpec((waves, block), lambda j: (0, j)),
        out_shape=jax.ShapeDtypeStruct((waves, total), jnp.bfloat16),
    )(*args)


def piece_tables(count, local_angles, axis):
    here = lax.axis_index(axis)
    blocks = count // local_angles
    wave_index = jnp.arange(count, dtype=jnp.int32) - count // 2
    scaling = 1.0 / math.sqrt(count)
    columns = []
    for shift in range(blocks):
        angle_index = ((here - shift) % blocks) * local_angles + jnp.arange(local_angles, dtype=jnp.int32)
        residues = wave_index[:, None] * angle_index[None, :] % count
        phases = 2.0 * math.pi * residues.astype(jnp.float32) / count
        columns.append((jnp.cos(phases) * scaling).astype(jnp.bfloat16))
        columns.append((jnp.sin(phases) * scaling).astype(jnp.bfloat16))
    return jnp.concatenate(columns, axis=1)


def dft_tables(count):
    wave_index = jnp.arange(count, dtype=jnp.int32) - count // 2
    angle_index = jnp.arange(count, dtype=jnp.int32)
    residues = wave_index[:, None] * angle_index[None, :] % count
    phases = 2.0 * math.pi * residues.astype(jnp.float32) / count
    scaling = 1.0 / math.sqrt(count)
    return (
        (jnp.cos(phases) * scaling).astype(jnp.bfloat16),
        (jnp.sin(phases) * scaling).astype(jnp.bfloat16),
    )


def combine_parts(cos_part, sin_part, half):
    real_part = cos_part[..., :half] + sin_part[..., half:]
    imag_part = cos_part[..., half:] - sin_part[..., :half]
    return jnp.concatenate([real_part, imag_part], axis=-1).astype(jnp.bfloat16)


def complex_blocks(product, half):
    upper_rows = product[..., :half, :]
    lower_rows = product[..., half:, :]
    pieces = []
    for offset in (0, 2 * half):
        pieces.append(
            upper_rows[..., offset : offset + half]
            + lower_rows[..., offset + half : offset + 2 * half]
        )
        pieces.append(
            upper_rows[..., offset + half : offset + 2 * half]
            - lower_rows[..., offset : offset + half]
        )
    return jnp.concatenate(pieces, axis=-1)


def local(direct_snapshots, adjoint_snapshots, quad_weight, mean_velocity, diffusivity):
    local_angles, axial_cells, radial_cells, columns = direct_snapshots.shape
    snap_count = columns // 2
    total_angles = local_angles * lax.axis_size("ka")
    table = piece_tables(total_angles, local_angles, "ka")
    first_wave = lax.axis_index("ka") * local_angles
    band_count = lax.axis_size("ka")
    band = radial_cells // band_count
    lanes = axial_cells * band * columns
    norm_factor = 1.0 / math.sqrt(axial_cells * lax.axis_size("gx") * radial_cells)
    band_weight = lax.dynamic_slice_in_dim(
        quad_weight * norm_factor, lax.axis_index("ka") * band, band, axis=1
    )
    lane_weight = jnp.broadcast_to(band_weight[:, :, None], (axial_cells, band, columns)).reshape(1, lanes)

    def transform_all(snapshots, weight=None):
        pieces = [piece.reshape(local_angles, lanes) for piece in exchange(snapshots, "ka", 2)]
        modes = dft(table, pieces, weight)
        return modes.reshape(total_angles, axial_cells, band, columns)

    direct_modes = in_source_order(exchange(transform_all(direct_snapshots), "ka", 0), "ka", 2)
    weighted = in_source_order(
        exchange(transform_all(adjoint_snapshots, lane_weight), "ka", 0), "ka", 2
    )
    padded = padded_2(direct_modes, (("gx", 1),), 1)
    field_f32 = direct_modes.astype(jnp.float32)
    forward = padded[:, 2:].astype(jnp.float32)
    behind = padded[:, :-2].astype(jnp.float32)
    radial_pad = jnp.pad(field_f32, ((0, 0), (0, 0), (1, 1), (0, 0)))
    outward = radial_pad[:, :, 2:]
    inward = radial_pad[:, :, :-2]
    radius = 0.25 + (jnp.arange(radial_cells, dtype=jnp.float32) + 0.5) / radial_cells
    wavenumber = (
        first_wave + jnp.arange(local_angles, dtype=jnp.int32) - total_angles // 2
    ).astype(jnp.float32) / total_angles
    azimuthal = (wavenumber[:, None] / radius[None, :]) ** 2
    velocity = mean_velocity[None, :, :, None]
    diffusion = diffusivity[None, :, :, None]
    image = (
        -velocity * (forward - behind) * 0.5
        + diffusion
        * (
            forward
            + behind
            + outward
            + inward
            - 4.0 * field_f32
            - azimuthal[:, None, :, None] * field_f32
        )
    ).astype(jnp.bfloat16)
    left_side = weighted.reshape(local_angles, -1, columns)
    product = jnp.concatenate(
        [
            jnp.einsum(
                "kpa,kpb->kab",
                left_side,
                right.reshape(local_angles, -1, columns),
                preferred_element_type=jnp.float32,
            )
            for right in (direct_modes, image)
        ],
        axis=-1,
    )
    gram_terms = complex_blocks(product, snap_count).reshape(local_angles * snap_count, 2 * columns)
    row_count = gram_terms.shape[0] // lax.axis_size("gx")
    row_index = lax.axis_index("gx") * row_count + jnp.arange(row_count, dtype=jnp.int32)
    owner = row_index // snap_count
    selector = (owner[:, None] == jnp.arange(local_angles, dtype=jnp.int32)[None, :]).astype(
        jnp.float32
    )
    shares = gram_terms.astype(jnp.bfloat16).reshape(lax.axis_size("gx"), row_count, 2 * columns)
    own_rows = sum(piece.astype(jnp.float32) for piece in exchange(shares, "gx", 0, True))[0]
    row_energy = jnp.sum(own_rows[:, :columns] ** 2, axis=1)
    energy = jnp.sum(gather_small(jnp.sum(selector * row_energy[:, None], axis=0), "gx"), axis=0)
    mean_sq = energy / (2.0 * snap_count * snap_count)
    row_scale = jnp.sum(selector * lax.rsqrt(mean_sq + epsilon)[None, :], axis=1)
    hankel_gram = own_rows[:, :columns] * row_scale[:, None]
    reduced_operator = own_rows[:, columns:] * row_scale[:, None]
    hankel_norm = jnp.sqrt(mean_sq)
    return (hankel_gram, reduced_operator, hankel_norm)


def solution(mesh):
    placed = (
        P("ka", "gx", None, None),
        P("ka", "gx", None, None),
        P("gx", None),
        P("gx", None),
        P("gx", None),
    )
    return jax.shard_map(
        local,
        mesh=mesh,
        in_specs=placed,
        out_specs=(P(("ka", "gx"), None), P(("ka", "gx"), None), P("ka")),
        check_vma=False,
    )
```

```python
import functools
import math

import jax
import jax.numpy as jnp
from jax import lax
from jax.experimental import pallas as pl
from jax.experimental.pallas import tpu as pltpu
from jax.sharding import PartitionSpec as P

epsilon = 1e-06


def padded_2(cells, sides, width):
    for axis, dim in sides:
        count = lax.axis_size(axis)
        ends = count - 1
        head = lax.slice_in_dim(cells, 0, width, axis=dim)
        tail = lax.slice_in_dim(cells, cells.shape[dim] - width, cells.shape[dim], axis=dim)
        cells = jnp.concatenate(
            [
                lax.ppermute(tail, axis, [(i, (i + 1) % count) for i in range(ends)]),
                cells,
                lax.ppermute(head, axis, [((i + 1) % count, i) for i in range(ends)]),
            ],
            axis=dim,
        )
    return cells


def gather_small(values, axis):
    count = lax.axis_size(axis)
    copies = jnp.broadcast_to(values[None], (count,) + values.shape)
    return lax.all_to_all(copies, axis, split_axis=0, concat_axis=0, tiled=True)


def exchange(cells, axis, split_axis, far_first=False, separate=False):
    count = lax.axis_size(axis)
    here = lax.axis_index(axis)
    width = cells.shape[split_axis] // count
    shifts = list(range(count))
    if far_first:
        shifts = [0] + sorted(range(1, count), key=lambda shift: -min(shift, count - shift))
    pieces = []
    for shift in shifts:
        source = cells
        if separate:
            source, _ = lax.optimization_barrier((cells, jnp.int32(shift)))
        piece = lax.dynamic_slice_in_dim(source, ((here + shift) % count) * width, width, axis=split_axis)
        if shift:
            piece = lax.ppermute(piece, axis, [(j, (j + shift) % count) for j in range(count)])
        pieces.append(piece)
    return pieces


def in_source_order(pieces, axis, concat_axis):
    count = len(pieces)
    here = lax.axis_index(axis)
    stacked = jnp.stack(pieces)
    ordered = [lax.dynamic_index_in_dim(stacked, (here - source) % count, 0, keepdims=False) for source in range(count)]
    return jnp.concatenate(ordered, axis=concat_axis)


def shifted_tables(count, local_angles, axis):
    here = lax.axis_index(axis)
    blocks = count // local_angles
    wave_index = jnp.arange(count, dtype=jnp.int32) - count // 2
    position = jnp.arange(count, dtype=jnp.int32)
    angle_index = ((here - position // local_angles) % blocks) * local_angles + position % local_angles
    residues = wave_index[:, None] * angle_index[None, :] % count
    phases = 2.0 * math.pi * residues.astype(jnp.float32) / count
    scaling = 1.0 / math.sqrt(count)
    return (
        (jnp.cos(phases) * scaling).astype(jnp.bfloat16),
        (jnp.sin(phases) * scaling).astype(jnp.bfloat16),
    )


def dft_kernel(*refs, count, weighted):
    table_ref = refs[0]
    piece_refs = refs[1:1 + count]
    rest = refs[1 + count:]
    out_ref = rest[-1]
    width = piece_refs[0].shape[1]
    lane = lax.broadcasted_iota(jnp.int32, (1, width), 1) % 128
    low = lane < 64
    packed = piece_refs[0].shape[0] % 16 == 0
    rows = []
    for piece_ref in piece_refs:
        x = piece_ref[...]
        if not packed:
            x = x.astype(jnp.float32)
        swapped = jnp.where(low, pltpu.roll(x, width - 64, 1), -pltpu.roll(x, 64, 1))
        rows.append(x)
        rows.append(swapped)
    stacked = jnp.concatenate(rows, axis=0).astype(jnp.bfloat16)
    acc = jnp.dot(table_ref[...], stacked, preferred_element_type=jnp.float32)
    modes = acc.astype(jnp.bfloat16)
    if weighted:
        modes = (modes.astype(jnp.float32) * rest[0][...]).astype(jnp.bfloat16)
    out_ref[...] = modes

def dft(table, pieces, weight=None):
    count = len(pieces)
    angles, total = pieces[0].shape
    waves = table.shape[0]
    block = math.gcd(total, 4096)
    grid = (total // block,)
    in_specs = [pl.BlockSpec((waves, table.shape[1]), lambda j: (0, 0))]
    in_specs += [pl.BlockSpec((angles, block), lambda j: (0, j)) for _ in pieces]
    args = [table, *pieces]
    if weight is not None:
        in_specs.append(pl.BlockSpec((1, block), lambda j: (0, j)))
        args.append(weight)
    return pl.pallas_call(
        functools.partial(dft_kernel, count=count, weighted=weight is not None),
        grid=grid,
        in_specs=in_specs,
        out_specs=pl.BlockSpec((waves, block), lambda j: (0, j)),
        out_shape=jax.ShapeDtypeStruct((waves, total), jnp.bfloat16),
    )(*args)


def piece_tables(count, local_angles, axis):
    here = lax.axis_index(axis)
    blocks = count // local_angles
    wave_index = jnp.arange(count, dtype=jnp.int32) - count // 2
    scaling = 1.0 / math.sqrt(count)
    columns = []
    for shift in range(blocks):
        angle_index = ((here - shift) % blocks) * local_angles + jnp.arange(local_angles, dtype=jnp.int32)
        residues = wave_index[:, None] * angle_index[None, :] % count
        phases = 2.0 * math.pi * residues.astype(jnp.float32) / count
        columns.append((jnp.cos(phases) * scaling).astype(jnp.bfloat16))
        columns.append((jnp.sin(phases) * scaling).astype(jnp.bfloat16))
    return jnp.concatenate(columns, axis=1)


def dft_tables(count):
    wave_index = jnp.arange(count, dtype=jnp.int32) - count // 2
    angle_index = jnp.arange(count, dtype=jnp.int32)
    residues = wave_index[:, None] * angle_index[None, :] % count
    phases = 2.0 * math.pi * residues.astype(jnp.float32) / count
    scaling = 1.0 / math.sqrt(count)
    return (
        (jnp.cos(phases) * scaling).astype(jnp.bfloat16),
        (jnp.sin(phases) * scaling).astype(jnp.bfloat16),
    )


def combine_parts(cos_part, sin_part, half):
    real_part = cos_part[..., :half] + sin_part[..., half:]
    imag_part = cos_part[..., half:] - sin_part[..., :half]
    return jnp.concatenate([real_part, imag_part], axis=-1).astype(jnp.bfloat16)


def complex_blocks(product, half):
    upper_rows = product[..., :half, :]
    lower_rows = product[..., half:, :]
    pieces = []
    for offset in (0, 2 * half):
        pieces.append(
            upper_rows[..., offset : offset + half]
            + lower_rows[..., offset + half : offset + 2 * half]
        )
        pieces.append(
            upper_rows[..., offset + half : offset + 2 * half]
            - lower_rows[..., offset : offset + half]
        )
    return jnp.concatenate(pieces, axis=-1)


def local(direct_snapshots, adjoint_snapshots, quad_weight, mean_velocity, diffusivity):
    local_angles, axial_cells, radial_cells, columns = direct_snapshots.shape
    snap_count = columns // 2
    total_angles = local_angles * lax.axis_size("ka")
    table = piece_tables(total_angles, local_angles, "ka")
    first_wave = lax.axis_index("ka") * local_angles
    band_count = lax.axis_size("ka")
    band = radial_cells // band_count
    lanes = axial_cells * band * columns
    norm_factor = 1.0 / math.sqrt(axial_cells * lax.axis_size("gx") * radial_cells)
    band_weight = lax.dynamic_slice_in_dim(
        quad_weight * norm_factor, lax.axis_index("ka") * band, band, axis=1
    )
    lane_weight = jnp.broadcast_to(band_weight[:, :, None], (axial_cells, band, columns)).reshape(1, lanes)

    def transform_all(snapshots, weight=None):
        pieces = [piece.reshape(local_angles, lanes) for piece in exchange(snapshots, "ka", 2, separate=True)]
        modes = dft(table, pieces, weight)
        return modes.reshape(total_angles, axial_cells, band, columns)

    direct_modes = in_source_order(exchange(transform_all(direct_snapshots), "ka", 0), "ka", 2)
    weighted = in_source_order(
        exchange(transform_all(adjoint_snapshots, lane_weight), "ka", 0), "ka", 2
    )
    padded = padded_2(direct_modes, (("gx", 1),), 1)
    field_f32 = direct_modes.astype(jnp.float32)
    forward = padded[:, 2:].astype(jnp.float32)
    behind = padded[:, :-2].astype(jnp.float32)
    radial_pad = jnp.pad(field_f32, ((0, 0), (0, 0), (1, 1), (0, 0)))
    outward = radial_pad[:, :, 2:]
    inward = radial_pad[:, :, :-2]
    radius = 0.25 + (jnp.arange(radial_cells, dtype=jnp.float32) + 0.5) / radial_cells
    wavenumber = (
        first_wave + jnp.arange(local_angles, dtype=jnp.int32) - total_angles // 2
    ).astype(jnp.float32) / total_angles
    azimuthal = (wavenumber[:, None] / radius[None, :]) ** 2
    velocity = mean_velocity[None, :, :, None]
    diffusion = diffusivity[None, :, :, None]
    image = (
        -velocity * (forward - behind) * 0.5
        + diffusion
        * (
            forward
            + behind
            + outward
            + inward
            - 4.0 * field_f32
            - azimuthal[:, None, :, None] * field_f32
        )
    ).astype(jnp.bfloat16)
    right_side = jnp.concatenate([direct_modes, image], axis=-1)
    product = jnp.einsum(
        "kpa,kpb->kab",
        weighted.reshape(local_angles, -1, columns),
        right_side.reshape(local_angles, -1, 2 * columns),
        preferred_element_type=jnp.float32,
    )
    gram_terms = complex_blocks(product, snap_count).reshape(local_angles * snap_count, 2 * columns)
    row_count = gram_terms.shape[0] // lax.axis_size("gx")
    row_index = lax.axis_index("gx") * row_count + jnp.arange(row_count, dtype=jnp.int32)
    owner = row_index // snap_count
    selector = (owner[:, None] == jnp.arange(local_angles, dtype=jnp.int32)[None, :]).astype(
        jnp.float32
    )
    shares = gram_terms.astype(jnp.bfloat16).reshape(lax.axis_size("gx"), row_count, 2 * columns)
    own_rows = sum(piece.astype(jnp.float32) for piece in exchange(shares, "gx", 0, True))[0]
    row_energy = jnp.sum(own_rows[:, :columns] ** 2, axis=1)
    energy = jnp.sum(gather_small(jnp.sum(selector * row_energy[:, None], axis=0), "gx"), axis=0)
    mean_sq = energy / (2.0 * snap_count * snap_count)
    row_scale = jnp.sum(selector * lax.rsqrt(mean_sq + epsilon)[None, :], axis=1)
    hankel_gram = own_rows[:, :columns] * row_scale[:, None]
    reduced_operator = own_rows[:, columns:] * row_scale[:, None]
    hankel_norm = jnp.sqrt(mean_sq)
    return (hankel_gram, reduced_operator, hankel_norm)


def solution(mesh):
    placed = (
        P("ka", "gx", None, None),
        P("ka", "gx", None, None),
        P("gx", None),
        P("gx", None),
        P("gx", None),
    )
    return jax.shard_map(
        local,
        mesh=mesh,
        in_specs=placed,
        out_specs=(P(("ka", "gx"), None), P(("ka", "gx"), None), P("ka")),
        check_vma=False,
    )
```

```python
import functools
import math

import jax
import jax.numpy as jnp
from jax import lax
from jax.experimental import pallas as pl
from jax.experimental.pallas import tpu as pltpu
from jax.sharding import PartitionSpec as P

epsilon = 1e-06


def padded_2(cells, sides, width):
    for axis, dim in sides:
        count = lax.axis_size(axis)
        ends = count - 1
        head = lax.slice_in_dim(cells, 0, width, axis=dim)
        tail = lax.slice_in_dim(cells, cells.shape[dim] - width, cells.shape[dim], axis=dim)
        cells = jnp.concatenate(
            [
                lax.ppermute(tail, axis, [(i, (i + 1) % count) for i in range(ends)]),
                cells,
                lax.ppermute(head, axis, [((i + 1) % count, i) for i in range(ends)]),
            ],
            axis=dim,
        )
    return cells


def gather_small(values, axis):
    count = lax.axis_size(axis)
    copies = jnp.broadcast_to(values[None], (count,) + values.shape)
    return lax.all_to_all(copies, axis, split_axis=0, concat_axis=0, tiled=True)


def exchange(cells, axis, split_axis, far_first=False, separate=False):
    count = lax.axis_size(axis)
    here = lax.axis_index(axis)
    width = cells.shape[split_axis] // count
    shifts = list(range(count))
    if far_first:
        shifts = [0] + sorted(range(1, count), key=lambda shift: -min(shift, count - shift))
    pieces = []
    for shift in shifts:
        source = cells
        if separate:
            source, _ = lax.optimization_barrier((cells, jnp.int32(shift)))
        piece = lax.dynamic_slice_in_dim(source, ((here + shift) % count) * width, width, axis=split_axis)
        if shift:
            piece = lax.ppermute(piece, axis, [(j, (j + shift) % count) for j in range(count)])
        pieces.append(piece)
    return pieces


def in_source_order(pieces, axis, concat_axis):
    count = len(pieces)
    here = lax.axis_index(axis)
    stacked = jnp.stack(pieces)
    ordered = [lax.dynamic_index_in_dim(stacked, (here - source) % count, 0, keepdims=False) for source in range(count)]
    return jnp.concatenate(ordered, axis=concat_axis)


def shifted_tables(count, local_angles, axis):
    here = lax.axis_index(axis)
    blocks = count // local_angles
    wave_index = jnp.arange(count, dtype=jnp.int32) - count // 2
    position = jnp.arange(count, dtype=jnp.int32)
    angle_index = ((here - position // local_angles) % blocks) * local_angles + position % local_angles
    residues = wave_index[:, None] * angle_index[None, :] % count
    phases = 2.0 * math.pi * residues.astype(jnp.float32) / count
    scaling = 1.0 / math.sqrt(count)
    return (
        (jnp.cos(phases) * scaling).astype(jnp.bfloat16),
        (jnp.sin(phases) * scaling).astype(jnp.bfloat16),
    )


def dft_kernel(*refs, count, weighted):
    table_ref = refs[0]
    piece_refs = refs[1:1 + count]
    rest = refs[1 + count:]
    out_ref = rest[-1]
    width = piece_refs[0].shape[1]
    lane = lax.broadcasted_iota(jnp.int32, (1, width), 1) % 128
    low = lane < 64
    packed = piece_refs[0].shape[0] % 16 == 0
    rows = []
    for piece_ref in piece_refs:
        x = piece_ref[...]
        if not packed:
            x = x.astype(jnp.float32)
        swapped = jnp.where(low, pltpu.roll(x, width - 64, 1), -pltpu.roll(x, 64, 1))
        rows.append(x)
        rows.append(swapped)
    stacked = jnp.concatenate(rows, axis=0).astype(jnp.bfloat16)
    acc = jnp.dot(table_ref[...], stacked, preferred_element_type=jnp.float32)
    modes = acc.astype(jnp.bfloat16)
    if weighted:
        modes = (modes.astype(jnp.float32) * rest[0][...]).astype(jnp.bfloat16)
    out_ref[...] = modes

def dft(table, pieces, weight=None):
    count = len(pieces)
    angles, total = pieces[0].shape
    waves = table.shape[0]
    block = math.gcd(total, 4096)
    grid = (total // block,)
    in_specs = [pl.BlockSpec((waves, table.shape[1]), lambda j: (0, 0))]
    in_specs += [pl.BlockSpec((angles, block), lambda j: (0, j)) for _ in pieces]
    args = [table, *pieces]
    if weight is not None:
        in_specs.append(pl.BlockSpec((1, block), lambda j: (0, j)))
        args.append(weight)
    return pl.pallas_call(
        functools.partial(dft_kernel, count=count, weighted=weight is not None),
        grid=grid,
        in_specs=in_specs,
        out_specs=pl.BlockSpec((waves, block), lambda j: (0, j)),
        out_shape=jax.ShapeDtypeStruct((waves, total), jnp.bfloat16),
    )(*args)


def piece_tables(count, local_angles, axis):
    here = lax.axis_index(axis)
    blocks = count // local_angles
    wave_index = jnp.arange(count, dtype=jnp.int32) - count // 2
    scaling = 1.0 / math.sqrt(count)
    columns = []
    for shift in range(blocks):
        angle_index = ((here - shift) % blocks) * local_angles + jnp.arange(local_angles, dtype=jnp.int32)
        residues = wave_index[:, None] * angle_index[None, :] % count
        phases = 2.0 * math.pi * residues.astype(jnp.float32) / count
        columns.append((jnp.cos(phases) * scaling).astype(jnp.bfloat16))
        columns.append((jnp.sin(phases) * scaling).astype(jnp.bfloat16))
    return jnp.concatenate(columns, axis=1)


def dft_tables(count):
    wave_index = jnp.arange(count, dtype=jnp.int32) - count // 2
    angle_index = jnp.arange(count, dtype=jnp.int32)
    residues = wave_index[:, None] * angle_index[None, :] % count
    phases = 2.0 * math.pi * residues.astype(jnp.float32) / count
    scaling = 1.0 / math.sqrt(count)
    return (
        (jnp.cos(phases) * scaling).astype(jnp.bfloat16),
        (jnp.sin(phases) * scaling).astype(jnp.bfloat16),
    )


def combine_parts(cos_part, sin_part, half):
    real_part = cos_part[..., :half] + sin_part[..., half:]
    imag_part = cos_part[..., half:] - sin_part[..., :half]
    return jnp.concatenate([real_part, imag_part], axis=-1).astype(jnp.bfloat16)


def complex_blocks(product, half):
    upper_rows = product[..., :half, :]
    lower_rows = product[..., half:, :]
    pieces = []
    for offset in (0, 2 * half):
        pieces.append(
            upper_rows[..., offset : offset + half]
            + lower_rows[..., offset + half : offset + 2 * half]
        )
        pieces.append(
            upper_rows[..., offset + half : offset + 2 * half]
            - lower_rows[..., offset : offset + half]
        )
    return jnp.concatenate(pieces, axis=-1)


def local(direct_snapshots, adjoint_snapshots, quad_weight, mean_velocity, diffusivity):
    local_angles, axial_cells, radial_cells, columns = direct_snapshots.shape
    snap_count = columns // 2
    total_angles = local_angles * lax.axis_size("ka")
    table = piece_tables(total_angles, local_angles, "ka")
    first_wave = lax.axis_index("ka") * local_angles
    band_count = lax.axis_size("ka")
    band = radial_cells // band_count
    lanes = axial_cells * band * columns
    norm_factor = 1.0 / math.sqrt(axial_cells * lax.axis_size("gx") * radial_cells)
    band_weight = lax.dynamic_slice_in_dim(
        quad_weight * norm_factor, lax.axis_index("ka") * band, band, axis=1
    )
    lane_weight = jnp.broadcast_to(band_weight[:, :, None], (axial_cells, band, columns)).reshape(1, lanes)

    def transform_all(snapshots, weight=None):
        pieces = [piece.reshape(local_angles, lanes) for piece in exchange(snapshots, "ka", 2, separate=True)]
        modes = dft(table, pieces, weight)
        return modes.reshape(total_angles, axial_cells, band, columns)

    direct_modes = in_source_order(exchange(transform_all(direct_snapshots), "ka", 0, separate=True), "ka", 2)
    weighted = in_source_order(
        exchange(transform_all(adjoint_snapshots, lane_weight), "ka", 0, separate=True), "ka", 2
    )
    padded = padded_2(direct_modes, (("gx", 1),), 1)
    field_f32 = direct_modes.astype(jnp.float32)
    forward = padded[:, 2:].astype(jnp.float32)
    behind = padded[:, :-2].astype(jnp.float32)
    radial_pad = jnp.pad(field_f32, ((0, 0), (0, 0), (1, 1), (0, 0)))
    outward = radial_pad[:, :, 2:]
    inward = radial_pad[:, :, :-2]
    radius = 0.25 + (jnp.arange(radial_cells, dtype=jnp.float32) + 0.5) / radial_cells
    wavenumber = (
        first_wave + jnp.arange(local_angles, dtype=jnp.int32) - total_angles // 2
    ).astype(jnp.float32) / total_angles
    azimuthal = (wavenumber[:, None] / radius[None, :]) ** 2
    velocity = mean_velocity[None, :, :, None]
    diffusion = diffusivity[None, :, :, None]
    image = (
        -velocity * (forward - behind) * 0.5
        + diffusion
        * (
            forward
            + behind
            + outward
            + inward
            - 4.0 * field_f32
            - azimuthal[:, None, :, None] * field_f32
        )
    ).astype(jnp.bfloat16)
    right_side = jnp.concatenate([direct_modes, image], axis=-1)
    product = jnp.einsum(
        "kpa,kpb->kab",
        weighted.reshape(local_angles, -1, columns),
        right_side.reshape(local_angles, -1, 2 * columns),
        preferred_element_type=jnp.float32,
    )
    gram_terms = complex_blocks(product, snap_count).reshape(local_angles * snap_count, 2 * columns)
    row_count = gram_terms.shape[0] // lax.axis_size("gx")
    row_index = lax.axis_index("gx") * row_count + jnp.arange(row_count, dtype=jnp.int32)
    owner = row_index // snap_count
    selector = (owner[:, None] == jnp.arange(local_angles, dtype=jnp.int32)[None, :]).astype(
        jnp.float32
    )
    shares = gram_terms.astype(jnp.bfloat16).reshape(lax.axis_size("gx"), row_count, 2 * columns)
    own_rows = sum(piece.astype(jnp.float32) for piece in exchange(shares, "gx", 0, True, True))[0]
    row_energy = jnp.sum(own_rows[:, :columns] ** 2, axis=1)
    energy = jnp.sum(gather_small(jnp.sum(selector * row_energy[:, None], axis=0), "gx"), axis=0)
    mean_sq = energy / (2.0 * snap_count * snap_count)
    row_scale = jnp.sum(selector * lax.rsqrt(mean_sq + epsilon)[None, :], axis=1)
    hankel_gram = own_rows[:, :columns] * row_scale[:, None]
    reduced_operator = own_rows[:, columns:] * row_scale[:, None]
    hankel_norm = jnp.sqrt(mean_sq)
    return (hankel_gram, reduced_operator, hankel_norm)


def solution(mesh):
    placed = (
        P("ka", "gx", None, None),
        P("ka", "gx", None, None),
        P("gx", None),
        P("gx", None),
        P("gx", None),
    )
    return jax.shard_map(
        local,
        mesh=mesh,
        in_specs=placed,
        out_specs=(P(("ka", "gx"), None), P(("ka", "gx"), None), P("ka")),
        check_vma=False,
    )
```

```python
import functools
import math

import jax
import jax.numpy as jnp
from jax import lax
from jax.experimental import pallas as pl
from jax.experimental.pallas import tpu as pltpu
from jax.sharding import PartitionSpec as P

epsilon = 1e-06


def padded_2(cells, sides, width):
    for axis, dim in sides:
        count = lax.axis_size(axis)
        ends = count - 1
        head = lax.slice_in_dim(cells, 0, width, axis=dim)
        tail = lax.slice_in_dim(cells, cells.shape[dim] - width, cells.shape[dim], axis=dim)
        cells = jnp.concatenate(
            [
                lax.ppermute(tail, axis, [(i, (i + 1) % count) for i in range(ends)]),
                cells,
                lax.ppermute(head, axis, [((i + 1) % count, i) for i in range(ends)]),
            ],
            axis=dim,
        )
    return cells


def gather_small(values, axis):
    count = lax.axis_size(axis)
    copies = jnp.broadcast_to(values[None], (count,) + values.shape)
    return lax.all_to_all(copies, axis, split_axis=0, concat_axis=0, tiled=True)


def exchange(cells, axis, split_axis, far_first=False, separate=False):
    count = lax.axis_size(axis)
    here = lax.axis_index(axis)
    width = cells.shape[split_axis] // count
    shifts = list(range(count))
    if far_first:
        shifts = [0] + sorted(range(1, count), key=lambda shift: -min(shift, count - shift))
    pieces = []
    for shift in shifts:
        source = cells
        if separate:
            source, _ = lax.optimization_barrier((cells, jnp.int32(shift)))
        piece = lax.dynamic_slice_in_dim(source, ((here + shift) % count) * width, width, axis=split_axis)
        if shift:
            piece = lax.ppermute(piece, axis, [(j, (j + shift) % count) for j in range(count)])
        pieces.append(piece)
    return pieces


def in_source_order(pieces, axis, concat_axis):
    count = len(pieces)
    here = lax.axis_index(axis)
    stacked = jnp.stack(pieces)
    ordered = [lax.dynamic_index_in_dim(stacked, (here - source) % count, 0, keepdims=False) for source in range(count)]
    return jnp.concatenate(ordered, axis=concat_axis)


def shifted_tables(count, local_angles, axis):
    here = lax.axis_index(axis)
    blocks = count // local_angles
    wave_index = jnp.arange(count, dtype=jnp.int32) - count // 2
    position = jnp.arange(count, dtype=jnp.int32)
    angle_index = ((here - position // local_angles) % blocks) * local_angles + position % local_angles
    residues = wave_index[:, None] * angle_index[None, :] % count
    phases = 2.0 * math.pi * residues.astype(jnp.float32) / count
    scaling = 1.0 / math.sqrt(count)
    return (
        (jnp.cos(phases) * scaling).astype(jnp.bfloat16),
        (jnp.sin(phases) * scaling).astype(jnp.bfloat16),
    )


def dft_kernel(*refs, count, weighted):
    table_ref = refs[0]
    piece_refs = refs[1:1 + count]
    rest = refs[1 + count:]
    out_ref = rest[-1]
    width = piece_refs[0].shape[1]
    lane = lax.broadcasted_iota(jnp.int32, (1, width), 1) % 128
    low = lane < 64
    packed = piece_refs[0].shape[0] % 16 == 0
    rows = []
    for piece_ref in piece_refs:
        x = piece_ref[...]
        if not packed:
            x = x.astype(jnp.float32)
        swapped = jnp.where(low, pltpu.roll(x, width - 64, 1), -pltpu.roll(x, 64, 1))
        rows.append(x)
        rows.append(swapped)
    stacked = jnp.concatenate(rows, axis=0).astype(jnp.bfloat16)
    acc = jnp.dot(table_ref[...], stacked, preferred_element_type=jnp.float32)
    modes = acc.astype(jnp.bfloat16)
    if weighted:
        modes = (modes.astype(jnp.float32) * rest[0][...]).astype(jnp.bfloat16)
    out_ref[...] = modes

def dft(table, pieces, weight=None):
    count = len(pieces)
    angles, total = pieces[0].shape
    waves = table.shape[0]
    block = math.gcd(total, 4096)
    grid = (total // block,)
    in_specs = [pl.BlockSpec((waves, table.shape[1]), lambda j: (0, 0))]
    in_specs += [pl.BlockSpec((angles, block), lambda j: (0, j)) for _ in pieces]
    args = [table, *pieces]
    if weight is not None:
        in_specs.append(pl.BlockSpec((1, block), lambda j: (0, j)))
        args.append(weight)
    return pl.pallas_call(
        functools.partial(dft_kernel, count=count, weighted=weight is not None),
        grid=grid,
        in_specs=in_specs,
        out_specs=pl.BlockSpec((waves, block), lambda j: (0, j)),
        out_shape=jax.ShapeDtypeStruct((waves, total), jnp.bfloat16),
    )(*args)


def piece_tables(count, local_angles, axis):
    here = lax.axis_index(axis)
    blocks = count // local_angles
    wave_index = jnp.arange(count, dtype=jnp.int32) - count // 2
    scaling = 1.0 / math.sqrt(count)
    columns = []
    for shift in range(blocks):
        angle_index = ((here - shift) % blocks) * local_angles + jnp.arange(local_angles, dtype=jnp.int32)
        residues = wave_index[:, None] * angle_index[None, :] % count
        phases = 2.0 * math.pi * residues.astype(jnp.float32) / count
        columns.append((jnp.cos(phases) * scaling).astype(jnp.bfloat16))
        columns.append((jnp.sin(phases) * scaling).astype(jnp.bfloat16))
    return jnp.concatenate(columns, axis=1)


def dft_tables(count):
    wave_index = jnp.arange(count, dtype=jnp.int32) - count // 2
    angle_index = jnp.arange(count, dtype=jnp.int32)
    residues = wave_index[:, None] * angle_index[None, :] % count
    phases = 2.0 * math.pi * residues.astype(jnp.float32) / count
    scaling = 1.0 / math.sqrt(count)
    return (
        (jnp.cos(phases) * scaling).astype(jnp.bfloat16),
        (jnp.sin(phases) * scaling).astype(jnp.bfloat16),
    )


def combine_parts(cos_part, sin_part, half):
    real_part = cos_part[..., :half] + sin_part[..., half:]
    imag_part = cos_part[..., half:] - sin_part[..., :half]
    return jnp.concatenate([real_part, imag_part], axis=-1).astype(jnp.bfloat16)


def complex_blocks(product, half):
    upper_rows = product[..., :half, :]
    lower_rows = product[..., half:, :]
    pieces = []
    for offset in (0, 2 * half):
        pieces.append(
            upper_rows[..., offset : offset + half]
            + lower_rows[..., offset + half : offset + 2 * half]
        )
        pieces.append(
            upper_rows[..., offset + half : offset + 2 * half]
            - lower_rows[..., offset : offset + half]
        )
    return jnp.concatenate(pieces, axis=-1)


def local(direct_snapshots, adjoint_snapshots, quad_weight, mean_velocity, diffusivity):
    local_angles, axial_cells, radial_cells, columns = direct_snapshots.shape
    snap_count = columns // 2
    total_angles = local_angles * lax.axis_size("ka")
    table = piece_tables(total_angles, local_angles, "ka")
    first_wave = lax.axis_index("ka") * local_angles
    band_count = lax.axis_size("ka")
    band = radial_cells // band_count
    lanes = axial_cells * band * columns
    norm_factor = 1.0 / math.sqrt(axial_cells * lax.axis_size("gx") * radial_cells)
    band_weight = lax.dynamic_slice_in_dim(
        quad_weight * norm_factor, lax.axis_index("ka") * band, band, axis=1
    )
    lane_weight = jnp.broadcast_to(band_weight[:, :, None], (axial_cells, band, columns)).reshape(1, lanes)

    def transform_all(snapshots, weight=None):
        pieces = [piece.reshape(local_angles, lanes) for piece in exchange(snapshots, "ka", 2, separate=True)]
        modes = dft(table, pieces, weight)
        return modes.reshape(total_angles, axial_cells, band, columns)

    direct_pieces = exchange(transform_all(direct_snapshots), "ka", 0, separate=True)
    direct_modes = in_source_order(direct_pieces, "ka", 2)
    head = in_source_order([piece[:, :1] for piece in direct_pieces], "ka", 2)
    tail = in_source_order([piece[:, -1:] for piece in direct_pieces], "ka", 2)
    weighted = in_source_order(
        exchange(transform_all(adjoint_snapshots, lane_weight), "ka", 0, separate=True), "ka", 2
    )
    axial_count = lax.axis_size("gx")
    padded = jnp.concatenate(
        [
            lax.ppermute(tail, "gx", [(i, i + 1) for i in range(axial_count - 1)]),
            direct_modes,
            lax.ppermute(head, "gx", [(i + 1, i) for i in range(axial_count - 1)]),
        ],
        axis=1,
    )
    field_f32 = direct_modes.astype(jnp.float32)
    forward = padded[:, 2:].astype(jnp.float32)
    behind = padded[:, :-2].astype(jnp.float32)
    radial_pad = jnp.pad(field_f32, ((0, 0), (0, 0), (1, 1), (0, 0)))
    outward = radial_pad[:, :, 2:]
    inward = radial_pad[:, :, :-2]
    radius = 0.25 + (jnp.arange(radial_cells, dtype=jnp.float32) + 0.5) / radial_cells
    wavenumber = (
        first_wave + jnp.arange(local_angles, dtype=jnp.int32) - total_angles // 2
    ).astype(jnp.float32) / total_angles
    azimuthal = (wavenumber[:, None] / radius[None, :]) ** 2
    velocity = mean_velocity[None, :, :, None]
    diffusion = diffusivity[None, :, :, None]
    image = (
        -velocity * (forward - behind) * 0.5
        + diffusion
        * (
            forward
            + behind
            + outward
            + inward
            - 4.0 * field_f32
            - azimuthal[:, None, :, None] * field_f32
        )
    ).astype(jnp.bfloat16)
    right_side = jnp.concatenate([direct_modes, image], axis=-1)
    product = jnp.einsum(
        "kpa,kpb->kab",
        weighted.reshape(local_angles, -1, columns),
        right_side.reshape(local_angles, -1, 2 * columns),
        preferred_element_type=jnp.float32,
    )
    gram_terms = complex_blocks(product, snap_count).reshape(local_angles * snap_count, 2 * columns)
    row_count = gram_terms.shape[0] // lax.axis_size("gx")
    row_index = lax.axis_index("gx") * row_count + jnp.arange(row_count, dtype=jnp.int32)
    owner = row_index // snap_count
    selector = (owner[:, None] == jnp.arange(local_angles, dtype=jnp.int32)[None, :]).astype(
        jnp.float32
    )
    shares = gram_terms.astype(jnp.bfloat16).reshape(lax.axis_size("gx"), row_count, 2 * columns)
    own_rows = sum(piece.astype(jnp.float32) for piece in exchange(shares, "gx", 0, True, True))[0]
    row_energy = jnp.sum(own_rows[:, :columns] ** 2, axis=1)
    energy = jnp.sum(gather_small(jnp.sum(selector * row_energy[:, None], axis=0), "gx"), axis=0)
    mean_sq = energy / (2.0 * snap_count * snap_count)
    row_scale = jnp.sum(selector * lax.rsqrt(mean_sq + epsilon)[None, :], axis=1)
    hankel_gram = own_rows[:, :columns] * row_scale[:, None]
    reduced_operator = own_rows[:, columns:] * row_scale[:, None]
    hankel_norm = jnp.sqrt(mean_sq)
    return (hankel_gram, reduced_operator, hankel_norm)


def solution(mesh):
    placed = (
        P("ka", "gx", None, None),
        P("ka", "gx", None, None),
        P("gx", None),
        P("gx", None),
        P("gx", None),
    )
    return jax.shard_map(
        local,
        mesh=mesh,
        in_specs=placed,
        out_specs=(P(("ka", "gx"), None), P(("ka", "gx"), None), P("ka")),
        check_vma=False,
    )
```

```python
import functools
import math

import jax
import jax.numpy as jnp
from jax import lax
from jax.experimental import pallas as pl
from jax.experimental.pallas import tpu as pltpu
from jax.sharding import PartitionSpec as P

epsilon = 1e-06


def padded_2(cells, sides, width):
    for axis, dim in sides:
        count = lax.axis_size(axis)
        ends = count - 1
        head = lax.slice_in_dim(cells, 0, width, axis=dim)
        tail = lax.slice_in_dim(cells, cells.shape[dim] - width, cells.shape[dim], axis=dim)
        cells = jnp.concatenate(
            [
                lax.ppermute(tail, axis, [(i, (i + 1) % count) for i in range(ends)]),
                cells,
                lax.ppermute(head, axis, [((i + 1) % count, i) for i in range(ends)]),
            ],
            axis=dim,
        )
    return cells


def gather_small(values, axis):
    count = lax.axis_size(axis)
    copies = jnp.broadcast_to(values[None], (count,) + values.shape)
    return lax.all_to_all(copies, axis, split_axis=0, concat_axis=0, tiled=True)


def exchange(cells, axis, split_axis, far_first=False, separate=False):
    count = lax.axis_size(axis)
    here = lax.axis_index(axis)
    width = cells.shape[split_axis] // count
    shifts = list(range(count))
    if far_first:
        shifts = [0] + sorted(range(1, count), key=lambda shift: -min(shift, count - shift))
    pieces = [None] * count
    for shift in shifts:
        source = cells
        if separate:
            source, _ = lax.optimization_barrier((cells, jnp.int32(shift)))
        piece = lax.dynamic_slice_in_dim(source, ((here + shift) % count) * width, width, axis=split_axis)
        if shift:
            piece = lax.ppermute(piece, axis, [(j, (j + shift) % count) for j in range(count)])
        pieces[shift] = piece
    return pieces


def in_source_order(pieces, axis, concat_axis):
    count = len(pieces)
    here = lax.axis_index(axis)
    stacked = jnp.stack(pieces)
    ordered = [lax.dynamic_index_in_dim(stacked, (here - source) % count, 0, keepdims=False) for source in range(count)]
    return jnp.concatenate(ordered, axis=concat_axis)


def shifted_tables(count, local_angles, axis):
    here = lax.axis_index(axis)
    blocks = count // local_angles
    wave_index = jnp.arange(count, dtype=jnp.int32) - count // 2
    position = jnp.arange(count, dtype=jnp.int32)
    angle_index = ((here - position // local_angles) % blocks) * local_angles + position % local_angles
    residues = wave_index[:, None] * angle_index[None, :] % count
    phases = 2.0 * math.pi * residues.astype(jnp.float32) / count
    scaling = 1.0 / math.sqrt(count)
    return (
        (jnp.cos(phases) * scaling).astype(jnp.bfloat16),
        (jnp.sin(phases) * scaling).astype(jnp.bfloat16),
    )


def dft_kernel(*refs, count, weighted):
    table_ref = refs[0]
    piece_refs = refs[1:1 + count]
    rest = refs[1 + count:]
    out_ref = rest[-1]
    width = piece_refs[0].shape[1]
    lane = lax.broadcasted_iota(jnp.int32, (1, width), 1) % 128
    low = lane < 64
    packed = piece_refs[0].shape[0] % 16 == 0
    rows = []
    for piece_ref in piece_refs:
        x = piece_ref[...]
        if not packed:
            x = x.astype(jnp.float32)
        swapped = jnp.where(low, pltpu.roll(x, width - 64, 1), -pltpu.roll(x, 64, 1))
        rows.append(x)
        rows.append(swapped)
    stacked = jnp.concatenate(rows, axis=0).astype(jnp.bfloat16)
    acc = jnp.dot(table_ref[...], stacked, preferred_element_type=jnp.float32)
    modes = acc.astype(jnp.bfloat16)
    if weighted:
        modes = (modes.astype(jnp.float32) * rest[0][...]).astype(jnp.bfloat16)
    out_ref[...] = modes

def dft(table, pieces, weight=None):
    count = len(pieces)
    angles, total = pieces[0].shape
    waves = table.shape[0]
    block = math.gcd(total, 4096)
    grid = (total // block,)
    in_specs = [pl.BlockSpec((waves, table.shape[1]), lambda j: (0, 0))]
    in_specs += [pl.BlockSpec((angles, block), lambda j: (0, j)) for _ in pieces]
    args = [table, *pieces]
    if weight is not None:
        in_specs.append(pl.BlockSpec((1, block), lambda j: (0, j)))
        args.append(weight)
    return pl.pallas_call(
        functools.partial(dft_kernel, count=count, weighted=weight is not None),
        grid=grid,
        in_specs=in_specs,
        out_specs=pl.BlockSpec((waves, block), lambda j: (0, j)),
        out_shape=jax.ShapeDtypeStruct((waves, total), jnp.bfloat16),
    )(*args)


def piece_tables(count, local_angles, axis):
    here = lax.axis_index(axis)
    blocks = count // local_angles
    wave_index = jnp.arange(count, dtype=jnp.int32) - count // 2
    scaling = 1.0 / math.sqrt(count)
    columns = []
    for shift in range(blocks):
        angle_index = ((here - shift) % blocks) * local_angles + jnp.arange(local_angles, dtype=jnp.int32)
        residues = wave_index[:, None] * angle_index[None, :] % count
        phases = 2.0 * math.pi * residues.astype(jnp.float32) / count
        columns.append((jnp.cos(phases) * scaling).astype(jnp.bfloat16))
        columns.append((jnp.sin(phases) * scaling).astype(jnp.bfloat16))
    return jnp.concatenate(columns, axis=1)


def dft_tables(count):
    wave_index = jnp.arange(count, dtype=jnp.int32) - count // 2
    angle_index = jnp.arange(count, dtype=jnp.int32)
    residues = wave_index[:, None] * angle_index[None, :] % count
    phases = 2.0 * math.pi * residues.astype(jnp.float32) / count
    scaling = 1.0 / math.sqrt(count)
    return (
        (jnp.cos(phases) * scaling).astype(jnp.bfloat16),
        (jnp.sin(phases) * scaling).astype(jnp.bfloat16),
    )


def combine_parts(cos_part, sin_part, half):
    real_part = cos_part[..., :half] + sin_part[..., half:]
    imag_part = cos_part[..., half:] - sin_part[..., :half]
    return jnp.concatenate([real_part, imag_part], axis=-1).astype(jnp.bfloat16)


def complex_blocks(product, half):
    upper_rows = product[..., :half, :]
    lower_rows = product[..., half:, :]
    pieces = []
    for offset in (0, 2 * half):
        pieces.append(
            upper_rows[..., offset : offset + half]
            + lower_rows[..., offset + half : offset + 2 * half]
        )
        pieces.append(
            upper_rows[..., offset + half : offset + 2 * half]
            - lower_rows[..., offset : offset + half]
        )
    return jnp.concatenate(pieces, axis=-1)


def local(direct_snapshots, adjoint_snapshots, quad_weight, mean_velocity, diffusivity):
    local_angles, axial_cells, radial_cells, columns = direct_snapshots.shape
    snap_count = columns // 2
    total_angles = local_angles * lax.axis_size("ka")
    table = piece_tables(total_angles, local_angles, "ka")
    first_wave = lax.axis_index("ka") * local_angles
    band_count = lax.axis_size("ka")
    band = radial_cells // band_count
    lanes = axial_cells * band * columns
    norm_factor = 1.0 / math.sqrt(axial_cells * lax.axis_size("gx") * radial_cells)
    band_weight = lax.dynamic_slice_in_dim(
        quad_weight * norm_factor, lax.axis_index("ka") * band, band, axis=1
    )
    lane_weight = jnp.broadcast_to(band_weight[:, :, None], (axial_cells, band, columns)).reshape(1, lanes)

    def transform_all(snapshots, weight=None):
        pieces = [piece.reshape(local_angles, lanes) for piece in exchange(snapshots, "ka", 2, True, True)]
        modes = dft(table, pieces, weight)
        return modes.reshape(total_angles, axial_cells, band, columns)

    direct_modes = in_source_order(exchange(transform_all(direct_snapshots), "ka", 0, separate=True), "ka", 2)
    weighted = in_source_order(
        exchange(transform_all(adjoint_snapshots, lane_weight), "ka", 0, separate=True), "ka", 2
    )
    padded = padded_2(direct_modes, (("gx", 1),), 1)
    field_f32 = direct_modes.astype(jnp.float32)
    forward = padded[:, 2:].astype(jnp.float32)
    behind = padded[:, :-2].astype(jnp.float32)
    radial_pad = jnp.pad(field_f32, ((0, 0), (0, 0), (1, 1), (0, 0)))
    outward = radial_pad[:, :, 2:]
    inward = radial_pad[:, :, :-2]
    radius = 0.25 + (jnp.arange(radial_cells, dtype=jnp.float32) + 0.5) / radial_cells
    wavenumber = (
        first_wave + jnp.arange(local_angles, dtype=jnp.int32) - total_angles // 2
    ).astype(jnp.float32) / total_angles
    azimuthal = (wavenumber[:, None] / radius[None, :]) ** 2
    velocity = mean_velocity[None, :, :, None]
    diffusion = diffusivity[None, :, :, None]
    image = (
        -velocity * (forward - behind) * 0.5
        + diffusion
        * (
            forward
            + behind
            + outward
            + inward
            - 4.0 * field_f32
            - azimuthal[:, None, :, None] * field_f32
        )
    ).astype(jnp.bfloat16)
    right_side = jnp.concatenate([direct_modes, image], axis=-1)
    product = jnp.einsum(
        "kpa,kpb->kab",
        weighted.reshape(local_angles, -1, columns),
        right_side.reshape(local_angles, -1, 2 * columns),
        preferred_element_type=jnp.float32,
    )
    gram_terms = complex_blocks(product, snap_count).reshape(local_angles * snap_count, 2 * columns)
    row_count = gram_terms.shape[0] // lax.axis_size("gx")
    row_index = lax.axis_index("gx") * row_count + jnp.arange(row_count, dtype=jnp.int32)
    owner = row_index // snap_count
    selector = (owner[:, None] == jnp.arange(local_angles, dtype=jnp.int32)[None, :]).astype(
        jnp.float32
    )
    shares = gram_terms.astype(jnp.bfloat16).reshape(lax.axis_size("gx"), row_count, 2 * columns)
    own_rows = sum(piece.astype(jnp.float32) for piece in exchange(shares, "gx", 0, True, True))[0]
    row_energy = jnp.sum(own_rows[:, :columns] ** 2, axis=1)
    energy = jnp.sum(gather_small(jnp.sum(selector * row_energy[:, None], axis=0), "gx"), axis=0)
    mean_sq = energy / (2.0 * snap_count * snap_count)
    row_scale = jnp.sum(selector * lax.rsqrt(mean_sq + epsilon)[None, :], axis=1)
    hankel_gram = own_rows[:, :columns] * row_scale[:, None]
    reduced_operator = own_rows[:, columns:] * row_scale[:, None]
    hankel_norm = jnp.sqrt(mean_sq)
    return (hankel_gram, reduced_operator, hankel_norm)


def solution(mesh):
    placed = (
        P("ka", "gx", None, None),
        P("ka", "gx", None, None),
        P("gx", None),
        P("gx", None),
        P("gx", None),
    )
    return jax.shard_map(
        local,
        mesh=mesh,
        in_specs=placed,
        out_specs=(P(("ka", "gx"), None), P(("ka", "gx"), None), P("ka")),
        check_vma=False,
    )
```

```python
import functools
import math

import jax
import jax.numpy as jnp
from jax import lax
from jax.experimental import pallas as pl
from jax.experimental.pallas import tpu as pltpu
from jax.sharding import PartitionSpec as P

epsilon = 1e-06


def padded_2(cells, sides, width):
    for axis, dim in sides:
        count = lax.axis_size(axis)
        ends = count - 1
        head = lax.slice_in_dim(cells, 0, width, axis=dim)
        tail = lax.slice_in_dim(cells, cells.shape[dim] - width, cells.shape[dim], axis=dim)
        cells = jnp.concatenate(
            [
                lax.ppermute(tail, axis, [(i, (i + 1) % count) for i in range(ends)]),
                cells,
                lax.ppermute(head, axis, [((i + 1) % count, i) for i in range(ends)]),
            ],
            axis=dim,
        )
    return cells


def gather_small(values, axis):
    count = lax.axis_size(axis)
    copies = jnp.broadcast_to(values[None], (count,) + values.shape)
    return lax.all_to_all(copies, axis, split_axis=0, concat_axis=0, tiled=True)


def exchange(cells, axis, split_axis, far_first=False, separate=False):
    count = lax.axis_size(axis)
    here = lax.axis_index(axis)
    width = cells.shape[split_axis] // count
    shifts = list(range(count))
    if far_first:
        shifts = [0] + sorted(range(1, count), key=lambda shift: -min(shift, count - shift))
    pieces = []
    for shift in shifts:
        source = cells
        if separate:
            source, _ = lax.optimization_barrier((cells, jnp.int32(shift)))
        piece = lax.dynamic_slice_in_dim(source, ((here + shift) % count) * width, width, axis=split_axis)
        if shift:
            piece = lax.ppermute(piece, axis, [(j, (j + shift) % count) for j in range(count)])
        pieces.append(piece)
    return pieces


def in_source_order(pieces, axis, concat_axis):
    count = len(pieces)
    here = lax.axis_index(axis)
    stacked = jnp.stack(pieces)
    ordered = [lax.dynamic_index_in_dim(stacked, (here - source) % count, 0, keepdims=False) for source in range(count)]
    return jnp.concatenate(ordered, axis=concat_axis)


def shifted_tables(count, local_angles, axis):
    here = lax.axis_index(axis)
    blocks = count // local_angles
    wave_index = jnp.arange(count, dtype=jnp.int32) - count // 2
    position = jnp.arange(count, dtype=jnp.int32)
    angle_index = ((here - position // local_angles) % blocks) * local_angles + position % local_angles
    residues = wave_index[:, None] * angle_index[None, :] % count
    phases = 2.0 * math.pi * residues.astype(jnp.float32) / count
    scaling = 1.0 / math.sqrt(count)
    return (
        (jnp.cos(phases) * scaling).astype(jnp.bfloat16),
        (jnp.sin(phases) * scaling).astype(jnp.bfloat16),
    )


def dft_kernel(*refs, count, weighted):
    table_ref = refs[0]
    piece_refs = refs[1:1 + count]
    rest = refs[1 + count:]
    out_ref = rest[-1]
    width = piece_refs[0].shape[1]
    lane = lax.broadcasted_iota(jnp.int32, (1, width), 1) % 128
    low = lane < 64
    packed = piece_refs[0].shape[0] % 16 == 0
    rows = []
    for piece_ref in piece_refs:
        x = piece_ref[...]
        if not packed:
            x = x.astype(jnp.float32)
        swapped = jnp.where(low, pltpu.roll(x, width - 64, 1), -pltpu.roll(x, 64, 1))
        rows.append(x)
        rows.append(swapped)
    stacked = jnp.concatenate(rows, axis=0).astype(jnp.bfloat16)
    acc = jnp.dot(table_ref[...], stacked, preferred_element_type=jnp.float32)
    modes = acc.astype(jnp.bfloat16)
    if weighted:
        modes = (modes.astype(jnp.float32) * rest[0][...]).astype(jnp.bfloat16)
    out_ref[...] = modes

def dft(table, pieces, weight=None):
    count = len(pieces)
    angles, total = pieces[0].shape
    waves = table.shape[0]
    block = math.gcd(total, 4096)
    grid = (total // block,)
    in_specs = [pl.BlockSpec((waves, table.shape[1]), lambda j: (0, 0))]
    in_specs += [pl.BlockSpec((angles, block), lambda j: (0, j)) for _ in pieces]
    args = [table, *pieces]
    if weight is not None:
        in_specs.append(pl.BlockSpec((1, block), lambda j: (0, j)))
        args.append(weight)
    return pl.pallas_call(
        functools.partial(dft_kernel, count=count, weighted=weight is not None),
        grid=grid,
        in_specs=in_specs,
        out_specs=pl.BlockSpec((waves, block), lambda j: (0, j)),
        out_shape=jax.ShapeDtypeStruct((waves, total), jnp.bfloat16),
    )(*args)


def piece_tables(count, local_angles, axis):
    here = lax.axis_index(axis)
    blocks = count // local_angles
    wave_index = jnp.arange(count, dtype=jnp.int32) - count // 2
    scaling = 1.0 / math.sqrt(count)
    columns = []
    for shift in range(blocks):
        angle_index = ((here - shift) % blocks) * local_angles + jnp.arange(local_angles, dtype=jnp.int32)
        residues = wave_index[:, None] * angle_index[None, :] % count
        phases = 2.0 * math.pi * residues.astype(jnp.float32) / count
        columns.append((jnp.cos(phases) * scaling).astype(jnp.bfloat16))
        columns.append((jnp.sin(phases) * scaling).astype(jnp.bfloat16))
    return jnp.concatenate(columns, axis=1)


def dft_tables(count):
    wave_index = jnp.arange(count, dtype=jnp.int32) - count // 2
    angle_index = jnp.arange(count, dtype=jnp.int32)
    residues = wave_index[:, None] * angle_index[None, :] % count
    phases = 2.0 * math.pi * residues.astype(jnp.float32) / count
    scaling = 1.0 / math.sqrt(count)
    return (
        (jnp.cos(phases) * scaling).astype(jnp.bfloat16),
        (jnp.sin(phases) * scaling).astype(jnp.bfloat16),
    )


def combine_parts(cos_part, sin_part, half):
    real_part = cos_part[..., :half] + sin_part[..., half:]
    imag_part = cos_part[..., half:] - sin_part[..., :half]
    return jnp.concatenate([real_part, imag_part], axis=-1).astype(jnp.bfloat16)


def complex_blocks(product, half):
    upper_rows = product[..., :half, :]
    lower_rows = product[..., half:, :]
    pieces = []
    for offset in (0, 2 * half):
        pieces.append(
            upper_rows[..., offset : offset + half]
            + lower_rows[..., offset + half : offset + 2 * half]
        )
        pieces.append(
            upper_rows[..., offset + half : offset + 2 * half]
            - lower_rows[..., offset : offset + half]
        )
    return jnp.concatenate(pieces, axis=-1)


def local(direct_snapshots, adjoint_snapshots, quad_weight, mean_velocity, diffusivity):
    local_angles, axial_cells, radial_cells, columns = direct_snapshots.shape
    snap_count = columns // 2
    total_angles = local_angles * lax.axis_size("ka")
    table = piece_tables(total_angles, local_angles, "ka")
    first_wave = lax.axis_index("ka") * local_angles
    band_count = lax.axis_size("ka")
    band = radial_cells // band_count
    lanes = axial_cells * band * columns
    norm_factor = 1.0 / math.sqrt(axial_cells * lax.axis_size("gx") * radial_cells)
    band_weight = lax.dynamic_slice_in_dim(
        quad_weight * norm_factor, lax.axis_index("ka") * band, band, axis=1
    )
    lane_weight = jnp.broadcast_to(band_weight[:, :, None], (axial_cells, band, columns)).reshape(1, lanes)

    def transform_all(snapshots, weight=None):
        pieces = [piece.reshape(local_angles, lanes) for piece in exchange(snapshots, "ka", 2, separate=True)]
        modes = dft(table, pieces, weight)
        return modes.reshape(total_angles, axial_cells, band, columns)

    direct_modes = in_source_order(exchange(transform_all(direct_snapshots), "ka", 0, separate=True), "ka", 2)
    weighted = in_source_order(
        exchange(transform_all(adjoint_snapshots, lane_weight), "ka", 0, separate=True), "ka", 2
    )
    padded = padded_2(direct_modes, (("gx", 1),), 1)
    field_f32 = direct_modes.astype(jnp.float32)
    forward = padded[:, 2:].astype(jnp.float32)
    behind = padded[:, :-2].astype(jnp.float32)
    radial_pad = jnp.pad(field_f32, ((0, 0), (0, 0), (1, 1), (0, 0)))
    outward = radial_pad[:, :, 2:]
    inward = radial_pad[:, :, :-2]
    radius = 0.25 + (jnp.arange(radial_cells, dtype=jnp.float32) + 0.5) / radial_cells
    wavenumber = (
        first_wave + jnp.arange(local_angles, dtype=jnp.int32) - total_angles // 2
    ).astype(jnp.float32) / total_angles
    azimuthal = (wavenumber[:, None] / radius[None, :]) ** 2
    velocity = mean_velocity[None, :, :, None]
    diffusion = diffusivity[None, :, :, None]
    image = (
        -velocity * (forward - behind) * 0.5
        + diffusion
        * (
            forward
            + behind
            + outward
            + inward
            - 4.0 * field_f32
            - azimuthal[:, None, :, None] * field_f32
        )
    ).astype(jnp.bfloat16)
    right_side = jnp.concatenate([direct_modes, image], axis=-1)
    product = jnp.einsum(
        "kpa,kpb->kab",
        weighted.reshape(local_angles, -1, columns),
        right_side.reshape(local_angles, -1, 2 * columns),
        preferred_element_type=jnp.float32,
    )
    gram_terms = complex_blocks(product, snap_count).reshape(local_angles * snap_count, 2 * columns)
    row_count = gram_terms.shape[0] // lax.axis_size("gx")
    row_index = lax.axis_index("gx") * row_count + jnp.arange(row_count, dtype=jnp.int32)
    owner = row_index // snap_count
    selector = (owner[:, None] == jnp.arange(local_angles, dtype=jnp.int32)[None, :]).astype(
        jnp.float32
    )
    shares = gram_terms.astype(jnp.bfloat16).reshape(lax.axis_size("gx"), row_count, 2 * columns)
    own_rows = sum(piece.astype(jnp.float32) for piece in exchange(shares, "gx", 0, True, True))[0]
    row_energy = jnp.sum(own_rows[:, :columns] ** 2, axis=1)
    partial_energy = jnp.sum(selector * row_energy[:, None], axis=0)
    energy = jnp.sum(gather_small(partial_energy, "gx"), axis=0)
    mean_sq = energy / (2.0 * snap_count * snap_count)
    own_sq = partial_energy / (2.0 * snap_count * snap_count) if row_count % snap_count == 0 else mean_sq
    row_scale = jnp.sum(selector * lax.rsqrt(own_sq + epsilon)[None, :], axis=1)
    hankel_gram = own_rows[:, :columns] * row_scale[:, None]
    reduced_operator = own_rows[:, columns:] * row_scale[:, None]
    hankel_norm = jnp.sqrt(mean_sq)
    return (hankel_gram, reduced_operator, hankel_norm)


def solution(mesh):
    placed = (
        P("ka", "gx", None, None),
        P("ka", "gx", None, None),
        P("gx", None),
        P("gx", None),
        P("gx", None),
    )
    return jax.shard_map(
        local,
        mesh=mesh,
        in_specs=placed,
        out_specs=(P(("ka", "gx"), None), P(("ka", "gx"), None), P("ka")),
        check_vma=False,
    )
```

```python
import functools
import math

import jax
import jax.numpy as jnp
from jax import lax
from jax.experimental import pallas as pl
from jax.experimental.pallas import tpu as pltpu
from jax.sharding import PartitionSpec as P

epsilon = 1e-06


def padded_2(cells, sides, width):
    for axis, dim in sides:
        count = lax.axis_size(axis)
        ends = count - 1
        head = lax.slice_in_dim(cells, 0, width, axis=dim)
        tail = lax.slice_in_dim(cells, cells.shape[dim] - width, cells.shape[dim], axis=dim)
        cells = jnp.concatenate(
            [
                lax.ppermute(tail, axis, [(i, (i + 1) % count) for i in range(ends)]),
                cells,
                lax.ppermute(head, axis, [((i + 1) % count, i) for i in range(ends)]),
            ],
            axis=dim,
        )
    return cells


def gather_small(values, axis):
    count = lax.axis_size(axis)
    copies = jnp.broadcast_to(values[None], (count,) + values.shape)
    return lax.all_to_all(copies, axis, split_axis=0, concat_axis=0, tiled=True)


def exchange(cells, axis, split_axis, far_first=False, separate=False):
    count = lax.axis_size(axis)
    here = lax.axis_index(axis)
    width = cells.shape[split_axis] // count
    shifts = list(range(count))
    if far_first:
        shifts = [0] + sorted(range(1, count), key=lambda shift: -min(shift, count - shift))
    pieces = []
    for shift in shifts:
        source = cells
        if separate:
            source, _ = lax.optimization_barrier((cells, jnp.int32(shift)))
        piece = lax.dynamic_slice_in_dim(source, ((here + shift) % count) * width, width, axis=split_axis)
        if shift:
            piece = lax.ppermute(piece, axis, [(j, (j + shift) % count) for j in range(count)])
        pieces.append(piece)
    return pieces


def in_source_order(pieces, axis, concat_axis):
    count = len(pieces)
    here = lax.axis_index(axis)
    stacked = jnp.stack(pieces)
    ordered = [lax.dynamic_index_in_dim(stacked, (here - source) % count, 0, keepdims=False) for source in range(count)]
    return jnp.concatenate(ordered, axis=concat_axis)


def shifted_tables(count, local_angles, axis):
    here = lax.axis_index(axis)
    blocks = count // local_angles
    wave_index = jnp.arange(count, dtype=jnp.int32) - count // 2
    position = jnp.arange(count, dtype=jnp.int32)
    angle_index = ((here - position // local_angles) % blocks) * local_angles + position % local_angles
    residues = wave_index[:, None] * angle_index[None, :] % count
    phases = 2.0 * math.pi * residues.astype(jnp.float32) / count
    scaling = 1.0 / math.sqrt(count)
    return (
        (jnp.cos(phases) * scaling).astype(jnp.bfloat16),
        (jnp.sin(phases) * scaling).astype(jnp.bfloat16),
    )


def dft_kernel(*refs, count, weighted):
    table_ref = refs[0]
    piece_refs = refs[1:1 + count]
    rest = refs[1 + count:]
    out_ref = rest[-1]
    width = piece_refs[0].shape[1]
    lane = lax.broadcasted_iota(jnp.int32, (1, width), 1) % 128
    low = lane < 64
    packed = piece_refs[0].shape[0] % 16 == 0
    rows = []
    for piece_ref in piece_refs:
        x = piece_ref[...]
        if not packed:
            x = x.astype(jnp.float32)
        swapped = jnp.where(low, pltpu.roll(x, width - 64, 1), -pltpu.roll(x, 64, 1))
        rows.append(x)
        rows.append(swapped)
    stacked = jnp.concatenate(rows, axis=0).astype(jnp.bfloat16)
    acc = jnp.dot(table_ref[...], stacked, preferred_element_type=jnp.float32)
    modes = acc.astype(jnp.bfloat16)
    if weighted:
        modes = (modes.astype(jnp.float32) * rest[0][...]).astype(jnp.bfloat16)
    out_ref[...] = modes

def dft(table, pieces, weight=None):
    count = len(pieces)
    angles, total = pieces[0].shape
    waves = table.shape[0]
    block = math.gcd(total, 4096)
    grid = (total // block,)
    in_specs = [pl.BlockSpec((waves, table.shape[1]), lambda j: (0, 0))]
    in_specs += [pl.BlockSpec((angles, block), lambda j: (0, j)) for _ in pieces]
    args = [table, *pieces]
    if weight is not None:
        in_specs.append(pl.BlockSpec((1, block), lambda j: (0, j)))
        args.append(weight)
    return pl.pallas_call(
        functools.partial(dft_kernel, count=count, weighted=weight is not None),
        grid=grid,
        in_specs=in_specs,
        out_specs=pl.BlockSpec((waves, block), lambda j: (0, j)),
        out_shape=jax.ShapeDtypeStruct((waves, total), jnp.bfloat16),
        cost_estimate=pl.CostEstimate(
            flops=2 * waves * table.shape[1] * total,
            transcendentals=0,
            bytes_accessed=2 * (count * angles * total + waves * total + table.size),
        ),
    )(*args)


def piece_tables(count, local_angles, axis):
    here = lax.axis_index(axis)
    blocks = count // local_angles
    wave_index = jnp.arange(count, dtype=jnp.int32) - count // 2
    scaling = 1.0 / math.sqrt(count)
    columns = []
    for shift in range(blocks):
        angle_index = ((here - shift) % blocks) * local_angles + jnp.arange(local_angles, dtype=jnp.int32)
        residues = wave_index[:, None] * angle_index[None, :] % count
        phases = 2.0 * math.pi * residues.astype(jnp.float32) / count
        columns.append((jnp.cos(phases) * scaling).astype(jnp.bfloat16))
        columns.append((jnp.sin(phases) * scaling).astype(jnp.bfloat16))
    return jnp.concatenate(columns, axis=1)


def dft_tables(count):
    wave_index = jnp.arange(count, dtype=jnp.int32) - count // 2
    angle_index = jnp.arange(count, dtype=jnp.int32)
    residues = wave_index[:, None] * angle_index[None, :] % count
    phases = 2.0 * math.pi * residues.astype(jnp.float32) / count
    scaling = 1.0 / math.sqrt(count)
    return (
        (jnp.cos(phases) * scaling).astype(jnp.bfloat16),
        (jnp.sin(phases) * scaling).astype(jnp.bfloat16),
    )


def combine_parts(cos_part, sin_part, half):
    real_part = cos_part[..., :half] + sin_part[..., half:]
    imag_part = cos_part[..., half:] - sin_part[..., :half]
    return jnp.concatenate([real_part, imag_part], axis=-1).astype(jnp.bfloat16)


def complex_blocks(product, half):
    upper_rows = product[..., :half, :]
    lower_rows = product[..., half:, :]
    pieces = []
    for offset in (0, 2 * half):
        pieces.append(
            upper_rows[..., offset : offset + half]
            + lower_rows[..., offset + half : offset + 2 * half]
        )
        pieces.append(
            upper_rows[..., offset + half : offset + 2 * half]
            - lower_rows[..., offset : offset + half]
        )
    return jnp.concatenate(pieces, axis=-1)


def local(direct_snapshots, adjoint_snapshots, quad_weight, mean_velocity, diffusivity):
    local_angles, axial_cells, radial_cells, columns = direct_snapshots.shape
    snap_count = columns // 2
    total_angles = local_angles * lax.axis_size("ka")
    table = piece_tables(total_angles, local_angles, "ka")
    first_wave = lax.axis_index("ka") * local_angles
    band_count = lax.axis_size("ka")
    band = radial_cells // band_count
    lanes = axial_cells * band * columns
    norm_factor = 1.0 / math.sqrt(axial_cells * lax.axis_size("gx") * radial_cells)
    band_weight = lax.dynamic_slice_in_dim(
        quad_weight * norm_factor, lax.axis_index("ka") * band, band, axis=1
    )
    lane_weight = jnp.broadcast_to(band_weight[:, :, None], (axial_cells, band, columns)).reshape(1, lanes)

    def transform_all(snapshots, weight=None):
        pieces = [piece.reshape(local_angles, lanes) for piece in exchange(snapshots, "ka", 2, separate=True)]
        modes = dft(table, pieces, weight)
        return modes.reshape(total_angles, axial_cells, band, columns)

    direct_modes = in_source_order(exchange(transform_all(direct_snapshots), "ka", 0, separate=True), "ka", 2)
    weighted = in_source_order(
        exchange(transform_all(adjoint_snapshots, lane_weight), "ka", 0, separate=True), "ka", 2
    )
    padded = padded_2(direct_modes, (("gx", 1),), 1)
    field_f32 = direct_modes.astype(jnp.float32)
    forward = padded[:, 2:].astype(jnp.float32)
    behind = padded[:, :-2].astype(jnp.float32)
    radial_pad = jnp.pad(field_f32, ((0, 0), (0, 0), (1, 1), (0, 0)))
    outward = radial_pad[:, :, 2:]
    inward = radial_pad[:, :, :-2]
    radius = 0.25 + (jnp.arange(radial_cells, dtype=jnp.float32) + 0.5) / radial_cells
    wavenumber = (
        first_wave + jnp.arange(local_angles, dtype=jnp.int32) - total_angles // 2
    ).astype(jnp.float32) / total_angles
    azimuthal = (wavenumber[:, None] / radius[None, :]) ** 2
    velocity = mean_velocity[None, :, :, None]
    diffusion = diffusivity[None, :, :, None]
    image = (
        -velocity * (forward - behind) * 0.5
        + diffusion
        * (
            forward
            + behind
            + outward
            + inward
            - 4.0 * field_f32
            - azimuthal[:, None, :, None] * field_f32
        )
    ).astype(jnp.bfloat16)
    right_side = jnp.concatenate([direct_modes, image], axis=-1)
    product = jnp.einsum(
        "kpa,kpb->kab",
        weighted.reshape(local_angles, -1, columns),
        right_side.reshape(local_angles, -1, 2 * columns),
        preferred_element_type=jnp.float32,
    )
    gram_terms = complex_blocks(product, snap_count).reshape(local_angles * snap_count, 2 * columns)
    row_count = gram_terms.shape[0] // lax.axis_size("gx")
    row_index = lax.axis_index("gx") * row_count + jnp.arange(row_count, dtype=jnp.int32)
    owner = row_index // snap_count
    selector = (owner[:, None] == jnp.arange(local_angles, dtype=jnp.int32)[None, :]).astype(
        jnp.float32
    )
    shares = gram_terms.astype(jnp.bfloat16).reshape(lax.axis_size("gx"), row_count, 2 * columns)
    own_rows = sum(piece.astype(jnp.float32) for piece in exchange(shares, "gx", 0, True, True))[0]
    row_energy = jnp.sum(own_rows[:, :columns] ** 2, axis=1)
    energy = jnp.sum(gather_small(jnp.sum(selector * row_energy[:, None], axis=0), "gx"), axis=0)
    mean_sq = energy / (2.0 * snap_count * snap_count)
    row_scale = jnp.sum(selector * lax.rsqrt(mean_sq + epsilon)[None, :], axis=1)
    hankel_gram = own_rows[:, :columns] * row_scale[:, None]
    reduced_operator = own_rows[:, columns:] * row_scale[:, None]
    hankel_norm = jnp.sqrt(mean_sq)
    return (hankel_gram, reduced_operator, hankel_norm)


def solution(mesh):
    placed = (
        P("ka", "gx", None, None),
        P("ka", "gx", None, None),
        P("gx", None),
        P("gx", None),
        P("gx", None),
    )
    return jax.shard_map(
        local,
        mesh=mesh,
        in_specs=placed,
        out_specs=(P(("ka", "gx"), None), P(("ka", "gx"), None), P("ka")),
        check_vma=False,
    )
```

```python
import functools
import math

import jax
import jax.numpy as jnp
from jax import lax
from jax.experimental import pallas as pl
from jax.experimental.pallas import tpu as pltpu
from jax.sharding import PartitionSpec as P

epsilon = 1e-06


def padded_2(cells, sides, width):
    for axis, dim in sides:
        count = lax.axis_size(axis)
        ends = count - 1
        head = lax.slice_in_dim(cells, 0, width, axis=dim)
        tail = lax.slice_in_dim(cells, cells.shape[dim] - width, cells.shape[dim], axis=dim)
        cells = jnp.concatenate(
            [
                lax.ppermute(tail, axis, [(i, (i + 1) % count) for i in range(ends)]),
                cells,
                lax.ppermute(head, axis, [((i + 1) % count, i) for i in range(ends)]),
            ],
            axis=dim,
        )
    return cells


def gather_small(values, axis):
    count = lax.axis_size(axis)
    copies = jnp.broadcast_to(values[None], (count,) + values.shape)
    return lax.all_to_all(copies, axis, split_axis=0, concat_axis=0, tiled=True)


def exchange(cells, axis, split_axis, far_first=False, separate=False):
    count = lax.axis_size(axis)
    here = lax.axis_index(axis)
    width = cells.shape[split_axis] // count
    shifts = list(range(count))
    if far_first:
        shifts = [0] + sorted(range(1, count), key=lambda shift: -min(shift, count - shift))
    pieces = []
    for shift in shifts:
        source = cells
        if separate:
            source, _ = lax.optimization_barrier((cells, jnp.int32(shift)))
        piece = lax.dynamic_slice_in_dim(source, ((here + shift) % count) * width, width, axis=split_axis)
        if shift:
            piece = lax.ppermute(piece, axis, [(j, (j + shift) % count) for j in range(count)])
        pieces.append(piece)
    return pieces


def in_source_order(pieces, axis, concat_axis):
    count = len(pieces)
    here = lax.axis_index(axis)
    stacked = jnp.stack(pieces)
    ordered = [lax.dynamic_index_in_dim(stacked, (here - source) % count, 0, keepdims=False) for source in range(count)]
    return jnp.concatenate(ordered, axis=concat_axis)


def shifted_tables(count, local_angles, axis):
    here = lax.axis_index(axis)
    blocks = count // local_angles
    wave_index = jnp.arange(count, dtype=jnp.int32) - count // 2
    position = jnp.arange(count, dtype=jnp.int32)
    angle_index = ((here - position // local_angles) % blocks) * local_angles + position % local_angles
    residues = wave_index[:, None] * angle_index[None, :] % count
    phases = 2.0 * math.pi * residues.astype(jnp.float32) / count
    scaling = 1.0 / math.sqrt(count)
    return (
        (jnp.cos(phases) * scaling).astype(jnp.bfloat16),
        (jnp.sin(phases) * scaling).astype(jnp.bfloat16),
    )


def dft_kernel(*refs, count, weighted):
    table_ref = refs[0]
    piece_refs = refs[1:1 + count]
    rest = refs[1 + count:]
    out_ref = rest[-1]
    width = piece_refs[0].shape[1]
    lane = lax.broadcasted_iota(jnp.int32, (1, width), 1) % 128
    low = lane < 64
    packed = piece_refs[0].shape[0] % 16 == 0
    rows = []
    for piece_ref in piece_refs:
        x = piece_ref[...]
        if not packed:
            x = x.astype(jnp.float32)
        swapped = jnp.where(low, pltpu.roll(x, width - 64, 1), -pltpu.roll(x, 64, 1))
        rows.append(x)
        rows.append(swapped)
    stacked = jnp.concatenate(rows, axis=0).astype(jnp.bfloat16)
    acc = jnp.dot(table_ref[...], stacked, preferred_element_type=jnp.float32)
    modes = acc.astype(jnp.bfloat16)
    if weighted:
        modes = (modes.astype(jnp.float32) * rest[0][...]).astype(jnp.bfloat16)
    out_ref[...] = modes

def dft(table, pieces, weight=None):
    count = len(pieces)
    angles, total = pieces[0].shape
    waves = table.shape[0]
    block = math.gcd(total, 4096)
    grid = (total // block,)
    in_specs = [pl.BlockSpec((waves, table.shape[1]), lambda j: (0, 0))]
    in_specs += [pl.BlockSpec((angles, block), lambda j: (0, j)) for _ in pieces]
    args = [table, *pieces]
    if weight is not None:
        in_specs.append(pl.BlockSpec((1, block), lambda j: (0, j)))
        args.append(weight)
    return pl.pallas_call(
        functools.partial(dft_kernel, count=count, weighted=weight is not None),
        grid=grid,
        in_specs=in_specs,
        out_specs=pl.BlockSpec((waves, block), lambda j: (0, j)),
        out_shape=jax.ShapeDtypeStruct((waves, total), jnp.bfloat16),
    )(*args)


def piece_tables(count, local_angles, axis):
    here = lax.axis_index(axis)
    blocks = count // local_angles
    wave_index = jnp.arange(count, dtype=jnp.int32) - count // 2
    scaling = 1.0 / math.sqrt(count)
    columns = []
    for shift in range(blocks):
        angle_index = ((here - shift) % blocks) * local_angles + jnp.arange(local_angles, dtype=jnp.int32)
        residues = wave_index[:, None] * angle_index[None, :] % count
        phases = 2.0 * math.pi * residues.astype(jnp.float32) / count
        columns.append((jnp.cos(phases) * scaling).astype(jnp.bfloat16))
        columns.append((jnp.sin(phases) * scaling).astype(jnp.bfloat16))
    return jnp.concatenate(columns, axis=1)


def dft_tables(count):
    wave_index = jnp.arange(count, dtype=jnp.int32) - count // 2
    angle_index = jnp.arange(count, dtype=jnp.int32)
    residues = wave_index[:, None] * angle_index[None, :] % count
    phases = 2.0 * math.pi * residues.astype(jnp.float32) / count
    scaling = 1.0 / math.sqrt(count)
    return (
        (jnp.cos(phases) * scaling).astype(jnp.bfloat16),
        (jnp.sin(phases) * scaling).astype(jnp.bfloat16),
    )


def combine_parts(cos_part, sin_part, half):
    real_part = cos_part[..., :half] + sin_part[..., half:]
    imag_part = cos_part[..., half:] - sin_part[..., :half]
    return jnp.concatenate([real_part, imag_part], axis=-1).astype(jnp.bfloat16)


def complex_blocks(product, half):
    upper_rows = product[..., :half, :]
    lower_rows = product[..., half:, :]
    pieces = []
    for offset in (0, 2 * half):
        pieces.append(
            upper_rows[..., offset : offset + half]
            + lower_rows[..., offset + half : offset + 2 * half]
        )
        pieces.append(
            upper_rows[..., offset + half : offset + 2 * half]
            - lower_rows[..., offset : offset + half]
        )
    return jnp.concatenate(pieces, axis=-1)


def local(direct_snapshots, adjoint_snapshots, quad_weight, mean_velocity, diffusivity):
    local_angles, axial_cells, radial_cells, columns = direct_snapshots.shape
    snap_count = columns // 2
    total_angles = local_angles * lax.axis_size("ka")
    table = piece_tables(total_angles, local_angles, "ka")
    first_wave = lax.axis_index("ka") * local_angles
    band_count = lax.axis_size("ka")
    band = radial_cells // band_count
    lanes = axial_cells * band * columns
    norm_factor = 1.0 / math.sqrt(axial_cells * lax.axis_size("gx") * radial_cells)
    band_weight = lax.dynamic_slice_in_dim(
        quad_weight * norm_factor, lax.axis_index("ka") * band, band, axis=1
    )
    lane_weight = jnp.broadcast_to(band_weight[:, :, None], (axial_cells, band, columns)).reshape(1, lanes)

    def transform_all(snapshots, weight=None):
        pieces = [piece.reshape(local_angles, lanes) for piece in exchange(snapshots, "ka", 2, separate=True)]
        modes = dft(table, pieces, weight)
        return modes.reshape(total_angles, axial_cells, band, columns)

    direct_modes = in_source_order(exchange(transform_all(direct_snapshots), "ka", 0, separate=True), "ka", 2)
    weighted = in_source_order(
        exchange(transform_all(adjoint_snapshots, lane_weight), "ka", 0, separate=True), "ka", 2
    )
    padded = padded_2(direct_modes, (("gx", 1),), 1)
    field_f32 = direct_modes.astype(jnp.float32)
    forward = padded[:, 2:].astype(jnp.float32)
    behind = padded[:, :-2].astype(jnp.float32)
    radial_pad = jnp.pad(direct_modes, ((0, 0), (0, 0), (1, 1), (0, 0))).astype(jnp.float32)
    outward = radial_pad[:, :, 2:]
    inward = radial_pad[:, :, :-2]
    radius = 0.25 + (jnp.arange(radial_cells, dtype=jnp.float32) + 0.5) / radial_cells
    wavenumber = (
        first_wave + jnp.arange(local_angles, dtype=jnp.int32) - total_angles // 2
    ).astype(jnp.float32) / total_angles
    azimuthal = (wavenumber[:, None] / radius[None, :]) ** 2
    velocity = mean_velocity[None, :, :, None]
    diffusion = diffusivity[None, :, :, None]
    image = (
        -velocity * (forward - behind) * 0.5
        + diffusion
        * (
            forward
            + behind
            + outward
            + inward
            - 4.0 * field_f32
            - azimuthal[:, None, :, None] * field_f32
        )
    ).astype(jnp.bfloat16)
    right_side = jnp.concatenate([direct_modes, image], axis=-1)
    product = jnp.einsum(
        "kpa,kpb->kab",
        weighted.reshape(local_angles, -1, columns),
        right_side.reshape(local_angles, -1, 2 * columns),
        preferred_element_type=jnp.float32,
    )
    gram_terms = complex_blocks(product, snap_count).reshape(local_angles * snap_count, 2 * columns)
    row_count = gram_terms.shape[0] // lax.axis_size("gx")
    row_index = lax.axis_index("gx") * row_count + jnp.arange(row_count, dtype=jnp.int32)
    owner = row_index // snap_count
    selector = (owner[:, None] == jnp.arange(local_angles, dtype=jnp.int32)[None, :]).astype(
        jnp.float32
    )
    shares = gram_terms.astype(jnp.bfloat16).reshape(lax.axis_size("gx"), row_count, 2 * columns)
    own_rows = sum(piece.astype(jnp.float32) for piece in exchange(shares, "gx", 0, True, True))[0]
    row_energy = jnp.sum(own_rows[:, :columns] ** 2, axis=1)
    energy = jnp.sum(gather_small(jnp.sum(selector * row_energy[:, None], axis=0), "gx"), axis=0)
    mean_sq = energy / (2.0 * snap_count * snap_count)
    row_scale = jnp.sum(selector * lax.rsqrt(mean_sq + epsilon)[None, :], axis=1)
    hankel_gram = own_rows[:, :columns] * row_scale[:, None]
    reduced_operator = own_rows[:, columns:] * row_scale[:, None]
    hankel_norm = jnp.sqrt(mean_sq)
    return (hankel_gram, reduced_operator, hankel_norm)


def solution(mesh):
    placed = (
        P("ka", "gx", None, None),
        P("ka", "gx", None, None),
        P("gx", None),
        P("gx", None),
        P("gx", None),
    )
    return jax.shard_map(
        local,
        mesh=mesh,
        in_specs=placed,
        out_specs=(P(("ka", "gx"), None), P(("ka", "gx"), None), P("ka")),
        check_vma=False,
    )
```

```python
import functools
import math

import jax
import jax.numpy as jnp
from jax import lax
from jax.experimental import pallas as pl
from jax.experimental.pallas import tpu as pltpu
from jax.sharding import PartitionSpec as P

epsilon = 1e-06


def padded_2(cells, sides, width):
    for axis, dim in sides:
        count = lax.axis_size(axis)
        ends = count - 1
        head = lax.slice_in_dim(cells, 0, width, axis=dim)
        tail = lax.slice_in_dim(cells, cells.shape[dim] - width, cells.shape[dim], axis=dim)
        cells = jnp.concatenate(
            [
                lax.ppermute(tail, axis, [(i, (i + 1) % count) for i in range(ends)]),
                cells,
                lax.ppermute(head, axis, [((i + 1) % count, i) for i in range(ends)]),
            ],
            axis=dim,
        )
    return cells


def gather_small(values, axis):
    count = lax.axis_size(axis)
    copies = jnp.broadcast_to(values[None], (count,) + values.shape)
    return lax.all_to_all(copies, axis, split_axis=0, concat_axis=0, tiled=True)


def exchange(cells, axis, split_axis, far_first=False, separate=False, dtype=None):
    count = lax.axis_size(axis)
    here = lax.axis_index(axis)
    width = cells.shape[split_axis] // count
    shifts = list(range(count))
    if far_first:
        shifts = [0] + sorted(range(1, count), key=lambda shift: -min(shift, count - shift))
    pieces = []
    for shift in shifts:
        source = cells
        if separate:
            source, _ = lax.optimization_barrier((cells, jnp.int32(shift)))
        piece = lax.dynamic_slice_in_dim(source, ((here + shift) % count) * width, width, axis=split_axis)
        if dtype is not None:
            piece = piece.astype(dtype)
        if shift:
            piece = lax.ppermute(piece, axis, [(j, (j + shift) % count) for j in range(count)])
        pieces.append(piece)
    return pieces


def in_source_order(pieces, axis, concat_axis):
    count = len(pieces)
    here = lax.axis_index(axis)
    stacked = jnp.stack(pieces)
    ordered = [lax.dynamic_index_in_dim(stacked, (here - source) % count, 0, keepdims=False) for source in range(count)]
    return jnp.concatenate(ordered, axis=concat_axis)


def shifted_tables(count, local_angles, axis):
    here = lax.axis_index(axis)
    blocks = count // local_angles
    wave_index = jnp.arange(count, dtype=jnp.int32) - count // 2
    position = jnp.arange(count, dtype=jnp.int32)
    angle_index = ((here - position // local_angles) % blocks) * local_angles + position % local_angles
    residues = wave_index[:, None] * angle_index[None, :] % count
    phases = 2.0 * math.pi * residues.astype(jnp.float32) / count
    scaling = 1.0 / math.sqrt(count)
    return (
        (jnp.cos(phases) * scaling).astype(jnp.bfloat16),
        (jnp.sin(phases) * scaling).astype(jnp.bfloat16),
    )


def dft_kernel(*refs, count, weighted):
    table_ref = refs[0]
    piece_refs = refs[1:1 + count]
    rest = refs[1 + count:]
    out_ref = rest[-1]
    width = piece_refs[0].shape[1]
    lane = lax.broadcasted_iota(jnp.int32, (1, width), 1) % 128
    low = lane < 64
    packed = piece_refs[0].shape[0] % 16 == 0
    rows = []
    for piece_ref in piece_refs:
        x = piece_ref[...]
        if not packed:
            x = x.astype(jnp.float32)
        swapped = jnp.where(low, pltpu.roll(x, width - 64, 1), -pltpu.roll(x, 64, 1))
        rows.append(x)
        rows.append(swapped)
    stacked = jnp.concatenate(rows, axis=0).astype(jnp.bfloat16)
    acc = jnp.dot(table_ref[...], stacked, preferred_element_type=jnp.float32)
    modes = acc.astype(jnp.bfloat16)
    if weighted:
        modes = (modes.astype(jnp.float32) * rest[0][...]).astype(jnp.bfloat16)
    out_ref[...] = modes

def dft(table, pieces, weight=None):
    count = len(pieces)
    angles, total = pieces[0].shape
    waves = table.shape[0]
    block = math.gcd(total, 4096)
    grid = (total // block,)
    in_specs = [pl.BlockSpec((waves, table.shape[1]), lambda j: (0, 0))]
    in_specs += [pl.BlockSpec((angles, block), lambda j: (0, j)) for _ in pieces]
    args = [table, *pieces]
    if weight is not None:
        in_specs.append(pl.BlockSpec((1, block), lambda j: (0, j)))
        args.append(weight)
    return pl.pallas_call(
        functools.partial(dft_kernel, count=count, weighted=weight is not None),
        grid=grid,
        in_specs=in_specs,
        out_specs=pl.BlockSpec((waves, block), lambda j: (0, j)),
        out_shape=jax.ShapeDtypeStruct((waves, total), jnp.bfloat16),
    )(*args)


def piece_tables(count, local_angles, axis):
    here = lax.axis_index(axis)
    blocks = count // local_angles
    wave_index = jnp.arange(count, dtype=jnp.int32) - count // 2
    scaling = 1.0 / math.sqrt(count)
    columns = []
    for shift in range(blocks):
        angle_index = ((here - shift) % blocks) * local_angles + jnp.arange(local_angles, dtype=jnp.int32)
        residues = wave_index[:, None] * angle_index[None, :] % count
        phases = 2.0 * math.pi * residues.astype(jnp.float32) / count
        columns.append((jnp.cos(phases) * scaling).astype(jnp.bfloat16))
        columns.append((jnp.sin(phases) * scaling).astype(jnp.bfloat16))
    return jnp.concatenate(columns, axis=1)


def dft_tables(count):
    wave_index = jnp.arange(count, dtype=jnp.int32) - count // 2
    angle_index = jnp.arange(count, dtype=jnp.int32)
    residues = wave_index[:, None] * angle_index[None, :] % count
    phases = 2.0 * math.pi * residues.astype(jnp.float32) / count
    scaling = 1.0 / math.sqrt(count)
    return (
        (jnp.cos(phases) * scaling).astype(jnp.bfloat16),
        (jnp.sin(phases) * scaling).astype(jnp.bfloat16),
    )


def combine_parts(cos_part, sin_part, half):
    real_part = cos_part[..., :half] + sin_part[..., half:]
    imag_part = cos_part[..., half:] - sin_part[..., :half]
    return jnp.concatenate([real_part, imag_part], axis=-1).astype(jnp.bfloat16)


def complex_blocks(product, half):
    upper_rows = product[..., :half, :]
    lower_rows = product[..., half:, :]
    pieces = []
    for offset in (0, 2 * half):
        pieces.append(
            upper_rows[..., offset : offset + half]
            + lower_rows[..., offset + half : offset + 2 * half]
        )
        pieces.append(
            upper_rows[..., offset + half : offset + 2 * half]
            - lower_rows[..., offset : offset + half]
        )
    return jnp.concatenate(pieces, axis=-1)


def local(direct_snapshots, adjoint_snapshots, quad_weight, mean_velocity, diffusivity):
    local_angles, axial_cells, radial_cells, columns = direct_snapshots.shape
    snap_count = columns // 2
    total_angles = local_angles * lax.axis_size("ka")
    table = piece_tables(total_angles, local_angles, "ka")
    first_wave = lax.axis_index("ka") * local_angles
    band_count = lax.axis_size("ka")
    band = radial_cells // band_count
    lanes = axial_cells * band * columns
    norm_factor = 1.0 / math.sqrt(axial_cells * lax.axis_size("gx") * radial_cells)
    band_weight = lax.dynamic_slice_in_dim(
        quad_weight * norm_factor, lax.axis_index("ka") * band, band, axis=1
    )
    lane_weight = jnp.broadcast_to(band_weight[:, :, None], (axial_cells, band, columns)).reshape(1, lanes)

    def transform_all(snapshots, weight=None):
        pieces = [piece.reshape(local_angles, lanes) for piece in exchange(snapshots, "ka", 2, separate=True)]
        modes = dft(table, pieces, weight)
        return modes.reshape(total_angles, axial_cells, band, columns)

    direct_modes = in_source_order(exchange(transform_all(direct_snapshots), "ka", 0, separate=True), "ka", 2)
    weighted = in_source_order(
        exchange(transform_all(adjoint_snapshots, lane_weight), "ka", 0, separate=True), "ka", 2
    )
    padded = padded_2(direct_modes, (("gx", 1),), 1)
    field_f32 = direct_modes.astype(jnp.float32)
    forward = padded[:, 2:].astype(jnp.float32)
    behind = padded[:, :-2].astype(jnp.float32)
    radial_pad = jnp.pad(direct_modes, ((0, 0), (0, 0), (1, 1), (0, 0))).astype(jnp.float32)
    outward = radial_pad[:, :, 2:]
    inward = radial_pad[:, :, :-2]
    radius = 0.25 + (jnp.arange(radial_cells, dtype=jnp.float32) + 0.5) / radial_cells
    wavenumber = (
        first_wave + jnp.arange(local_angles, dtype=jnp.int32) - total_angles // 2
    ).astype(jnp.float32) / total_angles
    azimuthal = (wavenumber[:, None] / radius[None, :]) ** 2
    velocity = mean_velocity[None, :, :, None]
    diffusion = diffusivity[None, :, :, None]
    image = (
        -velocity * (forward - behind) * 0.5
        + diffusion
        * (
            forward
            + behind
            + outward
            + inward
            - 4.0 * field_f32
            - azimuthal[:, None, :, None] * field_f32
        )
    ).astype(jnp.bfloat16)
    right_side = jnp.concatenate([direct_modes, image], axis=-1)
    product = jnp.einsum(
        "kpa,kpb->kab",
        weighted.reshape(local_angles, -1, columns),
        right_side.reshape(local_angles, -1, 2 * columns),
        preferred_element_type=jnp.float32,
    )
    gram_terms = complex_blocks(product, snap_count).reshape(local_angles * snap_count, 2 * columns)
    row_count = gram_terms.shape[0] // lax.axis_size("gx")
    row_index = lax.axis_index("gx") * row_count + jnp.arange(row_count, dtype=jnp.int32)
    owner = row_index // snap_count
    selector = (owner[:, None] == jnp.arange(local_angles, dtype=jnp.int32)[None, :]).astype(
        jnp.float32
    )
    shares = gram_terms.reshape(lax.axis_size("gx"), row_count, 2 * columns)
    own_rows = sum(piece.astype(jnp.float32) for piece in exchange(shares, "gx", 0, True, True, jnp.bfloat16))[0]
    row_energy = jnp.sum(own_rows[:, :columns] ** 2, axis=1)
    energy = jnp.sum(gather_small(jnp.sum(selector * row_energy[:, None], axis=0), "gx"), axis=0)
    mean_sq = energy / (2.0 * snap_count * snap_count)
    row_scale = jnp.sum(selector * lax.rsqrt(mean_sq + epsilon)[None, :], axis=1)
    hankel_gram = own_rows[:, :columns] * row_scale[:, None]
    reduced_operator = own_rows[:, columns:] * row_scale[:, None]
    hankel_norm = jnp.sqrt(mean_sq)
    return (hankel_gram, reduced_operator, hankel_norm)


def solution(mesh):
    placed = (
        P("ka", "gx", None, None),
        P("ka", "gx", None, None),
        P("gx", None),
        P("gx", None),
        P("gx", None),
    )
    return jax.shard_map(
        local,
        mesh=mesh,
        in_specs=placed,
        out_specs=(P(("ka", "gx"), None), P(("ka", "gx"), None), P("ka")),
        check_vma=False,
    )
```
